32 devices in a mesh: row: 4 (over x, core), col: 8 (over z, y).
Axes of the slice: x: 2, y: 2, z: 4, core: 2. Of those that a mesh axis runs over, the one named last changes fastest.
Arguments:
- embed: bfloat16 [1024, 768], P(('row', 'col'))
- beta: bfloat16 [1024], P(('row', 'col')), may hold values from 16 to 400
- block_mask: int32 [8, 8], P('row'), may hold values from 0 to 1, as said below
- counts: int32 [8], replicated, may hold values from 2 to 128
- probes: float32 [64, 1024], P(None, ('row', 'col')), may hold values from -6 to 6
Outputs:
- spectral: float32 [64, 1024], P(None, ('row', 'col'))
The draws below stay inside these ranges and needn't reach their ends.
Inputs may be any that keep to these rules, and one draw needn't show every extreme that they name: `block_mask`: every diagonal entry is 1.
All inputs are finite; a program needn't handle non-finite values.
Results may differ from the reference program's by a relative error of at most 0.012.
The reference program's roundings to bfloat16 on the way count: a program that leaves them out, or rounds other values in their place, can miss the bound.
Values may be sent and summed in bfloat16 or wider, within the bound.
No kernel may reach another device: no remote copies, remote signals or barrier semaphores. Data moves between devices by JAX's collectives and lax.ppermute only.
A program may use at most 64 MiB of HBM per device.

```python
import math
import jax
import jax.numpy as jnp
from jax import lax

D = 768
PROBES = 64
BLK = 128
ITERS = 2
FILES = 1024
ROW_FILES = 256
COL_FILES = 128
NB = 8


def draw_embed(key, part):
    return jax.random.normal(key, (FILES, D), jnp.float32).astype(jnp.bfloat16)


def draw_beta(key, part):
    log_values = jax.random.uniform(key, (FILES,), jnp.float32, math.log(16.0), math.log(400.0))
    values = jnp.exp(log_values)
    return jnp.clip(values, 16.0, 400.0).astype(jnp.bfloat16)


def draw_block_mask(key, part):
    block_count = FILES // BLK
    tile_rows = ROW_FILES // BLK
    tile_cols = COL_FILES // BLK
    key_one, key_two = jax.random.split(key)
    tile_level = jnp.left_shift(1, jax.random.randint(key_one, (block_count // tile_rows, block_count // tile_cols), 0, 4))
    level_wide = jnp.repeat(jnp.repeat(tile_level, tile_rows, axis=0), tile_cols, axis=1)
    rolled = jax.random.randint(key_two, (block_count, block_count), 0, 8)
    diagonal_on = jnp.arange(block_count)[:, None] == jnp.arange(block_count)[None, :]
    return jnp.where((rolled < level_wide) | diagonal_on, 1, 0).astype(jnp.int32)


def place_ends(drawn, own_key, smallest, top_value):
    dims = drawn.shape
    place = [jax.random.randint(jax.random.fold_in(own_key, axis), (), 0, dims[axis]) for axis in range(len(dims))]
    drawn = drawn.at[tuple(place)].set(smallest)
    longest = dims.index(max(dims))
    place[longest] = (place[longest] + 1) % dims[longest]
    return drawn.at[tuple(place)].set(top_value)


def levels(own_key, shape, pieces, smallest, largest):
    loudness, own = 1.0, jax.random.fold_in(own_key, 6)
    for position, blocks in pieces:
        heights = jnp.exp(jax.random.uniform(jax.random.fold_in(own, position), (blocks,), jnp.float32, smallest / len(pieces), largest / len(pieces)))
        loudness = loudness * jnp.repeat(heights, shape[position] // blocks).reshape([-1 if axis == position else 1 for axis in range(len(shape))])
    return loudness


def scatter_about(key, dims, deviation, limit, shards=(), kind=jnp.bfloat16):
    values = deviation * jax.random.normal(key, dims, jnp.float32)
    if shards:
        values = values * levels(key, dims, shards, -0.22, 0.18)
    return jnp.clip(values, -limit, limit).astype(kind)


def setup_inputs(seed: int = 0) -> dict:
    key_list = jax.random.split(jax.random.key(seed), 6)
    embed = draw_embed(jax.random.fold_in(key_list[5], 71), 0)
    beta = draw_beta(jax.random.fold_in(key_list[5], 71), 0)
    block_mask = draw_block_mask(jax.random.fold_in(key_list[5], 71), 0)
    counts = place_ends(jax.random.randint(key_list[3], (NB,), 2, BLK + 1), jax.random.fold_in(key_list[3], 1), 2, BLK).astype(jnp.int32)
    probes = scatter_about(key_list[4], (PROBES, FILES), 1.0, 6.0, ((1, 32),), jnp.float32)
    return {"embed": embed, "beta": beta, "block_mask": block_mask, "counts": counts, "probes": probes}


def reference(embed, beta, block_mask, counts, probes):
    file_count = embed.shape[0]
    values = embed.astype(jnp.float32)
    unit_vec = (values * lax.rsqrt(lax.optimization_barrier(jnp.mean(values * values, axis=1, keepdims=True)) + 1e-06)).astype(jnp.bfloat16)
    scale = beta.astype(jnp.float32) / D
    col_ids = jnp.arange(file_count, dtype=jnp.int32)
    col_block = col_ids // BLK
    col_live = col_ids % BLK < counts[col_block]
    block_ids = jnp.arange(file_count // BLK, dtype=jnp.int32)

    def weights_of(blk_index):
        row_start = blk_index * BLK
        row_vecs = lax.dynamic_slice_in_dim(unit_vec, row_start, BLK, 0)
        row_scale = lax.dynamic_slice_in_dim(scale, row_start, BLK, 0)
        scores = jnp.dot(row_vecs, unit_vec.T, preferred_element_type=jnp.float32) * row_scale[:, None]
        mask_row = lax.dynamic_index_in_dim(block_mask, blk_index, 0, keepdims=False)
        row_ids = row_start + jnp.arange(BLK, dtype=jnp.int32)
        allowed = (mask_row[col_block] == 1)[None, :] & col_live[None, :] & (row_ids[:, None] != col_ids[None, :])
        masked = jnp.where(allowed, scores, -1e+30)
        row_top = lax.optimization_barrier(jnp.max(masked, axis=1))
        row_mass = lax.optimization_barrier(jnp.sum(jnp.where(allowed, jnp.exp(masked - row_top[:, None]), 0.0), axis=1))
        return jnp.where(allowed, jnp.exp(masked - row_top[:, None]) / row_mass[:, None], 0.0)

    def add_mass(running, blk_index):
        return (running + lax.optimization_barrier(jnp.sum(weights_of(blk_index), axis=0)), None)
    col_mass, _ = lax.scan(add_mass, jnp.zeros((file_count,), jnp.float32), block_ids)
    inv_root = lax.rsqrt((1.0 + col_mass) * 0.5)
    probe_state = probes
    for sweep in range(ITERS):
        scaled = (probe_state * inv_root[None, :]).astype(jnp.bfloat16)

        def project(running, blk_index):
            affinity = weights_of(blk_index).astype(jnp.bfloat16)
            row_part = jnp.dot(scaled, affinity.T, preferred_element_type=jnp.float32)
            row_probe = lax.dynamic_slice_in_dim(scaled, blk_index * BLK, BLK, 1)
            return (running + jnp.dot(row_probe, affinity, preferred_element_type=jnp.float32), row_part)
        col_part, row_parts = lax.scan(project, jnp.zeros((PROBES, file_count), jnp.float32), block_ids)
        row_total = jnp.transpose(row_parts, (1, 0, 2)).reshape(PROBES, file_count)
        probe_state = (row_total + col_part) * (0.5 * inv_root)[None, :]
    return probe_state
```

```python
import jax
import jax.numpy as jnp
from jax import lax
from jax.sharding import PartitionSpec as P

ITERS = 2
AXES = ("row", "col")
A2A_BYTES = 8 << 20
REPLICATE_CELLS = 1 << 21


def gather_rows(x, n_dev):
    if n_dev * x.size * x.dtype.itemsize <= A2A_BYTES:
        wide = jnp.broadcast_to(x[None], (n_dev,) + x.shape)
        return lax.all_to_all(wide, AXES, 0, 0, tiled=True)
    return lax.all_gather(x, AXES, axis=0, tiled=False)


def normalize(embed):
    values = embed.astype(jnp.float32)
    return (values * lax.rsqrt(jnp.mean(values * values, axis=1, keepdims=True) + 1e-06)).astype(
        jnp.bfloat16
    )


def pack_rows(flat, width):
    rows = -(-flat.shape[0] // width)
    return jnp.pad(flat, (0, rows * width - flat.shape[0])).reshape(rows, width), rows


def body(embed, beta, block_mask, counts, probes):
    n_dev = lax.axis_size("row") * lax.axis_size("col")
    n_row = lax.axis_size("row")
    me = lax.axis_index(AXES)
    shard, feat = embed.shape
    files = shard * n_dev
    nb = block_mask.shape[1]
    blk = files // nb
    local_blocks = block_mask.shape[0]

    unit_own = normalize(embed)
    beta_rows, beta_n = pack_rows(beta, feat)
    mask_rows, mask_n = pack_rows(block_mask.reshape(-1).astype(jnp.bfloat16), feat)
    replicate = files * files <= REPLICATE_CELLS
    if replicate:
        got = gather_rows(jnp.concatenate([unit_own, beta_rows, mask_rows], axis=0), n_dev)
        unit_all = got[:, :shard].reshape(files, feat)
        extra = got[:, shard:]
    else:
        unit_all = gather_rows(unit_own, n_dev).reshape(files, feat)
        extra = gather_rows(jnp.concatenate([beta_rows, mask_rows], axis=0), n_dev)
    beta_all = extra[:, 0, :shard].reshape(files)
    mask_got = extra[:, beta_n:, :].reshape(n_dev, -1)[:, : local_blocks * nb]
    per_row = n_dev // n_row
    mask_full = (
        mask_got.reshape(n_row, per_row, local_blocks, nb)[:, 0].reshape(nb, nb).astype(jnp.int32)
    )
    scale_all = beta_all.astype(jnp.float32) / feat

    col_ids = lax.iota(jnp.int32, files)
    col_block = col_ids // blk
    col_live = col_ids % blk < jnp.take(counts, col_block, axis=0)

    if replicate:
        probes_all = gather_rows(probes, n_dev)
        probes_all = jnp.transpose(probes_all, (1, 0, 2)).reshape(probes.shape[0], files)
        gram = lax.dot_general(
            unit_all, unit_all, (((1,), (1,)), ((), ())), preferred_element_type=jnp.float32
        )
        scores = gram * scale_all[:, None]
        block_ok = jnp.take(jnp.take(mask_full, col_block, axis=0), col_block, axis=1) == 1
        allowed = block_ok & col_live[None, :] & (col_ids[:, None] != col_ids[None, :])
        masked = jnp.where(allowed, scores, -1e30)
        row_top = jnp.max(masked, axis=1)
        row_mass = jnp.sum(jnp.where(allowed, jnp.exp(masked - row_top[:, None]), 0.0), axis=1)
        weights = jnp.where(allowed, jnp.exp(masked - row_top[:, None]) / row_mass[:, None], 0.0)
        col_mass = jnp.sum(weights, axis=0)
        inv_root = lax.rsqrt((1.0 + col_mass) * 0.5)
        affinity = weights.astype(jnp.bfloat16)
        state = probes_all
        for sweep in range(ITERS):
            scaled = (state * inv_root[None, :]).astype(jnp.bfloat16)
            row_part = lax.dot_general(
                scaled, affinity, (((1,), (1,)), ((), ())), preferred_element_type=jnp.float32
            )
            col_part = jnp.dot(scaled, affinity, preferred_element_type=jnp.float32)
            state = (row_part + col_part) * (0.5 * inv_root)[None, :]
        return lax.dynamic_slice_in_dim(state, me * shard, shard, 1)

    own_ids = me * shard + lax.iota(jnp.int32, shard)
    own_block = own_ids // blk
    gram = lax.dot_general(
        unit_own, unit_all, (((1,), (1,)), ((), ())), preferred_element_type=jnp.float32
    )
    own_scale = lax.dynamic_slice_in_dim(scale_all, me * shard, shard, 0)
    scores = gram * own_scale[:, None]
    row_ok = jnp.take(jnp.take(mask_full, own_block, axis=0), col_block, axis=1) == 1
    allowed = row_ok & col_live[None, :] & (own_ids[:, None] != col_ids[None, :])
    masked = jnp.where(allowed, scores, -1e30)
    row_top = jnp.max(masked, axis=1)
    row_mass = jnp.sum(jnp.where(allowed, jnp.exp(masked - row_top[:, None]), 0.0), axis=1)
    weights = jnp.where(allowed, jnp.exp(masked - row_top[:, None]) / row_mass[:, None], 0.0)
    stats = gather_rows(jnp.stack([row_top, row_mass], axis=1), n_dev).reshape(files, 2)
    top_all, mass_all = stats[:, 0], stats[:, 1]
    scores_t = gram * scale_all[None, :]
    own_live = jnp.take(col_live, own_ids, axis=0)
    col_ok = jnp.take(jnp.take(mask_full, col_block, axis=0), own_block, axis=1).T == 1
    allowed_t = col_ok & own_live[:, None] & (own_ids[:, None] != col_ids[None, :])
    masked_t = jnp.where(allowed_t, scores_t, -1e30)
    weights_t = jnp.where(
        allowed_t, jnp.exp(masked_t - top_all[None, :]) / mass_all[None, :], 0.0
    )
    col_mass = jnp.sum(weights_t, axis=1)
    inv_root = lax.rsqrt((1.0 + col_mass) * 0.5)
    aff_rows = weights.astype(jnp.bfloat16)
    aff_cols = weights_t.astype(jnp.bfloat16)
    state = probes
    for sweep in range(ITERS):
        scaled = (state * inv_root[None, :]).astype(jnp.bfloat16)
        scaled_all = gather_rows(scaled.T, n_dev).reshape(files, probes.shape[0])
        row_part = jnp.dot(aff_rows, scaled_all, preferred_element_type=jnp.float32)
        col_part = jnp.dot(aff_cols, scaled_all, preferred_element_type=jnp.float32)
        state = ((row_part + col_part) * (0.5 * inv_root)[:, None]).T
    return state


def solution(mesh):
    placed = (
        P(AXES, None),
        P(AXES),
        P("row", None),
        P(),
        P(None, AXES),
    )
    return jax.shard_map(body, mesh=mesh, in_specs=placed, out_specs=P(None, AXES), check_vma=False)
```

```python
import jax
import jax.numpy as jnp
from jax import lax
from jax.sharding import PartitionSpec as P

ITERS = 2
AXES = ("row", "col")
A2A_BYTES = 8 << 20
REPLICATE_CELLS = 1 << 21


def gather_rows(x, n_dev):
    if n_dev * x.size * x.dtype.itemsize <= A2A_BYTES:
        wide = jnp.broadcast_to(x[None], (n_dev,) + x.shape)
        return lax.all_to_all(wide, AXES, 0, 0, tiled=True)
    return lax.all_gather(x, AXES, axis=0, tiled=False)


def gather_halves(x, n_dev, n_row):
    if n_row % 2:
        return gather_rows(x, n_dev)
    rows = x.shape[0] + x.shape[0] % 2
    halves = jnp.pad(x, ((0, rows - x.shape[0]), (0, 0))).reshape(2, rows // 2, x.shape[1])
    per_row = n_dev // n_row
    wide = jnp.broadcast_to(
        halves[None, :, None], (n_row // 2, 2, per_row, rows // 2, x.shape[1])
    ).reshape(n_dev, rows // 2, x.shape[1])
    mine = lax.all_to_all(wide, AXES, 0, 0, tiled=True)
    other = lax.ppermute(mine, "row", [(r, r ^ 1) for r in range(n_row)])
    first = lax.axis_index("row") % 2 == 0
    low = jnp.where(first, mine, other)
    high = jnp.where(first, other, mine)
    return jnp.concatenate([low, high], axis=1)[:, : x.shape[0]]


def normalize(embed):
    values = embed.astype(jnp.float32)
    return (values * lax.rsqrt(jnp.mean(values * values, axis=1, keepdims=True) + 1e-06)).astype(
        jnp.bfloat16
    )


def split3(x):
    hi = lax.reduce_precision(x, exponent_bits=8, mantissa_bits=7)
    rest = x - hi
    mid = lax.reduce_precision(rest, exponent_bits=8, mantissa_bits=7)
    lo = rest - mid
    return jnp.stack([hi, mid, lo]).astype(jnp.bfloat16)


def join3(parts):
    parts = parts.astype(jnp.float32)
    return (parts[0] + parts[1]) + parts[2]


def pack_rows(flat, width):
    rows = -(-flat.shape[0] // width)
    return jnp.pad(flat, (0, rows * width - flat.shape[0])).reshape(rows, width), rows


def body(embed, beta, block_mask, counts, probes):
    n_dev = lax.axis_size("row") * lax.axis_size("col")
    n_row = lax.axis_size("row")
    me = lax.axis_index(AXES)
    shard, feat = embed.shape
    files = shard * n_dev
    nb = block_mask.shape[1]
    blk = files // nb
    local_blocks = block_mask.shape[0]

    unit_own = normalize(embed)
    beta_rows, beta_n = pack_rows(beta, feat)
    mask_rows, mask_n = pack_rows(block_mask.reshape(-1).astype(jnp.bfloat16), feat)
    replicate = files * files <= REPLICATE_CELLS
    if replicate:
        probe_rows, probe_n = pack_rows(split3(probes).reshape(-1), feat)
        payload = jnp.concatenate([unit_own, beta_rows, mask_rows, probe_rows], axis=0)
        got = gather_halves(payload, n_dev, n_row)
        unit_all = got[:, :shard].reshape(files, feat)
        extra = got[:, shard : shard + beta_n + mask_n]
        probe_parts = got[:, shard + beta_n + mask_n :].reshape(n_dev, -1)[:, : 3 * probes.size]
        probe_parts = probe_parts.reshape(n_dev, 3, probes.shape[0], shard)
        probes_all = jnp.transpose(join3(jnp.moveaxis(probe_parts, 1, 0)), (1, 0, 2))
        probes_all = probes_all.reshape(probes.shape[0], files)
    else:
        unit_all = gather_rows(unit_own, n_dev).reshape(files, feat)
        extra = gather_rows(jnp.concatenate([beta_rows, mask_rows], axis=0), n_dev)
    beta_all = extra[:, 0, :shard].reshape(files)
    mask_got = extra[:, beta_n:, :].reshape(n_dev, -1)[:, : local_blocks * nb]
    per_row = n_dev // n_row
    mask_full = (
        mask_got.reshape(n_row, per_row, local_blocks, nb)[:, 0].reshape(nb, nb).astype(jnp.int32)
    )
    scale_all = beta_all.astype(jnp.float32) / feat

    col_ids = lax.iota(jnp.int32, files)
    col_block = col_ids // blk
    in_block = lax.iota(jnp.int32, blk)
    col_live = (in_block[None, :] < counts[:, None]).reshape(files)

    if replicate:
        gram = lax.dot_general(
            unit_all, unit_all, (((1,), (1,)), ((), ())), preferred_element_type=jnp.float32
        )
        scores = gram * scale_all[:, None]
        block_ok = jnp.broadcast_to(
            (mask_full == 1)[:, None, :, None], (nb, blk, nb, blk)
        ).reshape(files, files)
        allowed = block_ok & col_live[None, :] & (col_ids[:, None] != col_ids[None, :])
        masked = jnp.where(allowed, scores, -1e30)
        row_top = jnp.max(masked, axis=1)
        row_mass = jnp.sum(jnp.where(allowed, jnp.exp(masked - row_top[:, None]), 0.0), axis=1)
        weights = jnp.where(allowed, jnp.exp(masked - row_top[:, None]) / row_mass[:, None], 0.0)
        col_mass = jnp.sum(weights, axis=0)
        inv_root = lax.rsqrt((1.0 + col_mass) * 0.5)
        affinity = weights.astype(jnp.bfloat16)
        state = probes_all
        for sweep in range(ITERS):
            scaled = (state * inv_root[None, :]).astype(jnp.bfloat16)
            row_part = lax.dot_general(
                scaled, affinity, (((1,), (1,)), ((), ())), preferred_element_type=jnp.float32
            )
            col_part = jnp.dot(scaled, affinity, preferred_element_type=jnp.float32)
            state = (row_part + col_part) * (0.5 * inv_root)[None, :]
        return lax.dynamic_slice_in_dim(state, me * shard, shard, 1)

    own_ids = me * shard + lax.iota(jnp.int32, shard)
    own_block = own_ids // blk
    gram = lax.dot_general(
        unit_own, unit_all, (((1,), (1,)), ((), ())), preferred_element_type=jnp.float32
    )
    own_scale = lax.dynamic_slice_in_dim(scale_all, me * shard, shard, 0)
    scores = gram * own_scale[:, None]
    row_ok = jnp.take(jnp.take(mask_full, own_block, axis=0), col_block, axis=1) == 1
    allowed = row_ok & col_live[None, :] & (own_ids[:, None] != col_ids[None, :])
    masked = jnp.where(allowed, scores, -1e30)
    row_top = jnp.max(masked, axis=1)
    row_mass = jnp.sum(jnp.where(allowed, jnp.exp(masked - row_top[:, None]), 0.0), axis=1)
    weights = jnp.where(allowed, jnp.exp(masked - row_top[:, None]) / row_mass[:, None], 0.0)
    stats = gather_rows(jnp.stack([row_top, row_mass], axis=1), n_dev).reshape(files, 2)
    top_all, mass_all = stats[:, 0], stats[:, 1]
    scores_t = gram * scale_all[None, :]
    own_live = jnp.take(col_live, own_ids, axis=0)
    col_ok = jnp.take(jnp.take(mask_full, col_block, axis=0), own_block, axis=1).T == 1
    allowed_t = col_ok & own_live[:, None] & (own_ids[:, None] != col_ids[None, :])
    masked_t = jnp.where(allowed_t, scores_t, -1e30)
    weights_t = jnp.where(
        allowed_t, jnp.exp(masked_t - top_all[None, :]) / mass_all[None, :], 0.0
    )
    col_mass = jnp.sum(weights_t, axis=1)
    inv_root = lax.rsqrt((1.0 + col_mass) * 0.5)
    aff_rows = weights.astype(jnp.bfloat16)
    aff_cols = weights_t.astype(jnp.bfloat16)
    state = probes
    for sweep in range(ITERS):
        scaled = (state * inv_root[None, :]).astype(jnp.bfloat16)
        scaled_all = gather_rows(scaled.T, n_dev).reshape(files, probes.shape[0])
        row_part = jnp.dot(aff_rows, scaled_all, preferred_element_type=jnp.float32)
        col_part = jnp.dot(aff_cols, scaled_all, preferred_element_type=jnp.float32)
        state = ((row_part + col_part) * (0.5 * inv_root)[:, None]).T
    return state


def solution(mesh):
    placed = (
        P(AXES, None),
        P(AXES),
        P("row", None),
        P(),
        P(None, AXES),
    )
    return jax.shard_map(body, mesh=mesh, in_specs=placed, out_specs=P(None, AXES), check_vma=False)
```

```python
import jax
import jax.numpy as jnp
from jax import lax
from jax.sharding import PartitionSpec as P

ITERS = 2
AXES = ("row", "col")
A2A_BYTES = 8 << 20
REPLICATE_CELLS = 1 << 21


def gather_rows(x, n_dev):
    if n_dev * x.size * x.dtype.itemsize <= A2A_BYTES:
        wide = jnp.broadcast_to(x[None], (n_dev,) + x.shape)
        return lax.all_to_all(wide, AXES, 0, 0, tiled=True)
    return lax.all_gather(x, AXES, axis=0, tiled=False)


def gather_halves(x, n_dev, n_row):
    if n_row % 2:
        return gather_rows(x, n_dev)
    rows = x.shape[0] + x.shape[0] % 2
    halves = jnp.pad(x, ((0, rows - x.shape[0]), (0, 0))).reshape(2, rows // 2, x.shape[1])
    per_row = n_dev // n_row
    wide = jnp.broadcast_to(
        halves[None, :, None], (n_row // 2, 2, per_row, rows // 2, x.shape[1])
    ).reshape(n_dev, rows // 2, x.shape[1])
    mine = lax.all_to_all(wide, AXES, 0, 0, tiled=True)
    other = lax.ppermute(mine, "row", [(r, r ^ 1) for r in range(n_row)])
    first = lax.axis_index("row") % 2 == 0
    low = jnp.where(first, mine, other)
    high = jnp.where(first, other, mine)
    return jnp.concatenate([low, high], axis=1)[:, : x.shape[0]]


def normalize(embed):
    values = embed.astype(jnp.float32)
    return (values * lax.rsqrt(jnp.mean(values * values, axis=1, keepdims=True) + 1e-06)).astype(
        jnp.bfloat16
    )


def split3(x):
    hi = lax.reduce_precision(x, exponent_bits=8, mantissa_bits=7)
    rest = x - hi
    mid = lax.reduce_precision(rest, exponent_bits=8, mantissa_bits=7)
    lo = rest - mid
    return jnp.stack([hi, mid, lo]).astype(jnp.bfloat16)


def join3(parts):
    parts = parts.astype(jnp.float32)
    return (parts[0] + parts[1]) + parts[2]


def pack_rows(flat, width):
    rows = -(-flat.shape[0] // width)
    return jnp.pad(flat, (0, rows * width - flat.shape[0])).reshape(rows, width), rows


def body(embed, beta, block_mask, counts, probes):
    n_dev = lax.axis_size("row") * lax.axis_size("col")
    n_row = lax.axis_size("row")
    me = lax.axis_index(AXES)
    shard, feat = embed.shape
    files = shard * n_dev
    nb = block_mask.shape[1]
    blk = files // nb
    local_blocks = block_mask.shape[0]

    unit_own = normalize(embed)
    beta_rows, beta_n = pack_rows(beta, feat)
    mask_rows, mask_n = pack_rows(block_mask.reshape(-1).astype(jnp.bfloat16), feat)
    replicate = files * files <= REPLICATE_CELLS
    if replicate:
        extra_flat = jnp.concatenate(
            [
                beta,
                block_mask.reshape(-1).astype(jnp.bfloat16),
                split3(probes).reshape(-1),
            ]
        )
        lanes = -(-extra_flat.shape[0] // (shard * 128)) * 128
        extra_cols = jnp.pad(extra_flat, (0, shard * lanes - extra_flat.shape[0])).reshape(
            shard, lanes
        )
        got = gather_halves(jnp.concatenate([unit_own, extra_cols], axis=1), n_dev, n_row)
        unit_all = got[:, :, :feat].reshape(files, feat)
        tail = got[:, :, feat:].reshape(n_dev, shard * lanes)
        beta_all = tail[:, :shard].reshape(files)
        mask_got = tail[:, shard : shard + local_blocks * nb]
        probe_parts = tail[:, shard + local_blocks * nb : shard + local_blocks * nb + 3 * probes.size]
        probe_parts = probe_parts.reshape(n_dev, 3, probes.shape[0], shard)
        probes_all = jnp.transpose(join3(jnp.moveaxis(probe_parts, 1, 0)), (1, 0, 2))
        probes_all = probes_all.reshape(probes.shape[0], files)
    else:
        unit_all = gather_rows(unit_own, n_dev).reshape(files, feat)
        extra = gather_rows(jnp.concatenate([beta_rows, mask_rows], axis=0), n_dev)
        beta_all = extra[:, 0, :shard].reshape(files)
        mask_got = extra[:, beta_n:, :].reshape(n_dev, -1)[:, : local_blocks * nb]
    per_row = n_dev // n_row
    mask_full = (
        mask_got.reshape(n_row, per_row, local_blocks, nb)[:, 0].reshape(nb, nb).astype(jnp.int32)
    )
    scale_all = beta_all.astype(jnp.float32) / feat

    col_ids = lax.iota(jnp.int32, files)
    col_block = col_ids // blk
    in_block = lax.iota(jnp.int32, blk)
    col_live = (in_block[None, :] < counts[:, None]).reshape(files)

    if replicate:
        gram = lax.dot_general(
            unit_all, unit_all, (((1,), (1,)), ((), ())), preferred_element_type=jnp.float32
        )
        scores = gram * scale_all[:, None]
        block_ok = jnp.broadcast_to(
            (mask_full == 1)[:, None, :, None], (nb, blk, nb, blk)
        ).reshape(files, files)
        allowed = block_ok & col_live[None, :] & (col_ids[:, None] != col_ids[None, :])
        masked = jnp.where(allowed, scores, -1e30)
        row_top = jnp.max(masked, axis=1)
        row_mass = jnp.sum(jnp.where(allowed, jnp.exp(masked - row_top[:, None]), 0.0), axis=1)
        weights = jnp.where(allowed, jnp.exp(masked - row_top[:, None]) / row_mass[:, None], 0.0)
        col_mass = jnp.sum(weights, axis=0)
        inv_root = lax.rsqrt((1.0 + col_mass) * 0.5)
        affinity = weights.astype(jnp.bfloat16)
        state = probes_all
        for sweep in range(ITERS):
            scaled = (state * inv_root[None, :]).astype(jnp.bfloat16)
            row_part = lax.dot_general(
                scaled, affinity, (((1,), (1,)), ((), ())), preferred_element_type=jnp.float32
            )
            col_part = jnp.dot(scaled, affinity, preferred_element_type=jnp.float32)
            state = (row_part + col_part) * (0.5 * inv_root)[None, :]
        return lax.dynamic_slice_in_dim(state, me * shard, shard, 1)

    own_ids = me * shard + lax.iota(jnp.int32, shard)
    own_block = own_ids // blk
    gram = lax.dot_general(
        unit_own, unit_all, (((1,), (1,)), ((), ())), preferred_element_type=jnp.float32
    )
    own_scale = lax.dynamic_slice_in_dim(scale_all, me * shard, shard, 0)
    scores = gram * own_scale[:, None]
    row_ok = jnp.take(jnp.take(mask_full, own_block, axis=0), col_block, axis=1) == 1
    allowed = row_ok & col_live[None, :] & (own_ids[:, None] != col_ids[None, :])
    masked = jnp.where(allowed, scores, -1e30)
    row_top = jnp.max(masked, axis=1)
    row_mass = jnp.sum(jnp.where(allowed, jnp.exp(masked - row_top[:, None]), 0.0), axis=1)
    weights = jnp.where(allowed, jnp.exp(masked - row_top[:, None]) / row_mass[:, None], 0.0)
    stats = gather_rows(jnp.stack([row_top, row_mass], axis=1), n_dev).reshape(files, 2)
    top_all, mass_all = stats[:, 0], stats[:, 1]
    scores_t = gram * scale_all[None, :]
    own_live = jnp.take(col_live, own_ids, axis=0)
    col_ok = jnp.take(jnp.take(mask_full, col_block, axis=0), own_block, axis=1).T == 1
    allowed_t = col_ok & own_live[:, None] & (own_ids[:, None] != col_ids[None, :])
    masked_t = jnp.where(allowed_t, scores_t, -1e30)
    weights_t = jnp.where(
        allowed_t, jnp.exp(masked_t - top_all[None, :]) / mass_all[None, :], 0.0
    )
    col_mass = jnp.sum(weights_t, axis=1)
    inv_root = lax.rsqrt((1.0 + col_mass) * 0.5)
    aff_rows = weights.astype(jnp.bfloat16)
    aff_cols = weights_t.astype(jnp.bfloat16)
    state = probes
    for sweep in range(ITERS):
        scaled = (state * inv_root[None, :]).astype(jnp.bfloat16)
        scaled_all = gather_rows(scaled.T, n_dev).reshape(files, probes.shape[0])
        row_part = jnp.dot(aff_rows, scaled_all, preferred_element_type=jnp.float32)
        col_part = jnp.dot(aff_cols, scaled_all, preferred_element_type=jnp.float32)
        state = ((row_part + col_part) * (0.5 * inv_root)[:, None]).T
    return state


def solution(mesh):
    placed = (
        P(AXES, None),
        P(AXES),
        P("row", None),
        P(),
        P(None, AXES),
    )
    return jax.shard_map(body, mesh=mesh, in_specs=placed, out_specs=P(None, AXES), check_vma=False)
```

```python
import jax
import jax.numpy as jnp
from jax import lax
from jax.experimental import pallas as pl
from jax.experimental.pallas import tpu as pltpu
from jax.sharding import PartitionSpec as P

ITERS = 2
AXES = ("row", "col")
A2A_BYTES = 8 << 20
REPLICATE_CELLS = 1 << 21


def gather_rows(x, n_dev):
    if n_dev * x.size * x.dtype.itemsize <= A2A_BYTES:
        wide = jnp.broadcast_to(x[None], (n_dev,) + x.shape)
        return lax.all_to_all(wide, AXES, 0, 0, tiled=True)
    return lax.all_gather(x, AXES, axis=0, tiled=False)


def gather_halves(x, n_dev, n_row):
    if n_row % 2:
        return gather_rows(x, n_dev)
    rows = x.shape[0] + x.shape[0] % 2
    halves = jnp.pad(x, ((0, rows - x.shape[0]), (0, 0))).reshape(2, rows // 2, x.shape[1])
    per_row = n_dev // n_row
    wide = jnp.broadcast_to(
        halves[None, :, None], (n_row // 2, 2, per_row, rows // 2, x.shape[1])
    ).reshape(n_dev, rows // 2, x.shape[1])
    mine = lax.all_to_all(wide, AXES, 0, 0, tiled=True)
    other = lax.ppermute(mine, "row", [(r, r ^ 1) for r in range(n_row)])
    first = lax.axis_index("row") % 2 == 0
    low = jnp.where(first, mine, other)
    high = jnp.where(first, other, mine)
    return jnp.concatenate([low, high], axis=1)[:, : x.shape[0]]


def dense_kernel(n_iter, tile, mine_ref, other_ref, scale_ref, rowmask_ref, probes_ref, out_ref, unit_s, aff_s):
    files, feat = unit_s.shape
    half = files // 2
    runs = half // tile
    unit_s[0:half, :] = mine_ref[:, 0:feat]
    unit_s[half:files, :] = other_ref[:, 0:feat]
    col_pos = lax.broadcasted_iota(jnp.int32, (tile, files), 1)
    row_pos = lax.broadcasted_iota(jnp.int32, (tile, files), 0)

    def step(t, colsum):
        p0 = pl.multiple_of(t * tile, tile)
        gram = lax.dot_general(
            unit_s[pl.ds(p0, tile), :],
            unit_s[...],
            (((1,), (1,)), ((), ())),
            preferred_element_type=jnp.float32,
        )
        scores = gram * scale_ref[pl.ds(p0, tile), :]
        ok = (rowmask_ref[pl.ds(t % runs, 1), :] > 0.0) & (row_pos + p0 != col_pos)
        masked = jnp.where(ok, scores, -1e30)
        top = jnp.max(masked, axis=1, keepdims=True)
        e = jnp.where(ok, jnp.exp(masked - top), 0.0)
        mass = jnp.sum(e, axis=1, keepdims=True)
        weights = e / mass
        aff_s[pl.ds(p0, tile), :] = weights.astype(jnp.bfloat16)
        return colsum + jnp.sum(weights, axis=0, keepdims=True)

    colsum = lax.fori_loop(0, files // tile, step, jnp.zeros((1, files), jnp.float32))
    inv_root = lax.rsqrt((1.0 + colsum) * 0.5)
    state = probes_ref[...]
    for sweep in range(n_iter):
        scaled = (state * inv_root).astype(jnp.bfloat16)
        row_part = lax.dot_general(
            scaled, aff_s[...], (((1,), (1,)), ((), ())), preferred_element_type=jnp.float32
        )
        col_part = jnp.dot(scaled, aff_s[...], preferred_element_type=jnp.float32)
        state = (row_part + col_part) * (0.5 * inv_root)
    out_ref[...] = state


def dense_call(mine, other, scale, rowmask, probes_int, feat):
    files = scale.shape[0]
    tile = files // (2 * rowmask.shape[0])
    vmem = pl.BlockSpec(memory_space=pltpu.VMEM)
    return pl.pallas_call(
        lambda *refs: dense_kernel(ITERS, tile, *refs),
        out_shape=jax.ShapeDtypeStruct(probes_int.shape, jnp.float32),
        in_specs=[vmem] * 5,
        out_specs=vmem,
        scratch_shapes=[
            pltpu.VMEM((files, feat), jnp.bfloat16),
            pltpu.VMEM((files, files), jnp.bfloat16),
        ],
        cost_estimate=pl.CostEstimate(
            flops=2 * files * files * feat + 4 * ITERS * files * files * probes_int.shape[0],
            transcendentals=files * files,
            bytes_accessed=files * (feat + 256) * 2 + 8 * files * probes_int.shape[0],
        ),
    )(mine, other, scale, rowmask, probes_int)


def dense_path(unit_own, beta, block_mask, counts, probes, n_dev, n_row, me):
    shard, feat = unit_own.shape
    files = shard * n_dev
    half_s = shard // 2
    half_f = files // 2
    nb = block_mask.shape[1]
    blk = files // nb
    local_blocks = block_mask.shape[0]
    n_probe = probes.shape[0]
    per_row = n_dev // n_row
    mask_flat = block_mask.reshape(-1).astype(jnp.bfloat16)
    mask_cols = -(-mask_flat.shape[0] // half_s)
    mask_part = jnp.pad(mask_flat, (0, half_s * mask_cols - mask_flat.shape[0]))
    mask_part = jnp.tile(mask_part.reshape(half_s, mask_cols), (2, 1))
    used = 3 * n_probe + 1 + mask_cols
    lanes = -(-used // 128) * 128
    payload = jnp.concatenate(
        [
            unit_own,
            jnp.moveaxis(split3(probes.T), 0, 1).reshape(shard, 3 * n_probe),
            beta[:, None],
            mask_part,
            jnp.zeros((shard, lanes - used), jnp.bfloat16),
        ],
        axis=1,
    )
    width = payload.shape[1]
    halves = payload.reshape(2, half_s, width)
    wide = jnp.broadcast_to(
        halves[None, :, None], (n_row // 2, 2, per_row, half_s, width)
    ).reshape(n_dev, half_s, width)
    mine = lax.all_to_all(wide, AXES, 0, 0, tiled=True)
    other = lax.ppermute(mine, "row", [(r, r ^ 1) for r in range(n_row)])
    core = lax.axis_index("row") % 2
    pos = lax.iota(jnp.int32, files)
    file_id = (
        (pos % half_f) // half_s * shard + (pos // half_f ^ core) * half_s + pos % half_s
    )
    mine2 = mine.reshape(half_f, width)
    other2 = other.reshape(half_f, width)
    tails = jnp.concatenate([mine2[:, feat:], other2[:, feat:]], axis=0)
    probes_int = join3(
        jnp.stack([tails[:, k * n_probe : (k + 1) * n_probe] for k in range(3)])
    ).T
    scale = (tails[:, 3 * n_probe].astype(jnp.float32) / feat)[:, None]
    mask_got = mine[:, :, feat + 3 * n_probe + 1 : feat + used].reshape(n_dev, -1)
    mask_got = mask_got[:, : local_blocks * nb]
    mask_full = mask_got.reshape(n_row, per_row, local_blocks, nb)[:, 0].reshape(nb, nb)
    col_block = file_id // blk
    live = file_id % blk < jnp.take(counts, col_block, axis=0)
    rowmask = jnp.where(
        live[None, :] & (jnp.take(mask_full, col_block, axis=1) == 1), 1.0, 0.0
    ).astype(jnp.float32)
    state = dense_call(mine2, other2, scale, rowmask, probes_int, feat)
    first = lax.dynamic_slice_in_dim(state, core * half_f + me * half_s, half_s, 1)
    second = lax.dynamic_slice_in_dim(state, (1 - core) * half_f + me * half_s, half_s, 1)
    return jnp.concatenate([first, second], axis=1)


def normalize(embed):
    values = embed.astype(jnp.float32)
    return (values * lax.rsqrt(jnp.mean(values * values, axis=1, keepdims=True) + 1e-06)).astype(
        jnp.bfloat16
    )


def split3(x):
    hi = lax.reduce_precision(x, exponent_bits=8, mantissa_bits=7)
    rest = x - hi
    mid = lax.reduce_precision(rest, exponent_bits=8, mantissa_bits=7)
    lo = rest - mid
    return jnp.stack([hi, mid, lo]).astype(jnp.bfloat16)


def join3(parts):
    parts = parts.astype(jnp.float32)
    return (parts[0] + parts[1]) + parts[2]


def pack_rows(flat, width):
    rows = -(-flat.shape[0] // width)
    return jnp.pad(flat, (0, rows * width - flat.shape[0])).reshape(rows, width), rows


def body(embed, beta, block_mask, counts, probes):
    n_dev = lax.axis_size("row") * lax.axis_size("col")
    n_row = lax.axis_size("row")
    me = lax.axis_index(AXES)
    shard, feat = embed.shape
    files = shard * n_dev
    nb = block_mask.shape[1]
    blk = files // nb
    local_blocks = block_mask.shape[0]

    unit_own = normalize(embed)
    beta_rows, beta_n = pack_rows(beta, feat)
    mask_rows, mask_n = pack_rows(block_mask.reshape(-1).astype(jnp.bfloat16), feat)
    replicate = files * files <= REPLICATE_CELLS
    n_probe = probes.shape[0]
    if (
        replicate
        and n_row % 2 == 0
        and shard % 2 == 0
        and blk % shard == 0
        and (blk // 2) % 8 == 0
        and files % 128 == 0
    ):
        return dense_path(unit_own, beta, block_mask, counts, probes, n_dev, n_row, me)
    if replicate:
        mask_flat = block_mask.reshape(-1).astype(jnp.bfloat16)
        mask_cols = -(-mask_flat.shape[0] // shard)
        mask_part = jnp.pad(mask_flat, (0, shard * mask_cols - mask_flat.shape[0]))
        used = 3 * n_probe + 1 + mask_cols
        lanes = -(-used // 128) * 128
        extra_cols = jnp.concatenate(
            [
                jnp.moveaxis(split3(probes.T), 0, 1).reshape(shard, 3 * n_probe),
                beta[:, None],
                mask_part.reshape(shard, mask_cols),
                jnp.zeros((shard, lanes - used), jnp.bfloat16),
            ],
            axis=1,
        )
        got = gather_halves(jnp.concatenate([unit_own, extra_cols], axis=1), n_dev, n_row)
        unit_all = got[:, :, :feat].reshape(files, feat)
        tail = got[:, :, feat:].reshape(files, lanes)
        probes_t = join3(
            jnp.stack([tail[:, k * n_probe : (k + 1) * n_probe] for k in range(3)])
        )
        beta_all = tail[:, 3 * n_probe]
        mask_got = got[:, :, feat + 3 * n_probe + 1 : feat + used].reshape(n_dev, -1)
        mask_got = mask_got[:, : local_blocks * nb]
    else:
        unit_all = gather_rows(unit_own, n_dev).reshape(files, feat)
        extra = gather_rows(jnp.concatenate([beta_rows, mask_rows], axis=0), n_dev)
        beta_all = extra[:, 0, :shard].reshape(files)
        mask_got = extra[:, beta_n:, :].reshape(n_dev, -1)[:, : local_blocks * nb]
    per_row = n_dev // n_row
    mask_full = (
        mask_got.reshape(n_row, per_row, local_blocks, nb)[:, 0].reshape(nb, nb).astype(jnp.int32)
    )
    scale_all = beta_all.astype(jnp.float32) / feat

    col_ids = lax.iota(jnp.int32, files)
    col_block = col_ids // blk
    in_block = lax.iota(jnp.int32, blk)
    col_live = (in_block[None, :] < counts[:, None]).reshape(files)

    if replicate:
        gram = lax.dot_general(
            unit_all, unit_all, (((1,), (1,)), ((), ())), preferred_element_type=jnp.float32
        )
        scores = gram * scale_all[:, None]
        block_ok = jnp.broadcast_to(
            (mask_full == 1)[:, None, :, None], (nb, blk, nb, blk)
        ).reshape(files, files)
        allowed = block_ok & col_live[None, :] & (col_ids[:, None] != col_ids[None, :])
        masked = jnp.where(allowed, scores, -1e30)
        row_top = jnp.max(masked, axis=1)
        row_mass = jnp.sum(jnp.where(allowed, jnp.exp(masked - row_top[:, None]), 0.0), axis=1)
        weights = jnp.where(allowed, jnp.exp(masked - row_top[:, None]) / row_mass[:, None], 0.0)
        col_mass = jnp.sum(weights, axis=0)
        inv_root = lax.rsqrt((1.0 + col_mass) * 0.5)
        affinity = weights.astype(jnp.bfloat16)
        state = probes_t
        for sweep in range(ITERS):
            scaled = (state * inv_root[:, None]).astype(jnp.bfloat16)
            row_part = jnp.dot(affinity, scaled, preferred_element_type=jnp.float32)
            col_part = lax.dot_general(
                affinity, scaled, (((0,), (0,)), ((), ())), preferred_element_type=jnp.float32
            )
            state = (row_part + col_part) * (0.5 * inv_root)[:, None]
        return lax.dynamic_slice_in_dim(state, me * shard, shard, 0).T

    own_ids = me * shard + lax.iota(jnp.int32, shard)
    own_block = own_ids // blk
    gram = lax.dot_general(
        unit_own, unit_all, (((1,), (1,)), ((), ())), preferred_element_type=jnp.float32
    )
    own_scale = lax.dynamic_slice_in_dim(scale_all, me * shard, shard, 0)
    scores = gram * own_scale[:, None]
    row_ok = jnp.take(jnp.take(mask_full, own_block, axis=0), col_block, axis=1) == 1
    allowed = row_ok & col_live[None, :] & (own_ids[:, None] != col_ids[None, :])
    masked = jnp.where(allowed, scores, -1e30)
    row_top = jnp.max(masked, axis=1)
    row_mass = jnp.sum(jnp.where(allowed, jnp.exp(masked - row_top[:, None]), 0.0), axis=1)
    weights = jnp.where(allowed, jnp.exp(masked - row_top[:, None]) / row_mass[:, None], 0.0)
    stats = gather_rows(jnp.stack([row_top, row_mass], axis=1), n_dev).reshape(files, 2)
    top_all, mass_all = stats[:, 0], stats[:, 1]
    scores_t = gram * scale_all[None, :]
    own_live = jnp.take(col_live, own_ids, axis=0)
    col_ok = jnp.take(jnp.take(mask_full, col_block, axis=0), own_block, axis=1).T == 1
    allowed_t = col_ok & own_live[:, None] & (own_ids[:, None] != col_ids[None, :])
    masked_t = jnp.where(allowed_t, scores_t, -1e30)
    weights_t = jnp.where(
        allowed_t, jnp.exp(masked_t - top_all[None, :]) / mass_all[None, :], 0.0
    )
    col_mass = jnp.sum(weights_t, axis=1)
    inv_root = lax.rsqrt((1.0 + col_mass) * 0.5)
    aff_rows = weights.astype(jnp.bfloat16)
    aff_cols = weights_t.astype(jnp.bfloat16)
    state = probes
    for sweep in range(ITERS):
        scaled = (state * inv_root[None, :]).astype(jnp.bfloat16)
        scaled_all = gather_rows(scaled.T, n_dev).reshape(files, probes.shape[0])
        row_part = jnp.dot(aff_rows, scaled_all, preferred_element_type=jnp.float32)
        col_part = jnp.dot(aff_cols, scaled_all, preferred_element_type=jnp.float32)
        state = ((row_part + col_part) * (0.5 * inv_root)[:, None]).T
    return state


def solution(mesh):
    placed = (
        P(AXES, None),
        P(AXES),
        P("row", None),
        P(),
        P(None, AXES),
    )
    return jax.shard_map(body, mesh=mesh, in_specs=placed, out_specs=P(None, AXES), check_vma=False)
```

```python
import jax
import jax.numpy as jnp
from jax import lax
from jax.experimental import pallas as pl
from jax.experimental.pallas import tpu as pltpu
from jax.sharding import PartitionSpec as P

ITERS = 2
AXES = ("row", "col")
A2A_BYTES = 8 << 20
REPLICATE_CELLS = 1 << 21


def gather_rows(x, n_dev):
    if n_dev * x.size * x.dtype.itemsize <= A2A_BYTES:
        wide = jnp.broadcast_to(x[None], (n_dev,) + x.shape)
        return lax.all_to_all(wide, AXES, 0, 0, tiled=True)
    return lax.all_gather(x, AXES, axis=0, tiled=False)


def gather_halves(x, n_dev, n_row):
    if n_row % 2:
        return gather_rows(x, n_dev)
    rows = x.shape[0] + x.shape[0] % 2
    halves = jnp.pad(x, ((0, rows - x.shape[0]), (0, 0))).reshape(2, rows // 2, x.shape[1])
    per_row = n_dev // n_row
    wide = jnp.broadcast_to(
        halves[None, :, None], (n_row // 2, 2, per_row, rows // 2, x.shape[1])
    ).reshape(n_dev, rows // 2, x.shape[1])
    mine = lax.all_to_all(wide, AXES, 0, 0, tiled=True)
    other = lax.ppermute(mine, "row", [(r, r ^ 1) for r in range(n_row)])
    first = lax.axis_index("row") % 2 == 0
    low = jnp.where(first, mine, other)
    high = jnp.where(first, other, mine)
    return jnp.concatenate([low, high], axis=1)[:, : x.shape[0]]


def dense_kernel(n_iter, tile, beta_lane, mine_ref, other_ref, rowmask_ref, probes_ref, out_ref, unit_t, scale_s, aff_s):
    feat, files = unit_t.shape
    half = files // 2
    runs = half // tile
    for k, ref in enumerate((mine_ref, other_ref)):
        unit_t[:, k * half : (k + 1) * half] = (
            ref[:, 0:feat].astype(jnp.float32).T.astype(jnp.bfloat16)
        )
        scale_s[k * half : (k + 1) * half, :] = (
            ref[:, beta_lane : beta_lane + 1].astype(jnp.float32) / feat
        )
    col_pos = lax.broadcasted_iota(jnp.int32, (tile, files), 1)
    row_pos = lax.broadcasted_iota(jnp.int32, (tile, files), 0)

    def step(t, colsum):
        p0 = pl.multiple_of(t * tile, tile)
        q0 = pl.multiple_of((t % runs) * tile, tile)
        rows = jnp.where(t < runs, mine_ref[pl.ds(q0, tile), 0:feat], other_ref[pl.ds(q0, tile), 0:feat])
        gram = jnp.dot(rows, unit_t[...], preferred_element_type=jnp.float32)
        scores = gram * scale_s[pl.ds(p0, tile), :]
        ok = (rowmask_ref[pl.ds(t % runs, 1), :] > 0.0) & (row_pos + p0 != col_pos)
        masked = jnp.where(ok, scores, -1e30)
        top = jnp.max(masked, axis=1, keepdims=True)
        e = jnp.where(ok, jnp.exp(masked - top), 0.0)
        mass = jnp.sum(e, axis=1, keepdims=True)
        weights = e / mass
        aff_s[pl.ds(p0, tile), :] = weights.astype(jnp.bfloat16)
        return colsum + jnp.sum(weights, axis=0, keepdims=True)

    colsum = lax.fori_loop(0, files // tile, step, jnp.zeros((1, files), jnp.float32))
    inv_root = lax.rsqrt((1.0 + colsum) * 0.5)
    state = probes_ref[...]
    for sweep in range(n_iter):
        scaled_f = (state * inv_root).astype(jnp.bfloat16).astype(jnp.float32)
        scaled = scaled_f.astype(jnp.bfloat16)
        row_t = jnp.dot(aff_s[...], scaled_f.T.astype(jnp.bfloat16), preferred_element_type=jnp.float32)
        col_part = jnp.dot(scaled, aff_s[...], preferred_element_type=jnp.float32)
        state = (row_t.T + col_part) * (0.5 * inv_root)
    out_ref[...] = state


def dense_call(mine, other, rowmask, probes_int, feat, beta_lane):
    files = 2 * mine.shape[0]
    tile = files // (2 * rowmask.shape[0])
    vmem = pl.BlockSpec(memory_space=pltpu.VMEM)
    return pl.pallas_call(
        lambda *refs: dense_kernel(ITERS, tile, beta_lane, *refs),
        out_shape=jax.ShapeDtypeStruct(probes_int.shape, jnp.float32),
        in_specs=[vmem] * 4,
        out_specs=vmem,
        scratch_shapes=[
            pltpu.VMEM((feat, files), jnp.bfloat16),
            pltpu.VMEM((files, 1), jnp.float32),
            pltpu.VMEM((files, files), jnp.bfloat16),
        ],
        cost_estimate=pl.CostEstimate(
            flops=2 * files * files * feat + 4 * ITERS * files * files * probes_int.shape[0],
            transcendentals=files * files,
            bytes_accessed=files * mine.shape[1] * 2 + 8 * files * probes_int.shape[0],
        ),
    )(mine, other, rowmask, probes_int)


def dense_path(unit_own, beta, block_mask, counts, probes, n_dev, n_row, me):
    shard, feat = unit_own.shape
    files = shard * n_dev
    half_s = shard // 2
    half_f = files // 2
    nb = block_mask.shape[1]
    blk = files // nb
    local_blocks = block_mask.shape[0]
    n_probe = probes.shape[0]
    per_row = n_dev // n_row
    mask_flat = block_mask.reshape(-1).astype(jnp.bfloat16)
    mask_cols = -(-mask_flat.shape[0] // half_s)
    mask_part = jnp.pad(mask_flat, (0, half_s * mask_cols - mask_flat.shape[0]))
    mask_part = jnp.tile(mask_part.reshape(half_s, mask_cols), (2, 1))
    used = 3 * n_probe + 1 + mask_cols
    lanes = -(-used // 128) * 128
    payload = jnp.concatenate(
        [
            unit_own,
            jnp.moveaxis(split3(probes.T), 0, 1).reshape(shard, 3 * n_probe),
            beta[:, None],
            mask_part,
            jnp.zeros((shard, lanes - used), jnp.bfloat16),
        ],
        axis=1,
    )
    width = payload.shape[1]
    halves = payload.reshape(2, half_s, width)
    wide = jnp.broadcast_to(
        halves[None, :, None], (n_row // 2, 2, per_row, half_s, width)
    ).reshape(n_dev, half_s, width)
    mine = lax.all_to_all(wide, AXES, 0, 0, tiled=True)
    other = lax.ppermute(mine, "row", [(r, r ^ 1) for r in range(n_row)])
    core = lax.axis_index("row") % 2
    pos = lax.iota(jnp.int32, files)
    run = blk // 2
    in_run = lax.iota(jnp.int32, files) % run
    run_dev = in_run // half_s
    half_of = jnp.broadcast_to((lax.iota(jnp.int32, 2) ^ core)[:, None, None], (2, nb, run))
    in_block = (run_dev % (blk // shard)) * shard + half_of.reshape(files) * half_s + in_run % half_s
    block_counts = jnp.broadcast_to(counts[None, :, None], (2, nb, run)).reshape(files)
    live = in_block < block_counts
    mine2 = mine.reshape(half_f, width)
    other2 = other.reshape(half_f, width)
    tails = jnp.concatenate([mine2[:, feat:], other2[:, feat:]], axis=0)
    probes_int = join3(
        jnp.stack([tails[:, k * n_probe : (k + 1) * n_probe] for k in range(3)])
    ).T
    mask_got = mine[:, :, feat + 3 * n_probe + 1 : feat + used].reshape(n_dev, -1)
    mask_got = mask_got[:, : local_blocks * nb]
    mask_full = mask_got.reshape(n_row, per_row, local_blocks, nb)[:, 0].reshape(nb, nb)
    block_ok = jnp.broadcast_to((mask_full == 1)[:, None, :, None], (nb, 2, nb, run))
    rowmask = jnp.where(block_ok.reshape(nb, files) & live[None, :], 1.0, 0.0).astype(jnp.float32)
    state = dense_call(mine2, other2, rowmask, probes_int, feat, feat + 3 * n_probe)
    first = lax.dynamic_slice_in_dim(state, core * half_f + me * half_s, half_s, 1)
    second = lax.dynamic_slice_in_dim(state, (1 - core) * half_f + me * half_s, half_s, 1)
    return jnp.concatenate([first, second], axis=1)


def normalize(embed):
    values = embed.astype(jnp.float32)
    return (values * lax.rsqrt(jnp.mean(values * values, axis=1, keepdims=True) + 1e-06)).astype(
        jnp.bfloat16
    )


def split3(x):
    hi = lax.reduce_precision(x, exponent_bits=8, mantissa_bits=7)
    rest = x - hi
    mid = lax.reduce_precision(rest, exponent_bits=8, mantissa_bits=7)
    lo = rest - mid
    return jnp.stack([hi, mid, lo]).astype(jnp.bfloat16)


def join3(parts):
    parts = parts.astype(jnp.float32)
    return (parts[0] + parts[1]) + parts[2]


def pack_rows(flat, width):
    rows = -(-flat.shape[0] // width)
    return jnp.pad(flat, (0, rows * width - flat.shape[0])).reshape(rows, width), rows


def body(embed, beta, block_mask, counts, probes):
    n_dev = lax.axis_size("row") * lax.axis_size("col")
    n_row = lax.axis_size("row")
    me = lax.axis_index(AXES)
    shard, feat = embed.shape
    files = shard * n_dev
    nb = block_mask.shape[1]
    blk = files // nb
    local_blocks = block_mask.shape[0]

    unit_own = normalize(embed)
    beta_rows, beta_n = pack_rows(beta, feat)
    mask_rows, mask_n = pack_rows(block_mask.reshape(-1).astype(jnp.bfloat16), feat)
    replicate = files * files <= REPLICATE_CELLS
    n_probe = probes.shape[0]
    if (
        replicate
        and n_row % 2 == 0
        and shard % 2 == 0
        and blk % shard == 0
        and (blk // 2) % 8 == 0
        and files % 128 == 0
    ):
        return dense_path(unit_own, beta, block_mask, counts, probes, n_dev, n_row, me)
    if replicate:
        mask_flat = block_mask.reshape(-1).astype(jnp.bfloat16)
        mask_cols = -(-mask_flat.shape[0] // shard)
        mask_part = jnp.pad(mask_flat, (0, shard * mask_cols - mask_flat.shape[0]))
        used = 3 * n_probe + 1 + mask_cols
        lanes = -(-used // 128) * 128
        extra_cols = jnp.concatenate(
            [
                jnp.moveaxis(split3(probes.T), 0, 1).reshape(shard, 3 * n_probe),
                beta[:, None],
                mask_part.reshape(shard, mask_cols),
                jnp.zeros((shard, lanes - used), jnp.bfloat16),
            ],
            axis=1,
        )
        got = gather_halves(jnp.concatenate([unit_own, extra_cols], axis=1), n_dev, n_row)
        unit_all = got[:, :, :feat].reshape(files, feat)
        tail = got[:, :, feat:].reshape(files, lanes)
        probes_t = join3(
            jnp.stack([tail[:, k * n_probe : (k + 1) * n_probe] for k in range(3)])
        )
        beta_all = tail[:, 3 * n_probe]
        mask_got = got[:, :, feat + 3 * n_probe + 1 : feat + used].reshape(n_dev, -1)
        mask_got = mask_got[:, : local_blocks * nb]
    else:
        unit_all = gather_rows(unit_own, n_dev).reshape(files, feat)
        extra = gather_rows(jnp.concatenate([beta_rows, mask_rows], axis=0), n_dev)
        beta_all = extra[:, 0, :shard].reshape(files)
        mask_got = extra[:, beta_n:, :].reshape(n_dev, -1)[:, : local_blocks * nb]
    per_row = n_dev // n_row
    mask_full = (
        mask_got.reshape(n_row, per_row, local_blocks, nb)[:, 0].reshape(nb, nb).astype(jnp.int32)
    )
    scale_all = beta_all.astype(jnp.float32) / feat

    col_ids = lax.iota(jnp.int32, files)
    col_block = col_ids // blk
    in_block = lax.iota(jnp.int32, blk)
    col_live = (in_block[None, :] < counts[:, None]).reshape(files)

    if replicate:
        gram = lax.dot_general(
            unit_all, unit_all, (((1,), (1,)), ((), ())), preferred_element_type=jnp.float32
        )
        scores = gram * scale_all[:, None]
        block_ok = jnp.broadcast_to(
            (mask_full == 1)[:, None, :, None], (nb, blk, nb, blk)
        ).reshape(files, files)
        allowed = block_ok & col_live[None, :] & (col_ids[:, None] != col_ids[None, :])
        masked = jnp.where(allowed, scores, -1e30)
        row_top = jnp.max(masked, axis=1)
        row_mass = jnp.sum(jnp.where(allowed, jnp.exp(masked - row_top[:, None]), 0.0), axis=1)
        weights = jnp.where(allowed, jnp.exp(masked - row_top[:, None]) / row_mass[:, None], 0.0)
        col_mass = jnp.sum(weights, axis=0)
        inv_root = lax.rsqrt((1.0 + col_mass) * 0.5)
        affinity = weights.astype(jnp.bfloat16)
        state = probes_t
        for sweep in range(ITERS):
            scaled = (state * inv_root[:, None]).astype(jnp.bfloat16)
            row_part = jnp.dot(affinity, scaled, preferred_element_type=jnp.float32)
            col_part = lax.dot_general(
                affinity, scaled, (((0,), (0,)), ((), ())), preferred_element_type=jnp.float32
            )
            state = (row_part + col_part) * (0.5 * inv_root)[:, None]
        return lax.dynamic_slice_in_dim(state, me * shard, shard, 0).T

    own_ids = me * shard + lax.iota(jnp.int32, shard)
    own_block = own_ids // blk
    gram = lax.dot_general(
        unit_own, unit_all, (((1,), (1,)), ((), ())), preferred_element_type=jnp.float32
    )
    own_scale = lax.dynamic_slice_in_dim(scale_all, me * shard, shard, 0)
    scores = gram * own_scale[:, None]
    row_ok = jnp.take(jnp.take(mask_full, own_block, axis=0), col_block, axis=1) == 1
    allowed = row_ok & col_live[None, :] & (own_ids[:, None] != col_ids[None, :])
    masked = jnp.where(allowed, scores, -1e30)
    row_top = jnp.max(masked, axis=1)
    row_mass = jnp.sum(jnp.where(allowed, jnp.exp(masked - row_top[:, None]), 0.0), axis=1)
    weights = jnp.where(allowed, jnp.exp(masked - row_top[:, None]) / row_mass[:, None], 0.0)
    stats = gather_rows(jnp.stack([row_top, row_mass], axis=1), n_dev).reshape(files, 2)
    top_all, mass_all = stats[:, 0], stats[:, 1]
    scores_t = gram * scale_all[None, :]
    own_live = jnp.take(col_live, own_ids, axis=0)
    col_ok = jnp.take(jnp.take(mask_full, col_block, axis=0), own_block, axis=1).T == 1
    allowed_t = col_ok & own_live[:, None] & (own_ids[:, None] != col_ids[None, :])
    masked_t = jnp.where(allowed_t, scores_t, -1e30)
    weights_t = jnp.where(
        allowed_t, jnp.exp(masked_t - top_all[None, :]) / mass_all[None, :], 0.0
    )
    col_mass = jnp.sum(weights_t, axis=1)
    inv_root = lax.rsqrt((1.0 + col_mass) * 0.5)
    aff_rows = weights.astype(jnp.bfloat16)
    aff_cols = weights_t.astype(jnp.bfloat16)
    state = probes
    for sweep in range(ITERS):
        scaled = (state * inv_root[None, :]).astype(jnp.bfloat16)
        scaled_all = gather_rows(scaled.T, n_dev).reshape(files, probes.shape[0])
        row_part = jnp.dot(aff_rows, scaled_all, preferred_element_type=jnp.float32)
        col_part = jnp.dot(aff_cols, scaled_all, preferred_element_type=jnp.float32)
        state = ((row_part + col_part) * (0.5 * inv_root)[:, None]).T
    return state


def solution(mesh):
    placed = (
        P(AXES, None),
        P(AXES),
        P("row", None),
        P(),
        P(None, AXES),
    )
    return jax.shard_map(body, mesh=mesh, in_specs=placed, out_specs=P(None, AXES), check_vma=False)
```

```python
import jax
import jax.numpy as jnp
from jax import lax
from jax.experimental import pallas as pl
from jax.experimental.pallas import tpu as pltpu
from jax.sharding import PartitionSpec as P

ITERS = 2
AXES = ("row", "col")
A2A_BYTES = 8 << 20
REPLICATE_CELLS = 1 << 21


def gather_rows(x, n_dev):
    if n_dev * x.size * x.dtype.itemsize <= A2A_BYTES:
        wide = jnp.broadcast_to(x[None], (n_dev,) + x.shape)
        return lax.all_to_all(wide, AXES, 0, 0, tiled=True)
    return lax.all_gather(x, AXES, axis=0, tiled=False)


def gather_halves(x, n_dev, n_row):
    if n_row % 2:
        return gather_rows(x, n_dev)
    rows = x.shape[0] + x.shape[0] % 2
    halves = jnp.pad(x, ((0, rows - x.shape[0]), (0, 0))).reshape(2, rows // 2, x.shape[1])
    per_row = n_dev // n_row
    wide = jnp.broadcast_to(
        halves[None, :, None], (n_row // 2, 2, per_row, rows // 2, x.shape[1])
    ).reshape(n_dev, rows // 2, x.shape[1])
    mine = lax.all_to_all(wide, AXES, 0, 0, tiled=True)
    other = lax.ppermute(mine, "row", [(r, r ^ 1) for r in range(n_row)])
    first = lax.axis_index("row") % 2 == 0
    low = jnp.where(first, mine, other)
    high = jnp.where(first, other, mine)
    return jnp.concatenate([low, high], axis=1)[:, : x.shape[0]]


def dense_kernel(n_iter, tile, beta_lane, mine_ref, other_ref, rowmask_ref, probes_ref, out_ref, unit_t, unit_s, scale_s, aff_s):
    feat, files = unit_t.shape
    half = files // 2
    runs = half // tile
    for k, ref in enumerate((mine_ref, other_ref)):
        unit_s[k * half : (k + 1) * half, :] = ref[:, 0:feat]
        unit_t[:, k * half : (k + 1) * half] = (
            ref[:, 0:feat].astype(jnp.float32).T.astype(jnp.bfloat16)
        )
        scale_s[k * half : (k + 1) * half, :] = (
            ref[:, beta_lane : beta_lane + 1].astype(jnp.float32) / feat
        )
    col_pos = lax.broadcasted_iota(jnp.int32, (tile, files), 1)
    row_pos = lax.broadcasted_iota(jnp.int32, (tile, files), 0)

    def step(t, colsum):
        p0 = pl.multiple_of(t * tile, tile)
        gram = jnp.dot(unit_s[pl.ds(p0, tile), :], unit_t[...], preferred_element_type=jnp.float32)
        scores = gram * scale_s[pl.ds(p0, tile), :]
        ok = (rowmask_ref[pl.ds(t % runs, 1), :] > 0.0) & (row_pos + p0 != col_pos)
        masked = jnp.where(ok, scores, -1e30)
        top = jnp.max(masked, axis=1, keepdims=True)
        e = jnp.exp(masked - top)
        mass = jnp.sum(e, axis=1, keepdims=True)
        weights = e * (1.0 / mass)
        aff_s[pl.ds(p0, tile), :] = weights.astype(jnp.bfloat16)
        return colsum + jnp.sum(weights, axis=0, keepdims=True)

    colsum = lax.fori_loop(0, files // tile, step, jnp.zeros((1, files), jnp.float32))
    inv_root = lax.rsqrt((1.0 + colsum) * 0.5)
    state = probes_ref[...]
    for sweep in range(n_iter):
        scaled_f = (state * inv_root).astype(jnp.bfloat16).astype(jnp.float32)
        scaled = scaled_f.astype(jnp.bfloat16)
        row_t = jnp.dot(aff_s[...], scaled_f.T.astype(jnp.bfloat16), preferred_element_type=jnp.float32)
        col_part = jnp.dot(scaled, aff_s[...], preferred_element_type=jnp.float32)
        state = (row_t.T + col_part) * (0.5 * inv_root)
    out_ref[...] = state


def dense_call(mine, other, rowmask, probes_int, feat, beta_lane):
    files = 2 * mine.shape[0]
    tile = files // (2 * rowmask.shape[0])
    vmem = pl.BlockSpec(memory_space=pltpu.VMEM)
    return pl.pallas_call(
        lambda *refs: dense_kernel(ITERS, tile, beta_lane, *refs),
        out_shape=jax.ShapeDtypeStruct(probes_int.shape, jnp.float32),
        in_specs=[vmem] * 4,
        out_specs=vmem,
        scratch_shapes=[
            pltpu.VMEM((feat, files), jnp.bfloat16),
            pltpu.VMEM((files, feat), jnp.bfloat16),
            pltpu.VMEM((files, 1), jnp.float32),
            pltpu.VMEM((files, files), jnp.bfloat16),
        ],
        cost_estimate=pl.CostEstimate(
            flops=2 * files * files * feat + 4 * ITERS * files * files * probes_int.shape[0],
            transcendentals=files * files,
            bytes_accessed=files * mine.shape[1] * 2 + 8 * files * probes_int.shape[0],
        ),
    )(mine, other, rowmask, probes_int)


def dense_path(unit_own, beta, block_mask, counts, probes, n_dev, n_row, me):
    shard, feat = unit_own.shape
    files = shard * n_dev
    half_s = shard // 2
    half_f = files // 2
    nb = block_mask.shape[1]
    blk = files // nb
    local_blocks = block_mask.shape[0]
    n_probe = probes.shape[0]
    per_row = n_dev // n_row
    mask_flat = block_mask.reshape(-1).astype(jnp.bfloat16)
    mask_cols = -(-mask_flat.shape[0] // half_s)
    mask_part = jnp.pad(mask_flat, (0, half_s * mask_cols - mask_flat.shape[0]))
    mask_part = jnp.tile(mask_part.reshape(half_s, mask_cols), (2, 1))
    used = 3 * n_probe + 1 + mask_cols
    lanes = -(-used // 128) * 128
    payload = jnp.concatenate(
        [
            unit_own,
            jnp.moveaxis(split3(probes.T), 0, 1).reshape(shard, 3 * n_probe),
            beta[:, None],
            mask_part,
            jnp.zeros((shard, lanes - used), jnp.bfloat16),
        ],
        axis=1,
    )
    width = payload.shape[1]
    halves = payload.reshape(2, half_s, width)
    wide = jnp.broadcast_to(
        halves[None, :, None], (n_row // 2, 2, per_row, half_s, width)
    ).reshape(n_dev, half_s, width)
    mine = lax.all_to_all(wide, AXES, 0, 0, tiled=True)
    other = lax.ppermute(mine, "row", [(r, r ^ 1) for r in range(n_row)])
    core = lax.axis_index("row") % 2
    pos = lax.iota(jnp.int32, files)
    run = blk // 2
    in_run = lax.iota(jnp.int32, files) % run
    run_dev = in_run // half_s
    half_of = jnp.broadcast_to((lax.iota(jnp.int32, 2) ^ core)[:, None, None], (2, nb, run))
    in_block = (run_dev % (blk // shard)) * shard + half_of.reshape(files) * half_s + in_run % half_s
    block_counts = jnp.broadcast_to(counts[None, :, None], (2, nb, run)).reshape(files)
    live = in_block < block_counts
    mine2 = mine.reshape(half_f, width)
    other2 = other.reshape(half_f, width)
    tails = jnp.concatenate([mine2[:, feat:], other2[:, feat:]], axis=0)
    probes_int = join3(
        jnp.stack([tails[:, k * n_probe : (k + 1) * n_probe] for k in range(3)])
    ).T
    mask_got = mine[:, :, feat + 3 * n_probe + 1 : feat + used].reshape(n_dev, -1)
    mask_got = mask_got[:, : local_blocks * nb]
    mask_full = mask_got.reshape(n_row, per_row, local_blocks, nb)[:, 0].reshape(nb, nb)
    block_ok = jnp.broadcast_to((mask_full == 1)[:, None, :, None], (nb, 2, nb, run))
    rowmask = jnp.where(block_ok.reshape(nb, files) & live[None, :], 1.0, 0.0).astype(jnp.float32)
    state = dense_call(mine2, other2, rowmask, probes_int, feat, feat + 3 * n_probe)
    first = lax.dynamic_slice_in_dim(state, core * half_f + me * half_s, half_s, 1)
    second = lax.dynamic_slice_in_dim(state, (1 - core) * half_f + me * half_s, half_s, 1)
    return jnp.concatenate([first, second], axis=1)


def normalize(embed):
    values = embed.astype(jnp.float32)
    return (values * lax.rsqrt(jnp.mean(values * values, axis=1, keepdims=True) + 1e-06)).astype(
        jnp.bfloat16
    )


def split3(x):
    hi = lax.reduce_precision(x, exponent_bits=8, mantissa_bits=7)
    rest = x - hi
    mid = lax.reduce_precision(rest, exponent_bits=8, mantissa_bits=7)
    lo = rest - mid
    return jnp.stack([hi, mid, lo]).astype(jnp.bfloat16)


def join3(parts):
    parts = parts.astype(jnp.float32)
    return (parts[0] + parts[1]) + parts[2]


def pack_rows(flat, width):
    rows = -(-flat.shape[0] // width)
    return jnp.pad(flat, (0, rows * width - flat.shape[0])).reshape(rows, width), rows


def body(embed, beta, block_mask, counts, probes):
    n_dev = lax.axis_size("row") * lax.axis_size("col")
    n_row = lax.axis_size("row")
    me = lax.axis_index(AXES)
    shard, feat = embed.shape
    files = shard * n_dev
    nb = block_mask.shape[1]
    blk = files // nb
    local_blocks = block_mask.shape[0]

    unit_own = normalize(embed)
    beta_rows, beta_n = pack_rows(beta, feat)
    mask_rows, mask_n = pack_rows(block_mask.reshape(-1).astype(jnp.bfloat16), feat)
    replicate = files * files <= REPLICATE_CELLS
    n_probe = probes.shape[0]
    if (
        replicate
        and n_row % 2 == 0
        and shard % 2 == 0
        and blk % shard == 0
        and (blk // 2) % 8 == 0
        and files % 128 == 0
    ):
        return dense_path(unit_own, beta, block_mask, counts, probes, n_dev, n_row, me)
    if replicate:
        mask_flat = block_mask.reshape(-1).astype(jnp.bfloat16)
        mask_cols = -(-mask_flat.shape[0] // shard)
        mask_part = jnp.pad(mask_flat, (0, shard * mask_cols - mask_flat.shape[0]))
        used = 3 * n_probe + 1 + mask_cols
        lanes = -(-used // 128) * 128
        extra_cols = jnp.concatenate(
            [
                jnp.moveaxis(split3(probes.T), 0, 1).reshape(shard, 3 * n_probe),
                beta[:, None],
                mask_part.reshape(shard, mask_cols),
                jnp.zeros((shard, lanes - used), jnp.bfloat16),
            ],
            axis=1,
        )
        got = gather_halves(jnp.concatenate([unit_own, extra_cols], axis=1), n_dev, n_row)
        unit_all = got[:, :, :feat].reshape(files, feat)
        tail = got[:, :, feat:].reshape(files, lanes)
        probes_t = join3(
            jnp.stack([tail[:, k * n_probe : (k + 1) * n_probe] for k in range(3)])
        )
        beta_all = tail[:, 3 * n_probe]
        mask_got = got[:, :, feat + 3 * n_probe + 1 : feat + used].reshape(n_dev, -1)
        mask_got = mask_got[:, : local_blocks * nb]
    else:
        unit_all = gather_rows(unit_own, n_dev).reshape(files, feat)
        extra = gather_rows(jnp.concatenate([beta_rows, mask_rows], axis=0), n_dev)
        beta_all = extra[:, 0, :shard].reshape(files)
        mask_got = extra[:, beta_n:, :].reshape(n_dev, -1)[:, : local_blocks * nb]
    per_row = n_dev // n_row
    mask_full = (
        mask_got.reshape(n_row, per_row, local_blocks, nb)[:, 0].reshape(nb, nb).astype(jnp.int32)
    )
    scale_all = beta_all.astype(jnp.float32) / feat

    col_ids = lax.iota(jnp.int32, files)
    col_block = col_ids // blk
    in_block = lax.iota(jnp.int32, blk)
    col_live = (in_block[None, :] < counts[:, None]).reshape(files)

    if replicate:
        gram = lax.dot_general(
            unit_all, unit_all, (((1,), (1,)), ((), ())), preferred_element_type=jnp.float32
        )
        scores = gram * scale_all[:, None]
        block_ok = jnp.broadcast_to(
            (mask_full == 1)[:, None, :, None], (nb, blk, nb, blk)
        ).reshape(files, files)
        allowed = block_ok & col_live[None, :] & (col_ids[:, None] != col_ids[None, :])
        masked = jnp.where(allowed, scores, -1e30)
        row_top = jnp.max(masked, axis=1)
        row_mass = jnp.sum(jnp.where(allowed, jnp.exp(masked - row_top[:, None]), 0.0), axis=1)
        weights = jnp.where(allowed, jnp.exp(masked - row_top[:, None]) / row_mass[:, None], 0.0)
        col_mass = jnp.sum(weights, axis=0)
        inv_root = lax.rsqrt((1.0 + col_mass) * 0.5)
        affinity = weights.astype(jnp.bfloat16)
        state = probes_t
        for sweep in range(ITERS):
            scaled = (state * inv_root[:, None]).astype(jnp.bfloat16)
            row_part = jnp.dot(affinity, scaled, preferred_element_type=jnp.float32)
            col_part = lax.dot_general(
                affinity, scaled, (((0,), (0,)), ((), ())), preferred_element_type=jnp.float32
            )
            state = (row_part + col_part) * (0.5 * inv_root)[:, None]
        return lax.dynamic_slice_in_dim(state, me * shard, shard, 0).T

    own_ids = me * shard + lax.iota(jnp.int32, shard)
    own_block = own_ids // blk
    gram = lax.dot_general(
        unit_own, unit_all, (((1,), (1,)), ((), ())), preferred_element_type=jnp.float32
    )
    own_scale = lax.dynamic_slice_in_dim(scale_all, me * shard, shard, 0)
    scores = gram * own_scale[:, None]
    row_ok = jnp.take(jnp.take(mask_full, own_block, axis=0), col_block, axis=1) == 1
    allowed = row_ok & col_live[None, :] & (own_ids[:, None] != col_ids[None, :])
    masked = jnp.where(allowed, scores, -1e30)
    row_top = jnp.max(masked, axis=1)
    row_mass = jnp.sum(jnp.where(allowed, jnp.exp(masked - row_top[:, None]), 0.0), axis=1)
    weights = jnp.where(allowed, jnp.exp(masked - row_top[:, None]) / row_mass[:, None], 0.0)
    stats = gather_rows(jnp.stack([row_top, row_mass], axis=1), n_dev).reshape(files, 2)
    top_all, mass_all = stats[:, 0], stats[:, 1]
    scores_t = gram * scale_all[None, :]
    own_live = jnp.take(col_live, own_ids, axis=0)
    col_ok = jnp.take(jnp.take(mask_full, col_block, axis=0), own_block, axis=1).T == 1
    allowed_t = col_ok & own_live[:, None] & (own_ids[:, None] != col_ids[None, :])
    masked_t = jnp.where(allowed_t, scores_t, -1e30)
    weights_t = jnp.where(
        allowed_t, jnp.exp(masked_t - top_all[None, :]) / mass_all[None, :], 0.0
    )
    col_mass = jnp.sum(weights_t, axis=1)
    inv_root = lax.rsqrt((1.0 + col_mass) * 0.5)
    aff_rows = weights.astype(jnp.bfloat16)
    aff_cols = weights_t.astype(jnp.bfloat16)
    state = probes
    for sweep in range(ITERS):
        scaled = (state * inv_root[None, :]).astype(jnp.bfloat16)
        scaled_all = gather_rows(scaled.T, n_dev).reshape(files, probes.shape[0])
        row_part = jnp.dot(aff_rows, scaled_all, preferred_element_type=jnp.float32)
        col_part = jnp.dot(aff_cols, scaled_all, preferred_element_type=jnp.float32)
        state = ((row_part + col_part) * (0.5 * inv_root)[:, None]).T
    return state


def solution(mesh):
    placed = (
        P(AXES, None),
        P(AXES),
        P("row", None),
        P(),
        P(None, AXES),
    )
    return jax.shard_map(body, mesh=mesh, in_specs=placed, out_specs=P(None, AXES), check_vma=False)
```

```python
import jax
import jax.numpy as jnp
from jax import lax
from jax.experimental import pallas as pl
from jax.experimental.pallas import tpu as pltpu
from jax.sharding import PartitionSpec as P

ITERS = 2
AXES = ("row", "col")
A2A_BYTES = 8 << 20
REPLICATE_CELLS = 1 << 21


def gather_rows(x, n_dev):
    if n_dev * x.size * x.dtype.itemsize <= A2A_BYTES:
        wide = jnp.broadcast_to(x[None], (n_dev,) + x.shape)
        return lax.all_to_all(wide, AXES, 0, 0, tiled=True)
    return lax.all_gather(x, AXES, axis=0, tiled=False)


def gather_halves(x, n_dev, n_row):
    if n_row % 2:
        return gather_rows(x, n_dev)
    rows = x.shape[0] + x.shape[0] % 2
    halves = jnp.pad(x, ((0, rows - x.shape[0]), (0, 0))).reshape(2, rows // 2, x.shape[1])
    per_row = n_dev // n_row
    wide = jnp.broadcast_to(
        halves[None, :, None], (n_row // 2, 2, per_row, rows // 2, x.shape[1])
    ).reshape(n_dev, rows // 2, x.shape[1])
    mine = lax.all_to_all(wide, AXES, 0, 0, tiled=True)
    other = lax.ppermute(mine, "row", [(r, r ^ 1) for r in range(n_row)])
    first = lax.axis_index("row") % 2 == 0
    low = jnp.where(first, mine, other)
    high = jnp.where(first, other, mine)
    return jnp.concatenate([low, high], axis=1)[:, : x.shape[0]]


def dense_kernel(n_iter, tile, beta_lane, mine_ref, other_ref, rowmask_ref, probes_ref, out_ref, unit_t, unit_s, scale_s, aff_s):
    feat, files = unit_t.shape
    half = files // 2
    runs = half // tile
    for k, ref in enumerate((mine_ref, other_ref)):
        unit_s[k * half : (k + 1) * half, :] = ref[:, 0:feat]
        unit_t[:, k * half : (k + 1) * half] = (
            ref[:, 0:feat].astype(jnp.float32).T.astype(jnp.bfloat16)
        )
        scale_s[k * half : (k + 1) * half, :] = (
            ref[:, beta_lane : beta_lane + 1].astype(jnp.float32) / feat
        )
    per_tile = rowmask_ref.shape[1]
    run = tile // per_tile
    col_pos = lax.broadcasted_iota(jnp.int32, (tile, files), 1)
    row_pos = lax.broadcasted_iota(jnp.int32, (tile, files), 0)

    def step(t, colsum):
        p0 = pl.multiple_of(t * tile, tile)
        gram = jnp.dot(unit_s[pl.ds(p0, tile), :], unit_t[...], preferred_element_type=jnp.float32)
        scores = gram * scale_s[pl.ds(p0, tile), :]
        runs_here = rowmask_ref[t % runs]
        block_row = jnp.broadcast_to(runs_here[:, None, :], (per_tile, run, files)).reshape(tile, files)
        ok = (block_row > 0.0) & (row_pos + p0 != col_pos)
        masked = jnp.where(ok, scores, -1e30)
        top = jnp.max(masked, axis=1, keepdims=True)
        e = jnp.exp(masked - top)
        mass = jnp.sum(e, axis=1, keepdims=True)
        weights = e * (1.0 / mass)
        aff_s[pl.ds(p0, tile), :] = weights.astype(jnp.bfloat16)
        return colsum + jnp.sum(weights, axis=0, keepdims=True)

    colsum = lax.fori_loop(0, files // tile, step, jnp.zeros((1, files), jnp.float32))
    inv_root = lax.rsqrt((1.0 + colsum) * 0.5)
    state = probes_ref[...]
    for sweep in range(n_iter):
        scaled_f = (state * inv_root).astype(jnp.bfloat16).astype(jnp.float32)
        scaled = scaled_f.astype(jnp.bfloat16)
        row_t = jnp.dot(aff_s[...], scaled_f.T.astype(jnp.bfloat16), preferred_element_type=jnp.float32)
        col_part = jnp.dot(scaled, aff_s[...], preferred_element_type=jnp.float32)
        state = (row_t.T + col_part) * (0.5 * inv_root)
    out_ref[...] = state


def dense_call(mine, other, rowmask, probes_int, feat, beta_lane):
    files = 2 * mine.shape[0]
    run = files // (2 * rowmask.shape[0])
    tile = run
    while tile * 2 <= min(256, files // 2) and (files // 2) % (tile * 2) == 0:
        tile *= 2
    rowmask = rowmask.reshape(-1, tile // run, files)
    vmem = pl.BlockSpec(memory_space=pltpu.VMEM)
    return pl.pallas_call(
        lambda *refs: dense_kernel(ITERS, tile, beta_lane, *refs),
        out_shape=jax.ShapeDtypeStruct(probes_int.shape, jnp.float32),
        in_specs=[vmem] * 4,
        out_specs=vmem,
        scratch_shapes=[
            pltpu.VMEM((feat, files), jnp.bfloat16),
            pltpu.VMEM((files, feat), jnp.bfloat16),
            pltpu.VMEM((files, 1), jnp.float32),
            pltpu.VMEM((files, files), jnp.bfloat16),
        ],
        cost_estimate=pl.CostEstimate(
            flops=2 * files * files * feat + 4 * ITERS * files * files * probes_int.shape[0],
            transcendentals=files * files,
            bytes_accessed=files * mine.shape[1] * 2 + 8 * files * probes_int.shape[0],
        ),
    )(mine, other, rowmask, probes_int)


def dense_path(unit_own, beta, block_mask, counts, probes, n_dev, n_row, me):
    shard, feat = unit_own.shape
    files = shard * n_dev
    half_s = shard // 2
    half_f = files // 2
    nb = block_mask.shape[1]
    blk = files // nb
    local_blocks = block_mask.shape[0]
    n_probe = probes.shape[0]
    per_row = n_dev // n_row
    mask_flat = block_mask.reshape(-1).astype(jnp.bfloat16)
    mask_cols = -(-mask_flat.shape[0] // half_s)
    mask_part = jnp.pad(mask_flat, (0, half_s * mask_cols - mask_flat.shape[0]))
    mask_part = jnp.tile(mask_part.reshape(half_s, mask_cols), (2, 1))
    used = 3 * n_probe + 1 + mask_cols
    lanes = -(-used // 128) * 128
    payload = jnp.concatenate(
        [
            unit_own,
            jnp.moveaxis(split3(probes.T), 0, 1).reshape(shard, 3 * n_probe),
            beta[:, None],
            mask_part,
            jnp.zeros((shard, lanes - used), jnp.bfloat16),
        ],
        axis=1,
    )
    width = payload.shape[1]
    halves = payload.reshape(2, half_s, width)
    wide = jnp.broadcast_to(
        halves[None, :, None], (n_row // 2, 2, per_row, half_s, width)
    ).reshape(n_dev, half_s, width)
    mine = lax.all_to_all(wide, AXES, 0, 0, tiled=True)
    other = lax.ppermute(mine, "row", [(r, r ^ 1) for r in range(n_row)])
    core = lax.axis_index("row") % 2
    pos = lax.iota(jnp.int32, files)
    run = blk // 2
    in_run = lax.iota(jnp.int32, files) % run
    run_dev = in_run // half_s
    half_of = jnp.broadcast_to((lax.iota(jnp.int32, 2) ^ core)[:, None, None], (2, nb, run))
    in_block = (run_dev % (blk // shard)) * shard + half_of.reshape(files) * half_s + in_run % half_s
    block_counts = jnp.broadcast_to(counts[None, :, None], (2, nb, run)).reshape(files)
    live = in_block < block_counts
    mine2 = mine.reshape(half_f, width)
    other2 = other.reshape(half_f, width)
    tails = jnp.concatenate([mine2[:, feat:], other2[:, feat:]], axis=0)
    probes_int = join3(
        jnp.stack([tails[:, k * n_probe : (k + 1) * n_probe] for k in range(3)])
    ).T
    mask_got = mine[:, :, feat + 3 * n_probe + 1 : feat + used].reshape(n_dev, -1)
    mask_got = mask_got[:, : local_blocks * nb]
    mask_full = mask_got.reshape(n_row, per_row, local_blocks, nb)[:, 0].reshape(nb, nb)
    block_ok = jnp.broadcast_to((mask_full == 1)[:, None, :, None], (nb, 2, nb, run))
    rowmask = jnp.where(block_ok.reshape(nb, files) & live[None, :], 1.0, 0.0).astype(jnp.float32)
    state = dense_call(mine2, other2, rowmask, probes_int, feat, feat + 3 * n_probe)
    first = lax.dynamic_slice_in_dim(state, core * half_f + me * half_s, half_s, 1)
    second = lax.dynamic_slice_in_dim(state, (1 - core) * half_f + me * half_s, half_s, 1)
    return jnp.concatenate([first, second], axis=1)


def normalize(embed):
    values = embed.astype(jnp.float32)
    return (values * lax.rsqrt(jnp.mean(values * values, axis=1, keepdims=True) + 1e-06)).astype(
        jnp.bfloat16
    )


def split3(x):
    hi = lax.reduce_precision(x, exponent_bits=8, mantissa_bits=7)
    rest = x - hi
    mid = lax.reduce_precision(rest, exponent_bits=8, mantissa_bits=7)
    lo = rest - mid
    return jnp.stack([hi, mid, lo]).astype(jnp.bfloat16)


def join3(parts):
    parts = parts.astype(jnp.float32)
    return (parts[0] + parts[1]) + parts[2]


def pack_rows(flat, width):
    rows = -(-flat.shape[0] // width)
    return jnp.pad(flat, (0, rows * width - flat.shape[0])).reshape(rows, width), rows


def body(embed, beta, block_mask, counts, probes):
    n_dev = lax.axis_size("row") * lax.axis_size("col")
    n_row = lax.axis_size("row")
    me = lax.axis_index(AXES)
    shard, feat = embed.shape
    files = shard * n_dev
    nb = block_mask.shape[1]
    blk = files // nb
    local_blocks = block_mask.shape[0]

    unit_own = normalize(embed)
    beta_rows, beta_n = pack_rows(beta, feat)
    mask_rows, mask_n = pack_rows(block_mask.reshape(-1).astype(jnp.bfloat16), feat)
    replicate = files * files <= REPLICATE_CELLS
    n_probe = probes.shape[0]
    if (
        replicate
        and n_row % 2 == 0
        and shard % 2 == 0
        and blk % shard == 0
        and (blk // 2) % 8 == 0
        and files % 128 == 0
    ):
        return dense_path(unit_own, beta, block_mask, counts, probes, n_dev, n_row, me)
    if replicate:
        mask_flat = block_mask.reshape(-1).astype(jnp.bfloat16)
        mask_cols = -(-mask_flat.shape[0] // shard)
        mask_part = jnp.pad(mask_flat, (0, shard * mask_cols - mask_flat.shape[0]))
        used = 3 * n_probe + 1 + mask_cols
        lanes = -(-used // 128) * 128
        extra_cols = jnp.concatenate(
            [
                jnp.moveaxis(split3(probes.T), 0, 1).reshape(shard, 3 * n_probe),
                beta[:, None],
                mask_part.reshape(shard, mask_cols),
                jnp.zeros((shard, lanes - used), jnp.bfloat16),
            ],
            axis=1,
        )
        got = gather_halves(jnp.concatenate([unit_own, extra_cols], axis=1), n_dev, n_row)
        unit_all = got[:, :, :feat].reshape(files, feat)
        tail = got[:, :, feat:].reshape(files, lanes)
        probes_t = join3(
            jnp.stack([tail[:, k * n_probe : (k + 1) * n_probe] for k in range(3)])
        )
        beta_all = tail[:, 3 * n_probe]
        mask_got = got[:, :, feat + 3 * n_probe + 1 : feat + used].reshape(n_dev, -1)
        mask_got = mask_got[:, : local_blocks * nb]
    else:
        unit_all = gather_rows(unit_own, n_dev).reshape(files, feat)
        extra = gather_rows(jnp.concatenate([beta_rows, mask_rows], axis=0), n_dev)
        beta_all = extra[:, 0, :shard].reshape(files)
        mask_got = extra[:, beta_n:, :].reshape(n_dev, -1)[:, : local_blocks * nb]
    per_row = n_dev // n_row
    mask_full = (
        mask_got.reshape(n_row, per_row, local_blocks, nb)[:, 0].reshape(nb, nb).astype(jnp.int32)
    )
    scale_all = beta_all.astype(jnp.float32) / feat

    col_ids = lax.iota(jnp.int32, files)
    col_block = col_ids // blk
    in_block = lax.iota(jnp.int32, blk)
    col_live = (in_block[None, :] < counts[:, None]).reshape(files)

    if replicate:
        gram = lax.dot_general(
            unit_all, unit_all, (((1,), (1,)), ((), ())), preferred_element_type=jnp.float32
        )
        scores = gram * scale_all[:, None]
        block_ok = jnp.broadcast_to(
            (mask_full == 1)[:, None, :, None], (nb, blk, nb, blk)
        ).reshape(files, files)
        allowed = block_ok & col_live[None, :] & (col_ids[:, None] != col_ids[None, :])
        masked = jnp.where(allowed, scores, -1e30)
        row_top = jnp.max(masked, axis=1)
        row_mass = jnp.sum(jnp.where(allowed, jnp.exp(masked - row_top[:, None]), 0.0), axis=1)
        weights = jnp.where(allowed, jnp.exp(masked - row_top[:, None]) / row_mass[:, None], 0.0)
        col_mass = jnp.sum(weights, axis=0)
        inv_root = lax.rsqrt((1.0 + col_mass) * 0.5)
        affinity = weights.astype(jnp.bfloat16)
        state = probes_t
        for sweep in range(ITERS):
            scaled = (state * inv_root[:, None]).astype(jnp.bfloat16)
            row_part = jnp.dot(affinity, scaled, preferred_element_type=jnp.float32)
            col_part = lax.dot_general(
                affinity, scaled, (((0,), (0,)), ((), ())), preferred_element_type=jnp.float32
            )
            state = (row_part + col_part) * (0.5 * inv_root)[:, None]
        return lax.dynamic_slice_in_dim(state, me * shard, shard, 0).T

    own_ids = me * shard + lax.iota(jnp.int32, shard)
    own_block = own_ids // blk
    gram = lax.dot_general(
        unit_own, unit_all, (((1,), (1,)), ((), ())), preferred_element_type=jnp.float32
    )
    own_scale = lax.dynamic_slice_in_dim(scale_all, me * shard, shard, 0)
    scores = gram * own_scale[:, None]
    row_ok = jnp.take(jnp.take(mask_full, own_block, axis=0), col_block, axis=1) == 1
    allowed = row_ok & col_live[None, :] & (own_ids[:, None] != col_ids[None, :])
    masked = jnp.where(allowed, scores, -1e30)
    row_top = jnp.max(masked, axis=1)
    row_mass = jnp.sum(jnp.where(allowed, jnp.exp(masked - row_top[:, None]), 0.0), axis=1)
    weights = jnp.where(allowed, jnp.exp(masked - row_top[:, None]) / row_mass[:, None], 0.0)
    stats = gather_rows(jnp.stack([row_top, row_mass], axis=1), n_dev).reshape(files, 2)
    top_all, mass_all = stats[:, 0], stats[:, 1]
    scores_t = gram * scale_all[None, :]
    own_live = jnp.take(col_live, own_ids, axis=0)
    col_ok = jnp.take(jnp.take(mask_full, col_block, axis=0), own_block, axis=1).T == 1
    allowed_t = col_ok & own_live[:, None] & (own_ids[:, None] != col_ids[None, :])
    masked_t = jnp.where(allowed_t, scores_t, -1e30)
    weights_t = jnp.where(
        allowed_t, jnp.exp(masked_t - top_all[None, :]) / mass_all[None, :], 0.0
    )
    col_mass = jnp.sum(weights_t, axis=1)
    inv_root = lax.rsqrt((1.0 + col_mass) * 0.5)
    aff_rows = weights.astype(jnp.bfloat16)
    aff_cols = weights_t.astype(jnp.bfloat16)
    state = probes
    for sweep in range(ITERS):
        scaled = (state * inv_root[None, :]).astype(jnp.bfloat16)
        scaled_all = gather_rows(scaled.T, n_dev).reshape(files, probes.shape[0])
        row_part = jnp.dot(aff_rows, scaled_all, preferred_element_type=jnp.float32)
        col_part = jnp.dot(aff_cols, scaled_all, preferred_element_type=jnp.float32)
        state = ((row_part + col_part) * (0.5 * inv_root)[:, None]).T
    return state


def solution(mesh):
    placed = (
        P(AXES, None),
        P(AXES),
        P("row", None),
        P(),
        P(None, AXES),
    )
    return jax.shard_map(body, mesh=mesh, in_specs=placed, out_specs=P(None, AXES), check_vma=False)
```

```python
import jax
import jax.numpy as jnp
from jax import lax
from jax.experimental import pallas as pl
from jax.experimental.pallas import tpu as pltpu
from jax.sharding import PartitionSpec as P

ITERS = 2
AXES = ("row", "col")
A2A_BYTES = 8 << 20
REPLICATE_CELLS = 1 << 21


def gather_rows(x, n_dev):
    if n_dev * x.size * x.dtype.itemsize <= A2A_BYTES:
        wide = jnp.broadcast_to(x[None], (n_dev,) + x.shape)
        return lax.all_to_all(wide, AXES, 0, 0, tiled=True)
    return lax.all_gather(x, AXES, axis=0, tiled=False)


def gather_halves(x, n_dev, n_row):
    if n_row % 2:
        return gather_rows(x, n_dev)
    rows = x.shape[0] + x.shape[0] % 2
    halves = jnp.pad(x, ((0, rows - x.shape[0]), (0, 0))).reshape(2, rows // 2, x.shape[1])
    per_row = n_dev // n_row
    wide = jnp.broadcast_to(
        halves[None, :, None], (n_row // 2, 2, per_row, rows // 2, x.shape[1])
    ).reshape(n_dev, rows // 2, x.shape[1])
    mine = lax.all_to_all(wide, AXES, 0, 0, tiled=True)
    other = lax.ppermute(mine, "row", [(r, r ^ 1) for r in range(n_row)])
    first = lax.axis_index("row") % 2 == 0
    low = jnp.where(first, mine, other)
    high = jnp.where(first, other, mine)
    return jnp.concatenate([low, high], axis=1)[:, : x.shape[0]]


def dense_kernel(n_iter, tile, beta_lane, mine_ref, other_ref, rowmask_ref, probes_ref, out_ref, unit_t, unit_s, scale_s, aff_s):
    feat, files = unit_t.shape
    half = files // 2
    runs = half // tile
    for k, ref in enumerate((mine_ref, other_ref)):
        unit_s[k * half : (k + 1) * half, :] = ref[:, 0:feat]
        unit_t[:, k * half : (k + 1) * half] = (
            ref[:, 0:feat].astype(jnp.float32).T.astype(jnp.bfloat16)
        )
        scale_s[k * half : (k + 1) * half, :] = (
            ref[:, beta_lane : beta_lane + 1].astype(jnp.float32) / feat
        )
    per_tile = rowmask_ref.shape[1]
    run = tile // per_tile
    col_pos = lax.broadcasted_iota(jnp.int32, (tile, files), 1)
    row_pos = lax.broadcasted_iota(jnp.int32, (tile, files), 0)

    def step(t, colsum):
        p0 = pl.multiple_of(t * tile, tile)
        gram = jnp.dot(unit_s[pl.ds(p0, tile), :], unit_t[...], preferred_element_type=jnp.float32)
        scores = gram * scale_s[pl.ds(p0, tile), :]
        runs_here = rowmask_ref[t % runs]
        block_row = jnp.broadcast_to(runs_here[:, None, :], (per_tile, run, files)).reshape(tile, files)
        ok = (block_row > 0.0) & (row_pos + p0 != col_pos)
        masked = jnp.where(ok, scores, -1e30)
        top = jnp.max(masked, axis=1, keepdims=True)
        e = jnp.exp(masked - top)
        mass = jnp.sum(e, axis=1, keepdims=True)
        weights = e * (1.0 / mass)
        aff_s[pl.ds(p0, tile), :] = weights.astype(jnp.bfloat16)
        return colsum + jnp.sum(weights, axis=0, keepdims=True)

    colsum = lax.fori_loop(0, files // tile, step, jnp.zeros((1, files), jnp.float32))
    inv_root = lax.rsqrt((1.0 + colsum) * 0.5)
    state = probes_ref[...]
    for sweep in range(n_iter):
        scaled_f = (state * inv_root).astype(jnp.bfloat16).astype(jnp.float32)
        scaled = scaled_f.astype(jnp.bfloat16)
        row_t = jnp.dot(aff_s[...], scaled_f.T.astype(jnp.bfloat16), preferred_element_type=jnp.float32)
        col_part = jnp.dot(scaled, aff_s[...], preferred_element_type=jnp.float32)
        state = (row_t.T + col_part) * (0.5 * inv_root)
    out_ref[...] = state


def dense_call(mine, other, rowmask, probes_int, feat, beta_lane):
    files = 2 * mine.shape[0]
    run = files // (2 * rowmask.shape[0])
    tile = run
    while tile * 2 <= min(512, files // 2) and (files // 2) % (tile * 2) == 0:
        tile *= 2
    rowmask = rowmask.reshape(-1, tile // run, files)
    vmem = pl.BlockSpec(memory_space=pltpu.VMEM)
    return pl.pallas_call(
        lambda *refs: dense_kernel(ITERS, tile, beta_lane, *refs),
        out_shape=jax.ShapeDtypeStruct(probes_int.shape, jnp.float32),
        in_specs=[vmem] * 4,
        out_specs=vmem,
        scratch_shapes=[
            pltpu.VMEM((feat, files), jnp.bfloat16),
            pltpu.VMEM((files, feat), jnp.bfloat16),
            pltpu.VMEM((files, 1), jnp.float32),
            pltpu.VMEM((files, files), jnp.bfloat16),
        ],
        cost_estimate=pl.CostEstimate(
            flops=2 * files * files * feat + 4 * ITERS * files * files * probes_int.shape[0],
            transcendentals=files * files,
            bytes_accessed=files * mine.shape[1] * 2 + 8 * files * probes_int.shape[0],
        ),
    )(mine, other, rowmask, probes_int)


def dense_path(unit_own, beta, block_mask, counts, probes, n_dev, n_row, me):
    shard, feat = unit_own.shape
    files = shard * n_dev
    half_s = shard // 2
    half_f = files // 2
    nb = block_mask.shape[1]
    blk = files // nb
    local_blocks = block_mask.shape[0]
    n_probe = probes.shape[0]
    per_row = n_dev // n_row
    mask_flat = block_mask.reshape(-1).astype(jnp.bfloat16)
    mask_cols = -(-mask_flat.shape[0] // half_s)
    mask_part = jnp.pad(mask_flat, (0, half_s * mask_cols - mask_flat.shape[0]))
    mask_part = jnp.tile(mask_part.reshape(half_s, mask_cols), (2, 1))
    used = 3 * n_probe + 1 + mask_cols
    lanes = -(-used // 128) * 128
    payload = jnp.concatenate(
        [
            unit_own,
            jnp.moveaxis(split3(probes.T), 0, 1).reshape(shard, 3 * n_probe),
            beta[:, None],
            mask_part,
            jnp.zeros((shard, lanes - used), jnp.bfloat16),
        ],
        axis=1,
    )
    width = payload.shape[1]
    halves = payload.reshape(2, half_s, width)
    wide = jnp.broadcast_to(
        halves[None, :, None], (n_row // 2, 2, per_row, half_s, width)
    ).reshape(n_dev, half_s, width)
    mine = lax.all_to_all(wide, AXES, 0, 0, tiled=True)
    other = lax.ppermute(mine, "row", [(r, r ^ 1) for r in range(n_row)])
    core = lax.axis_index("row") % 2
    pos = lax.iota(jnp.int32, files)
    run = blk // 2
    in_run = lax.iota(jnp.int32, files) % run
    run_dev = in_run // half_s
    half_of = jnp.broadcast_to((lax.iota(jnp.int32, 2) ^ core)[:, None, None], (2, nb, run))
    in_block = (run_dev % (blk // shard)) * shard + half_of.reshape(files) * half_s + in_run % half_s
    block_counts = jnp.broadcast_to(counts[None, :, None], (2, nb, run)).reshape(files)
    live = in_block < block_counts
    mine2 = mine.reshape(half_f, width)
    other2 = other.reshape(half_f, width)
    tails = jnp.concatenate([mine2[:, feat:], other2[:, feat:]], axis=0)
    probes_int = join3(
        jnp.stack([tails[:, k * n_probe : (k + 1) * n_probe] for k in range(3)])
    ).T
    mask_got = mine[:, :, feat + 3 * n_probe + 1 : feat + used].reshape(n_dev, -1)
    mask_got = mask_got[:, : local_blocks * nb]
    mask_full = mask_got.reshape(n_row, per_row, local_blocks, nb)[:, 0].reshape(nb, nb)
    block_ok = jnp.broadcast_to((mask_full == 1)[:, None, :, None], (nb, 2, nb, run))
    rowmask = jnp.where(block_ok.reshape(nb, files) & live[None, :], 1.0, 0.0).astype(jnp.float32)
    state = dense_call(mine2, other2, rowmask, probes_int, feat, feat + 3 * n_probe)
    first = lax.dynamic_slice_in_dim(state, core * half_f + me * half_s, half_s, 1)
    second = lax.dynamic_slice_in_dim(state, (1 - core) * half_f + me * half_s, half_s, 1)
    return jnp.concatenate([first, second], axis=1)


def normalize(embed):
    values = embed.astype(jnp.float32)
    return (values * lax.rsqrt(jnp.mean(values * values, axis=1, keepdims=True) + 1e-06)).astype(
        jnp.bfloat16
    )


def split3(x):
    hi = lax.reduce_precision(x, exponent_bits=8, mantissa_bits=7)
    rest = x - hi
    mid = lax.reduce_precision(rest, exponent_bits=8, mantissa_bits=7)
    lo = rest - mid
    return jnp.stack([hi, mid, lo]).astype(jnp.bfloat16)


def join3(parts):
    parts = parts.astype(jnp.float32)
    return (parts[0] + parts[1]) + parts[2]


def pack_rows(flat, width):
    rows = -(-flat.shape[0] // width)
    return jnp.pad(flat, (0, rows * width - flat.shape[0])).reshape(rows, width), rows


def body(embed, beta, block_mask, counts, probes):
    n_dev = lax.axis_size("row") * lax.axis_size("col")
    n_row = lax.axis_size("row")
    me = lax.axis_index(AXES)
    shard, feat = embed.shape
    files = shard * n_dev
    nb = block_mask.shape[1]
    blk = files // nb
    local_blocks = block_mask.shape[0]

    unit_own = normalize(embed)
    beta_rows, beta_n = pack_rows(beta, feat)
    mask_rows, mask_n = pack_rows(block_mask.reshape(-1).astype(jnp.bfloat16), feat)
    replicate = files * files <= REPLICATE_CELLS
    n_probe = probes.shape[0]
    if (
        replicate
        and n_row % 2 == 0
        and shard % 2 == 0
        and blk % shard == 0
        and (blk // 2) % 8 == 0
        and files % 128 == 0
    ):
        return dense_path(unit_own, beta, block_mask, counts, probes, n_dev, n_row, me)
    if replicate:
        mask_flat = block_mask.reshape(-1).astype(jnp.bfloat16)
        mask_cols = -(-mask_flat.shape[0] // shard)
        mask_part = jnp.pad(mask_flat, (0, shard * mask_cols - mask_flat.shape[0]))
        used = 3 * n_probe + 1 + mask_cols
        lanes = -(-used // 128) * 128
        extra_cols = jnp.concatenate(
            [
                jnp.moveaxis(split3(probes.T), 0, 1).reshape(shard, 3 * n_probe),
                beta[:, None],
                mask_part.reshape(shard, mask_cols),
                jnp.zeros((shard, lanes - used), jnp.bfloat16),
            ],
            axis=1,
        )
        got = gather_halves(jnp.concatenate([unit_own, extra_cols], axis=1), n_dev, n_row)
        unit_all = got[:, :, :feat].reshape(files, feat)
        tail = got[:, :, feat:].reshape(files, lanes)
        probes_t = join3(
            jnp.stack([tail[:, k * n_probe : (k + 1) * n_probe] for k in range(3)])
        )
        beta_all = tail[:, 3 * n_probe]
        mask_got = got[:, :, feat + 3 * n_probe + 1 : feat + used].reshape(n_dev, -1)
        mask_got = mask_got[:, : local_blocks * nb]
    else:
        unit_all = gather_rows(unit_own, n_dev).reshape(files, feat)
        extra = gather_rows(jnp.concatenate([beta_rows, mask_rows], axis=0), n_dev)
        beta_all = extra[:, 0, :shard].reshape(files)
        mask_got = extra[:, beta_n:, :].reshape(n_dev, -1)[:, : local_blocks * nb]
    per_row = n_dev // n_row
    mask_full = (
        mask_got.reshape(n_row, per_row, local_blocks, nb)[:, 0].reshape(nb, nb).astype(jnp.int32)
    )
    scale_all = beta_all.astype(jnp.float32) / feat

    col_ids = lax.iota(jnp.int32, files)
    col_block = col_ids // blk
    in_block = lax.iota(jnp.int32, blk)
    col_live = (in_block[None, :] < counts[:, None]).reshape(files)

    if replicate:
        gram = lax.dot_general(
            unit_all, unit_all, (((1,), (1,)), ((), ())), preferred_element_type=jnp.float32
        )
        scores = gram * scale_all[:, None]
        block_ok = jnp.broadcast_to(
            (mask_full == 1)[:, None, :, None], (nb, blk, nb, blk)
        ).reshape(files, files)
        allowed = block_ok & col_live[None, :] & (col_ids[:, None] != col_ids[None, :])
        masked = jnp.where(allowed, scores, -1e30)
        row_top = jnp.max(masked, axis=1)
        row_mass = jnp.sum(jnp.where(allowed, jnp.exp(masked - row_top[:, None]), 0.0), axis=1)
        weights = jnp.where(allowed, jnp.exp(masked - row_top[:, None]) / row_mass[:, None], 0.0)
        col_mass = jnp.sum(weights, axis=0)
        inv_root = lax.rsqrt((1.0 + col_mass) * 0.5)
        affinity = weights.astype(jnp.bfloat16)
        state = probes_t
        for sweep in range(ITERS):
            scaled = (state * inv_root[:, None]).astype(jnp.bfloat16)
            row_part = jnp.dot(affinity, scaled, preferred_element_type=jnp.float32)
            col_part = lax.dot_general(
                affinity, scaled, (((0,), (0,)), ((), ())), preferred_element_type=jnp.float32
            )
            state = (row_part + col_part) * (0.5 * inv_root)[:, None]
        return lax.dynamic_slice_in_dim(state, me * shard, shard, 0).T

    own_ids = me * shard + lax.iota(jnp.int32, shard)
    own_block = own_ids // blk
    gram = lax.dot_general(
        unit_own, unit_all, (((1,), (1,)), ((), ())), preferred_element_type=jnp.float32
    )
    own_scale = lax.dynamic_slice_in_dim(scale_all, me * shard, shard, 0)
    scores = gram * own_scale[:, None]
    row_ok = jnp.take(jnp.take(mask_full, own_block, axis=0), col_block, axis=1) == 1
    allowed = row_ok & col_live[None, :] & (own_ids[:, None] != col_ids[None, :])
    masked = jnp.where(allowed, scores, -1e30)
    row_top = jnp.max(masked, axis=1)
    row_mass = jnp.sum(jnp.where(allowed, jnp.exp(masked - row_top[:, None]), 0.0), axis=1)
    weights = jnp.where(allowed, jnp.exp(masked - row_top[:, None]) / row_mass[:, None], 0.0)
    stats = gather_rows(jnp.stack([row_top, row_mass], axis=1), n_dev).reshape(files, 2)
    top_all, mass_all = stats[:, 0], stats[:, 1]
    scores_t = gram * scale_all[None, :]
    own_live = jnp.take(col_live, own_ids, axis=0)
    col_ok = jnp.take(jnp.take(mask_full, col_block, axis=0), own_block, axis=1).T == 1
    allowed_t = col_ok & own_live[:, None] & (own_ids[:, None] != col_ids[None, :])
    masked_t = jnp.where(allowed_t, scores_t, -1e30)
    weights_t = jnp.where(
        allowed_t, jnp.exp(masked_t - top_all[None, :]) / mass_all[None, :], 0.0
    )
    col_mass = jnp.sum(weights_t, axis=1)
    inv_root = lax.rsqrt((1.0 + col_mass) * 0.5)
    aff_rows = weights.astype(jnp.bfloat16)
    aff_cols = weights_t.astype(jnp.bfloat16)
    state = probes
    for sweep in range(ITERS):
        scaled = (state * inv_root[None, :]).astype(jnp.bfloat16)
        scaled_all = gather_rows(scaled.T, n_dev).reshape(files, probes.shape[0])
        row_part = jnp.dot(aff_rows, scaled_all, preferred_element_type=jnp.float32)
        col_part = jnp.dot(aff_cols, scaled_all, preferred_element_type=jnp.float32)
        state = ((row_part + col_part) * (0.5 * inv_root)[:, None]).T
    return state


def solution(mesh):
    placed = (
        P(AXES, None),
        P(AXES),
        P("row", None),
        P(),
        P(None, AXES),
    )
    return jax.shard_map(body, mesh=mesh, in_specs=placed, out_specs=P(None, AXES), check_vma=False)
```

```python
import jax
import jax.numpy as jnp
from jax import lax
from jax.experimental import pallas as pl
from jax.experimental.pallas import tpu as pltpu
from jax.sharding import PartitionSpec as P

ITERS = 2
PROBE_PARTS = 1
AXES = ("row", "col")
A2A_BYTES = 8 << 20
REPLICATE_CELLS = 1 << 21


def gather_rows(x, n_dev):
    if n_dev * x.size * x.dtype.itemsize <= A2A_BYTES:
        wide = jnp.broadcast_to(x[None], (n_dev,) + x.shape)
        return lax.all_to_all(wide, AXES, 0, 0, tiled=True)
    return lax.all_gather(x, AXES, axis=0, tiled=False)


def gather_halves(x, n_dev, n_row):
    if n_row % 2:
        return gather_rows(x, n_dev)
    rows = x.shape[0] + x.shape[0] % 2
    halves = jnp.pad(x, ((0, rows - x.shape[0]), (0, 0))).reshape(2, rows // 2, x.shape[1])
    per_row = n_dev // n_row
    wide = jnp.broadcast_to(
        halves[None, :, None], (n_row // 2, 2, per_row, rows // 2, x.shape[1])
    ).reshape(n_dev, rows // 2, x.shape[1])
    mine = lax.all_to_all(wide, AXES, 0, 0, tiled=True)
    other = lax.ppermute(mine, "row", [(r, r ^ 1) for r in range(n_row)])
    first = lax.axis_index("row") % 2 == 0
    low = jnp.where(first, mine, other)
    high = jnp.where(first, other, mine)
    return jnp.concatenate([low, high], axis=1)[:, : x.shape[0]]


def dense_kernel(n_iter, tile, beta_lane, n_parts, pos_ref, mine_ref, other_ref, rowmask_ref, out_ref, unit_t, unit_s, scale_s, aff_s):
    feat, files = unit_t.shape
    half = files // 2
    runs = half // tile
    for k, ref in enumerate((mine_ref, other_ref)):
        unit_s[k * half : (k + 1) * half, :] = ref[:, 0:feat]
        unit_t[:, k * half : (k + 1) * half] = (
            ref[:, 0:feat].astype(jnp.float32).T.astype(jnp.bfloat16)
        )
        scale_s[k * half : (k + 1) * half, :] = (
            ref[:, beta_lane : beta_lane + 1].astype(jnp.float32) / feat
        )
    per_tile = rowmask_ref.shape[1]
    run = tile // per_tile
    col_pos = lax.broadcasted_iota(jnp.int32, (tile, files), 1)
    row_pos = lax.broadcasted_iota(jnp.int32, (tile, files), 0)

    def step(t, colsum):
        p0 = pl.multiple_of(t * tile, tile)
        gram = jnp.dot(unit_s[pl.ds(p0, tile), :], unit_t[...], preferred_element_type=jnp.float32)
        scores = gram * scale_s[pl.ds(p0, tile), :]
        runs_here = rowmask_ref[t % runs]
        block_row = jnp.broadcast_to(runs_here[:, None, :], (per_tile, run, files)).reshape(tile, files)
        ok = (block_row > 0.0) & (row_pos + p0 != col_pos)
        masked = jnp.where(ok, scores, -1e30)
        top = jnp.max(masked, axis=1, keepdims=True)
        e = jnp.exp(masked - top)
        mass = jnp.sum(e, axis=1, keepdims=True)
        weights = e * (1.0 / mass)
        aff_s[pl.ds(p0, tile), :] = weights.astype(jnp.bfloat16)
        return colsum + jnp.sum(weights, axis=0, keepdims=True)

    colsum = lax.fori_loop(0, files // tile, step, jnp.zeros((1, files), jnp.float32))
    inv_root = lax.rsqrt((1.0 + colsum) * 0.5)
    n_probe, shard = out_ref.shape
    state = jnp.concatenate(
        [
            sum(
                ref[:, feat + k * n_probe : feat + (k + 1) * n_probe].astype(jnp.float32)
                for k in range(n_parts)
            ).T
            for ref in (mine_ref, other_ref)
        ],
        axis=1,
    )
    for sweep in range(n_iter):
        scaled_f = (state * inv_root).astype(jnp.bfloat16).astype(jnp.float32)
        scaled = scaled_f.astype(jnp.bfloat16)
        row_t = jnp.dot(aff_s[...], scaled_f.T.astype(jnp.bfloat16), preferred_element_type=jnp.float32)
        col_part = jnp.dot(scaled, aff_s[...], preferred_element_type=jnp.float32)
        state = (row_t.T + col_part) * (0.5 * inv_root)
    half_s = shard // 2
    col = lax.broadcasted_iota(jnp.int32, (files, shard), 0)
    j = lax.broadcasted_iota(jnp.int32, (files, shard), 1)
    target = jnp.where(j < half_s, pos_ref[0] + j, pos_ref[1] + j - half_s)
    pick = jnp.where(col == target, 1.0, 0.0).astype(jnp.float32)
    out_ref[...] = jnp.dot(
        state, pick, precision=lax.Precision.HIGHEST, preferred_element_type=jnp.float32
    )


def dense_call(positions, mine, other, rowmask, n_probe, shard, feat, beta_lane):
    files = 2 * mine.shape[0]
    run = files // (2 * rowmask.shape[0])
    tile = run
    while tile * 2 <= min(512, files // 2) and (files // 2) % (tile * 2) == 0:
        tile *= 2
    rowmask = rowmask.reshape(-1, tile // run, files)
    vmem = pl.BlockSpec(memory_space=pltpu.VMEM)
    smem = pl.BlockSpec(memory_space=pltpu.SMEM)
    return pl.pallas_call(
        lambda *refs: dense_kernel(ITERS, tile, beta_lane, PROBE_PARTS, *refs),
        out_shape=jax.ShapeDtypeStruct((n_probe, shard), jnp.float32),
        in_specs=[smem, vmem, vmem, vmem],
        out_specs=vmem,
        scratch_shapes=[
            pltpu.VMEM((feat, files), jnp.bfloat16),
            pltpu.VMEM((files, feat), jnp.bfloat16),
            pltpu.VMEM((files, 1), jnp.float32),
            pltpu.VMEM((files, files), jnp.bfloat16),
        ],
        cost_estimate=pl.CostEstimate(
            flops=2 * files * files * feat + 4 * ITERS * files * files * n_probe,
            transcendentals=files * files,
            bytes_accessed=files * mine.shape[1] * 2 + 4 * shard * n_probe,
        ),
    )(positions, mine, other, rowmask)


def dense_path(unit_own, beta, block_mask, counts, probes, n_dev, n_row, me):
    shard, feat = unit_own.shape
    files = shard * n_dev
    half_s = shard // 2
    half_f = files // 2
    nb = block_mask.shape[1]
    blk = files // nb
    local_blocks = block_mask.shape[0]
    n_probe = probes.shape[0]
    per_row = n_dev // n_row
    mask_flat = block_mask.reshape(-1).astype(jnp.bfloat16)
    mask_cols = -(-mask_flat.shape[0] // half_s)
    mask_part = jnp.pad(mask_flat, (0, half_s * mask_cols - mask_flat.shape[0]))
    mask_part = jnp.tile(mask_part.reshape(half_s, mask_cols), (2, 1))
    used = PROBE_PARTS * n_probe + 1 + mask_cols
    lanes = -(-used // 128) * 128
    payload = jnp.concatenate(
        [
            unit_own,
            jnp.moveaxis(split3(probes.T)[:PROBE_PARTS], 0, 1).reshape(shard, PROBE_PARTS * n_probe),
            beta[:, None],
            mask_part,
            jnp.zeros((shard, lanes - used), jnp.bfloat16),
        ],
        axis=1,
    )
    width = payload.shape[1]
    halves = payload.reshape(2, half_s, width)
    wide = jnp.broadcast_to(
        halves[None, :, None], (n_row // 2, 2, per_row, half_s, width)
    ).reshape(n_dev, half_s, width)
    mine = lax.all_to_all(wide, AXES, 0, 0, tiled=True)
    other = lax.ppermute(mine, "row", [(r, r ^ 1) for r in range(n_row)])
    core = lax.axis_index("row") % 2
    pos = lax.iota(jnp.int32, files)
    run = blk // 2
    in_run = lax.iota(jnp.int32, files) % run
    run_dev = in_run // half_s
    half_of = jnp.broadcast_to((lax.iota(jnp.int32, 2) ^ core)[:, None, None], (2, nb, run))
    in_block = (run_dev % (blk // shard)) * shard + half_of.reshape(files) * half_s + in_run % half_s
    block_counts = jnp.broadcast_to(counts[None, :, None], (2, nb, run)).reshape(files)
    live = in_block < block_counts
    mine2 = mine.reshape(half_f, width)
    other2 = other.reshape(half_f, width)
    mask_got = mine[:, :, feat + PROBE_PARTS * n_probe + 1 : feat + used].reshape(n_dev, -1)
    mask_got = mask_got[:, : local_blocks * nb]
    mask_full = mask_got.reshape(n_row, per_row, local_blocks, nb)[:, 0].reshape(nb, nb)
    block_ok = jnp.broadcast_to((mask_full == 1)[:, None, :, None], (nb, 2, nb, run))
    rowmask = jnp.where(block_ok.reshape(nb, files) & live[None, :], 1.0, 0.0).astype(jnp.float32)
    positions = jnp.stack(
        [core * half_f + me * half_s, (1 - core) * half_f + me * half_s]
    ).astype(jnp.int32)
    return dense_call(
        positions, mine2, other2, rowmask, n_probe, shard, feat, feat + PROBE_PARTS * n_probe
    )


def normalize(embed):
    values = embed.astype(jnp.float32)
    return (values * lax.rsqrt(jnp.mean(values * values, axis=1, keepdims=True) + 1e-06)).astype(
        jnp.bfloat16
    )


def split3(x):
    hi = lax.reduce_precision(x, exponent_bits=8, mantissa_bits=7)
    rest = x - hi
    mid = lax.reduce_precision(rest, exponent_bits=8, mantissa_bits=7)
    lo = rest - mid
    return jnp.stack([hi, mid, lo]).astype(jnp.bfloat16)


def join3(parts):
    parts = parts.astype(jnp.float32)
    if parts.shape[0] == 1:
        return parts[0]
    return (parts[0] + parts[1]) + parts[2]


def pack_rows(flat, width):
    rows = -(-flat.shape[0] // width)
    return jnp.pad(flat, (0, rows * width - flat.shape[0])).reshape(rows, width), rows


def body(embed, beta, block_mask, counts, probes):
    n_dev = lax.axis_size("row") * lax.axis_size("col")
    n_row = lax.axis_size("row")
    me = lax.axis_index(AXES)
    shard, feat = embed.shape
    files = shard * n_dev
    nb = block_mask.shape[1]
    blk = files // nb
    local_blocks = block_mask.shape[0]

    unit_own = normalize(embed)
    beta_rows, beta_n = pack_rows(beta, feat)
    mask_rows, mask_n = pack_rows(block_mask.reshape(-1).astype(jnp.bfloat16), feat)
    replicate = files * files <= REPLICATE_CELLS
    n_probe = probes.shape[0]
    if (
        replicate
        and n_row % 2 == 0
        and shard % 2 == 0
        and blk % shard == 0
        and (blk // 2) % 8 == 0
        and files % 128 == 0
    ):
        return dense_path(unit_own, beta, block_mask, counts, probes, n_dev, n_row, me)
    if replicate:
        mask_flat = block_mask.reshape(-1).astype(jnp.bfloat16)
        mask_cols = -(-mask_flat.shape[0] // shard)
        mask_part = jnp.pad(mask_flat, (0, shard * mask_cols - mask_flat.shape[0]))
        used = 3 * n_probe + 1 + mask_cols
        lanes = -(-used // 128) * 128
        extra_cols = jnp.concatenate(
            [
                jnp.moveaxis(split3(probes.T), 0, 1).reshape(shard, 3 * n_probe),
                beta[:, None],
                mask_part.reshape(shard, mask_cols),
                jnp.zeros((shard, lanes - used), jnp.bfloat16),
            ],
            axis=1,
        )
        got = gather_halves(jnp.concatenate([unit_own, extra_cols], axis=1), n_dev, n_row)
        unit_all = got[:, :, :feat].reshape(files, feat)
        tail = got[:, :, feat:].reshape(files, lanes)
        probes_t = join3(
            jnp.stack([tail[:, k * n_probe : (k + 1) * n_probe] for k in range(3)])
        )
        beta_all = tail[:, 3 * n_probe]
        mask_got = got[:, :, feat + 3 * n_probe + 1 : feat + used].reshape(n_dev, -1)
        mask_got = mask_got[:, : local_blocks * nb]
    else:
        unit_all = gather_rows(unit_own, n_dev).reshape(files, feat)
        extra = gather_rows(jnp.concatenate([beta_rows, mask_rows], axis=0), n_dev)
        beta_all = extra[:, 0, :shard].reshape(files)
        mask_got = extra[:, beta_n:, :].reshape(n_dev, -1)[:, : local_blocks * nb]
    per_row = n_dev // n_row
    mask_full = (
        mask_got.reshape(n_row, per_row, local_blocks, nb)[:, 0].reshape(nb, nb).astype(jnp.int32)
    )
    scale_all = beta_all.astype(jnp.float32) / feat

    col_ids = lax.iota(jnp.int32, files)
    col_block = col_ids // blk
    in_block = lax.iota(jnp.int32, blk)
    col_live = (in_block[None, :] < counts[:, None]).reshape(files)

    if replicate:
        gram = lax.dot_general(
            unit_all, unit_all, (((1,), (1,)), ((), ())), preferred_element_type=jnp.float32
        )
        scores = gram * scale_all[:, None]
        block_ok = jnp.broadcast_to(
            (mask_full == 1)[:, None, :, None], (nb, blk, nb, blk)
        ).reshape(files, files)
        allowed = block_ok & col_live[None, :] & (col_ids[:, None] != col_ids[None, :])
        masked = jnp.where(allowed, scores, -1e30)
        row_top = jnp.max(masked, axis=1)
        row_mass = jnp.sum(jnp.where(allowed, jnp.exp(masked - row_top[:, None]), 0.0), axis=1)
        weights = jnp.where(allowed, jnp.exp(masked - row_top[:, None]) / row_mass[:, None], 0.0)
        col_mass = jnp.sum(weights, axis=0)
        inv_root = lax.rsqrt((1.0 + col_mass) * 0.5)
        affinity = weights.astype(jnp.bfloat16)
        state = probes_t
        for sweep in range(ITERS):
            scaled = (state * inv_root[:, None]).astype(jnp.bfloat16)
            row_part = jnp.dot(affinity, scaled, preferred_element_type=jnp.float32)
            col_part = lax.dot_general(
                affinity, scaled, (((0,), (0,)), ((), ())), preferred_element_type=jnp.float32
            )
            state = (row_part + col_part) * (0.5 * inv_root)[:, None]
        return lax.dynamic_slice_in_dim(state, me * shard, shard, 0).T

    own_ids = me * shard + lax.iota(jnp.int32, shard)
    own_block = own_ids // blk
    gram = lax.dot_general(
        unit_own, unit_all, (((1,), (1,)), ((), ())), preferred_element_type=jnp.float32
    )
    own_scale = lax.dynamic_slice_in_dim(scale_all, me * shard, shard, 0)
    scores = gram * own_scale[:, None]
    row_ok = jnp.take(jnp.take(mask_full, own_block, axis=0), col_block, axis=1) == 1
    allowed = row_ok & col_live[None, :] & (own_ids[:, None] != col_ids[None, :])
    masked = jnp.where(allowed, scores, -1e30)
    row_top = jnp.max(masked, axis=1)
    row_mass = jnp.sum(jnp.where(allowed, jnp.exp(masked - row_top[:, None]), 0.0), axis=1)
    weights = jnp.where(allowed, jnp.exp(masked - row_top[:, None]) / row_mass[:, None], 0.0)
    stats = gather_rows(jnp.stack([row_top, row_mass], axis=1), n_dev).reshape(files, 2)
    top_all, mass_all = stats[:, 0], stats[:, 1]
    scores_t = gram * scale_all[None, :]
    own_live = jnp.take(col_live, own_ids, axis=0)
    col_ok = jnp.take(jnp.take(mask_full, col_block, axis=0), own_block, axis=1).T == 1
    allowed_t = col_ok & own_live[:, None] & (own_ids[:, None] != col_ids[None, :])
    masked_t = jnp.where(allowed_t, scores_t, -1e30)
    weights_t = jnp.where(
        allowed_t, jnp.exp(masked_t - top_all[None, :]) / mass_all[None, :], 0.0
    )
    col_mass = jnp.sum(weights_t, axis=1)
    inv_root = lax.rsqrt((1.0 + col_mass) * 0.5)
    aff_rows = weights.astype(jnp.bfloat16)
    aff_cols = weights_t.astype(jnp.bfloat16)
    state = probes
    for sweep in range(ITERS):
        scaled = (state * inv_root[None, :]).astype(jnp.bfloat16)
        scaled_all = gather_rows(scaled.T, n_dev).reshape(files, probes.shape[0])
        row_part = jnp.dot(aff_rows, scaled_all, preferred_element_type=jnp.float32)
        col_part = jnp.dot(aff_cols, scaled_all, preferred_element_type=jnp.float32)
        state = ((row_part + col_part) * (0.5 * inv_root)[:, None]).T
    return state


def solution(mesh):
    placed = (
        P(AXES, None),
        P(AXES),
        P("row", None),
        P(),
        P(None, AXES),
    )
    return jax.shard_map(body, mesh=mesh, in_specs=placed, out_specs=P(None, AXES), check_vma=False)
```

```python
import jax
import jax.numpy as jnp
from jax import lax
from jax.experimental import pallas as pl
from jax.experimental.pallas import tpu as pltpu
from jax.sharding import PartitionSpec as P

ITERS = 2
PROBE_PARTS = 1
AXES = ("row", "col")
A2A_BYTES = 8 << 20
REPLICATE_CELLS = 1 << 21


def gather_rows(x, n_dev):
    if n_dev * x.size * x.dtype.itemsize <= A2A_BYTES:
        wide = jnp.broadcast_to(x[None], (n_dev,) + x.shape)
        return lax.all_to_all(wide, AXES, 0, 0, tiled=True)
    return lax.all_gather(x, AXES, axis=0, tiled=False)


def gather_halves(x, n_dev, n_row):
    if n_row % 2:
        return gather_rows(x, n_dev)
    rows = x.shape[0] + x.shape[0] % 2
    halves = jnp.pad(x, ((0, rows - x.shape[0]), (0, 0))).reshape(2, rows // 2, x.shape[1])
    per_row = n_dev // n_row
    wide = jnp.broadcast_to(
        halves[None, :, None], (n_row // 2, 2, per_row, rows // 2, x.shape[1])
    ).reshape(n_dev, rows // 2, x.shape[1])
    mine = lax.all_to_all(wide, AXES, 0, 0, tiled=True)
    other = lax.ppermute(mine, "row", [(r, r ^ 1) for r in range(n_row)])
    first = lax.axis_index("row") % 2 == 0
    low = jnp.where(first, mine, other)
    high = jnp.where(first, other, mine)
    return jnp.concatenate([low, high], axis=1)[:, : x.shape[0]]


def dense_kernel(n_iter, tile, beta_lane, n_parts, mine_ref, other_ref, rowmask_ref, out_ref, unit_t, unit_s, scale_s, aff_s):
    feat, files = unit_t.shape
    half = files // 2
    runs = half // tile
    for k, ref in enumerate((mine_ref, other_ref)):
        values = ref[:, 0:feat].astype(jnp.float32)
        unit = (
            values * lax.rsqrt(jnp.mean(values * values, axis=1, keepdims=True) + 1e-06)
        ).astype(jnp.bfloat16)
        unit_s[k * half : (k + 1) * half, :] = unit
        unit_t[:, k * half : (k + 1) * half] = unit.astype(jnp.float32).T.astype(jnp.bfloat16)
        scale_s[k * half : (k + 1) * half, :] = (
            ref[:, beta_lane : beta_lane + 1].astype(jnp.float32) / feat
        )
    per_tile = rowmask_ref.shape[1]
    run = tile // per_tile
    col_pos = lax.broadcasted_iota(jnp.int32, (tile, files), 1)
    row_pos = lax.broadcasted_iota(jnp.int32, (tile, files), 0)

    def step(t, colsum):
        p0 = pl.multiple_of(t * tile, tile)
        gram = jnp.dot(unit_s[pl.ds(p0, tile), :], unit_t[...], preferred_element_type=jnp.float32)
        scores = gram * scale_s[pl.ds(p0, tile), :]
        runs_here = rowmask_ref[t % runs]
        block_row = jnp.broadcast_to(runs_here[:, None, :], (per_tile, run, files)).reshape(tile, files)
        ok = (block_row > 0.0) & (row_pos + p0 != col_pos)
        masked = jnp.where(ok, scores, -1e30)
        top = jnp.max(masked, axis=1, keepdims=True)
        e = jnp.exp(masked - top)
        mass = jnp.sum(e, axis=1, keepdims=True)
        weights = e * (1.0 / mass)
        aff_s[pl.ds(p0, tile), :] = weights.astype(jnp.bfloat16)
        return colsum + jnp.sum(weights, axis=0, keepdims=True)

    colsum = lax.fori_loop(0, files // tile, step, jnp.zeros((1, files), jnp.float32))
    inv_root = lax.rsqrt((1.0 + colsum) * 0.5)
    n_probe = out_ref.shape[0]
    state = jnp.concatenate(
        [
            sum(
                ref[:, feat + k * n_probe : feat + (k + 1) * n_probe].astype(jnp.float32)
                for k in range(n_parts)
            ).T
            for ref in (mine_ref, other_ref)
        ],
        axis=1,
    )
    for sweep in range(n_iter):
        scaled_f = (state * inv_root).astype(jnp.bfloat16).astype(jnp.float32)
        scaled = scaled_f.astype(jnp.bfloat16)
        row_t = jnp.dot(aff_s[...], scaled_f.T.astype(jnp.bfloat16), preferred_element_type=jnp.float32)
        col_part = jnp.dot(scaled, aff_s[...], preferred_element_type=jnp.float32)
        state = (row_t.T + col_part) * (0.5 * inv_root)
    out_ref[...] = state


def dense_call(mine, other, rowmask, n_probe, feat, beta_lane):
    files = 2 * mine.shape[0]
    run = files // (2 * rowmask.shape[0])
    tile = run
    while tile * 2 <= min(512, files // 2) and (files // 2) % (tile * 2) == 0:
        tile *= 2
    rowmask = rowmask.reshape(-1, tile // run, files)
    vmem = pl.BlockSpec(memory_space=pltpu.VMEM)
    return pl.pallas_call(
        lambda *refs: dense_kernel(ITERS, tile, beta_lane, PROBE_PARTS, *refs),
        out_shape=jax.ShapeDtypeStruct((n_probe, files), jnp.float32),
        in_specs=[vmem, vmem, vmem],
        out_specs=vmem,
        scratch_shapes=[
            pltpu.VMEM((feat, files), jnp.bfloat16),
            pltpu.VMEM((files, feat), jnp.bfloat16),
            pltpu.VMEM((files, 1), jnp.float32),
            pltpu.VMEM((files, files), jnp.bfloat16),
        ],
        cost_estimate=pl.CostEstimate(
            flops=2 * files * files * feat + 4 * ITERS * files * files * n_probe,
            transcendentals=files * files,
            bytes_accessed=files * mine.shape[1] * 2 + 4 * files * n_probe,
        ),
    )(mine, other, rowmask)


def dense_path(embed, beta, block_mask, counts, probes, n_dev, n_row, me):
    shard, feat = embed.shape
    files = shard * n_dev
    half_s = shard // 2
    half_f = files // 2
    nb = block_mask.shape[1]
    blk = files // nb
    local_blocks = block_mask.shape[0]
    n_probe = probes.shape[0]
    per_row = n_dev // n_row
    mask_flat = block_mask.reshape(-1).astype(jnp.bfloat16)
    mask_cols = -(-mask_flat.shape[0] // half_s)
    mask_part = jnp.pad(mask_flat, (0, half_s * mask_cols - mask_flat.shape[0]))
    mask_part = jnp.tile(mask_part.reshape(half_s, mask_cols), (2, 1))
    used = PROBE_PARTS * n_probe + 1 + mask_cols
    lanes = -(-used // 128) * 128
    payload = jnp.concatenate(
        [
            embed,
            jnp.moveaxis(split3(probes.T)[:PROBE_PARTS], 0, 1).reshape(shard, PROBE_PARTS * n_probe),
            beta[:, None],
            mask_part,
            jnp.zeros((shard, lanes - used), jnp.bfloat16),
        ],
        axis=1,
    )
    width = payload.shape[1]
    halves = payload.reshape(2, half_s, width)
    wide = jnp.broadcast_to(
        halves[None, :, None], (n_row // 2, 2, per_row, half_s, width)
    ).reshape(n_dev, half_s, width)
    mine = lax.all_to_all(wide, AXES, 0, 0, tiled=True)
    other = lax.ppermute(mine, "row", [(r, r ^ 1) for r in range(n_row)])
    core = lax.axis_index("row") % 2
    pos = lax.iota(jnp.int32, files)
    run = blk // 2
    in_run = lax.iota(jnp.int32, files) % run
    run_dev = in_run // half_s
    half_of = jnp.broadcast_to((lax.iota(jnp.int32, 2) ^ core)[:, None, None], (2, nb, run))
    in_block = (run_dev % (blk // shard)) * shard + half_of.reshape(files) * half_s + in_run % half_s
    block_counts = jnp.broadcast_to(counts[None, :, None], (2, nb, run)).reshape(files)
    live = in_block < block_counts
    mine2 = mine.reshape(half_f, width)
    other2 = other.reshape(half_f, width)
    mask_got = mine[:, :, feat + PROBE_PARTS * n_probe + 1 : feat + used].reshape(n_dev, -1)
    mask_got = mask_got[:, : local_blocks * nb]
    mask_full = mask_got.reshape(n_row, per_row, local_blocks, nb)[:, 0].reshape(nb, nb)
    block_ok = jnp.broadcast_to((mask_full == 1)[:, None, :, None], (nb, 2, nb, run))
    rowmask = jnp.where(block_ok.reshape(nb, files) & live[None, :], 1.0, 0.0).astype(jnp.float32)
    state = dense_call(mine2, other2, rowmask, n_probe, feat, feat + PROBE_PARTS * n_probe)
    first = lax.dynamic_slice_in_dim(state, core * half_f + me * half_s, half_s, 1)
    second = lax.dynamic_slice_in_dim(state, (1 - core) * half_f + me * half_s, half_s, 1)
    return jnp.concatenate([first, second], axis=1)


def normalize(embed):
    values = embed.astype(jnp.float32)
    return (values * lax.rsqrt(jnp.mean(values * values, axis=1, keepdims=True) + 1e-06)).astype(
        jnp.bfloat16
    )


def split3(x):
    hi = lax.reduce_precision(x, exponent_bits=8, mantissa_bits=7)
    rest = x - hi
    mid = lax.reduce_precision(rest, exponent_bits=8, mantissa_bits=7)
    lo = rest - mid
    return jnp.stack([hi, mid, lo]).astype(jnp.bfloat16)


def join3(parts):
    parts = parts.astype(jnp.float32)
    if parts.shape[0] == 1:
        return parts[0]
    return (parts[0] + parts[1]) + parts[2]


def pack_rows(flat, width):
    rows = -(-flat.shape[0] // width)
    return jnp.pad(flat, (0, rows * width - flat.shape[0])).reshape(rows, width), rows


def body(embed, beta, block_mask, counts, probes):
    n_dev = lax.axis_size("row") * lax.axis_size("col")
    n_row = lax.axis_size("row")
    me = lax.axis_index(AXES)
    shard, feat = embed.shape
    files = shard * n_dev
    nb = block_mask.shape[1]
    blk = files // nb
    local_blocks = block_mask.shape[0]

    unit_own = normalize(embed)
    beta_rows, beta_n = pack_rows(beta, feat)
    mask_rows, mask_n = pack_rows(block_mask.reshape(-1).astype(jnp.bfloat16), feat)
    replicate = files * files <= REPLICATE_CELLS
    n_probe = probes.shape[0]
    if (
        replicate
        and n_row % 2 == 0
        and shard % 2 == 0
        and blk % shard == 0
        and (blk // 2) % 8 == 0
        and files % 128 == 0
    ):
        return dense_path(embed, beta, block_mask, counts, probes, n_dev, n_row, me)
    if replicate:
        mask_flat = block_mask.reshape(-1).astype(jnp.bfloat16)
        mask_cols = -(-mask_flat.shape[0] // shard)
        mask_part = jnp.pad(mask_flat, (0, shard * mask_cols - mask_flat.shape[0]))
        used = 3 * n_probe + 1 + mask_cols
        lanes = -(-used // 128) * 128
        extra_cols = jnp.concatenate(
            [
                jnp.moveaxis(split3(probes.T), 0, 1).reshape(shard, 3 * n_probe),
                beta[:, None],
                mask_part.reshape(shard, mask_cols),
                jnp.zeros((shard, lanes - used), jnp.bfloat16),
            ],
            axis=1,
        )
        got = gather_halves(jnp.concatenate([unit_own, extra_cols], axis=1), n_dev, n_row)
        unit_all = got[:, :, :feat].reshape(files, feat)
        tail = got[:, :, feat:].reshape(files, lanes)
        probes_t = join3(
            jnp.stack([tail[:, k * n_probe : (k + 1) * n_probe] for k in range(3)])
        )
        beta_all = tail[:, 3 * n_probe]
        mask_got = got[:, :, feat + 3 * n_probe + 1 : feat + used].reshape(n_dev, -1)
        mask_got = mask_got[:, : local_blocks * nb]
    else:
        unit_all = gather_rows(unit_own, n_dev).reshape(files, feat)
        extra = gather_rows(jnp.concatenate([beta_rows, mask_rows], axis=0), n_dev)
        beta_all = extra[:, 0, :shard].reshape(files)
        mask_got = extra[:, beta_n:, :].reshape(n_dev, -1)[:, : local_blocks * nb]
    per_row = n_dev // n_row
    mask_full = (
        mask_got.reshape(n_row, per_row, local_blocks, nb)[:, 0].reshape(nb, nb).astype(jnp.int32)
    )
    scale_all = beta_all.astype(jnp.float32) / feat

    col_ids = lax.iota(jnp.int32, files)
    col_block = col_ids // blk
    in_block = lax.iota(jnp.int32, blk)
    col_live = (in_block[None, :] < counts[:, None]).reshape(files)

    if replicate:
        gram = lax.dot_general(
            unit_all, unit_all, (((1,), (1,)), ((), ())), preferred_element_type=jnp.float32
        )
        scores = gram * scale_all[:, None]
        block_ok = jnp.broadcast_to(
            (mask_full == 1)[:, None, :, None], (nb, blk, nb, blk)
        ).reshape(files, files)
        allowed = block_ok & col_live[None, :] & (col_ids[:, None] != col_ids[None, :])
        masked = jnp.where(allowed, scores, -1e30)
        row_top = jnp.max(masked, axis=1)
        row_mass = jnp.sum(jnp.where(allowed, jnp.exp(masked - row_top[:, None]), 0.0), axis=1)
        weights = jnp.where(allowed, jnp.exp(masked - row_top[:, None]) / row_mass[:, None], 0.0)
        col_mass = jnp.sum(weights, axis=0)
        inv_root = lax.rsqrt((1.0 + col_mass) * 0.5)
        affinity = weights.astype(jnp.bfloat16)
        state = probes_t
        for sweep in range(ITERS):
            scaled = (state * inv_root[:, None]).astype(jnp.bfloat16)
            row_part = jnp.dot(affinity, scaled, preferred_element_type=jnp.float32)
            col_part = lax.dot_general(
                affinity, scaled, (((0,), (0,)), ((), ())), preferred_element_type=jnp.float32
            )
            state = (row_part + col_part) * (0.5 * inv_root)[:, None]
        return lax.dynamic_slice_in_dim(state, me * shard, shard, 0).T

    own_ids = me * shard + lax.iota(jnp.int32, shard)
    own_block = own_ids // blk
    gram = lax.dot_general(
        unit_own, unit_all, (((1,), (1,)), ((), ())), preferred_element_type=jnp.float32
    )
    own_scale = lax.dynamic_slice_in_dim(scale_all, me * shard, shard, 0)
    scores = gram * own_scale[:, None]
    row_ok = jnp.take(jnp.take(mask_full, own_block, axis=0), col_block, axis=1) == 1
    allowed = row_ok & col_live[None, :] & (own_ids[:, None] != col_ids[None, :])
    masked = jnp.where(allowed, scores, -1e30)
    row_top = jnp.max(masked, axis=1)
    row_mass = jnp.sum(jnp.where(allowed, jnp.exp(masked - row_top[:, None]), 0.0), axis=1)
    weights = jnp.where(allowed, jnp.exp(masked - row_top[:, None]) / row_mass[:, None], 0.0)
    stats = gather_rows(jnp.stack([row_top, row_mass], axis=1), n_dev).reshape(files, 2)
    top_all, mass_all = stats[:, 0], stats[:, 1]
    scores_t = gram * scale_all[None, :]
    own_live = jnp.take(col_live, own_ids, axis=0)
    col_ok = jnp.take(jnp.take(mask_full, col_block, axis=0), own_block, axis=1).T == 1
    allowed_t = col_ok & own_live[:, None] & (own_ids[:, None] != col_ids[None, :])
    masked_t = jnp.where(allowed_t, scores_t, -1e30)
    weights_t = jnp.where(
        allowed_t, jnp.exp(masked_t - top_all[None, :]) / mass_all[None, :], 0.0
    )
    col_mass = jnp.sum(weights_t, axis=1)
    inv_root = lax.rsqrt((1.0 + col_mass) * 0.5)
    aff_rows = weights.astype(jnp.bfloat16)
    aff_cols = weights_t.astype(jnp.bfloat16)
    state = probes
    for sweep in range(ITERS):
        scaled = (state * inv_root[None, :]).astype(jnp.bfloat16)
        scaled_all = gather_rows(scaled.T, n_dev).reshape(files, probes.shape[0])
        row_part = jnp.dot(aff_rows, scaled_all, preferred_element_type=jnp.float32)
        col_part = jnp.dot(aff_cols, scaled_all, preferred_element_type=jnp.float32)
        state = ((row_part + col_part) * (0.5 * inv_root)[:, None]).T
    return state


def solution(mesh):
    placed = (
        P(AXES, None),
        P(AXES),
        P("row", None),
        P(),
        P(None, AXES),
    )
    return jax.shard_map(body, mesh=mesh, in_specs=placed, out_specs=P(None, AXES), check_vma=False)
```

```python
import jax
import jax.numpy as jnp
from jax import lax
from jax.experimental import pallas as pl
from jax.experimental.pallas import tpu as pltpu
from jax.sharding import PartitionSpec as P

ITERS = 2
PROBE_PARTS = 1
AXES = ("row", "col")
A2A_BYTES = 8 << 20
REPLICATE_CELLS = 1 << 21


def gather_rows(x, n_dev):
    if n_dev * x.size * x.dtype.itemsize <= A2A_BYTES:
        wide = jnp.broadcast_to(x[None], (n_dev,) + x.shape)
        return lax.all_to_all(wide, AXES, 0, 0, tiled=True)
    return lax.all_gather(x, AXES, axis=0, tiled=False)


def gather_halves(x, n_dev, n_row):
    if n_row % 2:
        return gather_rows(x, n_dev)
    rows = x.shape[0] + x.shape[0] % 2
    halves = jnp.pad(x, ((0, rows - x.shape[0]), (0, 0))).reshape(2, rows // 2, x.shape[1])
    per_row = n_dev // n_row
    wide = jnp.broadcast_to(
        halves[None, :, None], (n_row // 2, 2, per_row, rows // 2, x.shape[1])
    ).reshape(n_dev, rows // 2, x.shape[1])
    mine = lax.all_to_all(wide, AXES, 0, 0, tiled=True)
    other = lax.ppermute(mine, "row", [(r, r ^ 1) for r in range(n_row)])
    first = lax.axis_index("row") % 2 == 0
    low = jnp.where(first, mine, other)
    high = jnp.where(first, other, mine)
    return jnp.concatenate([low, high], axis=1)[:, : x.shape[0]]


def dense_kernel(n_iter, tile, beta_lane, n_parts, mine_ref, other_ref, rowmask_ref, out_ref, unit_t, unit_s, scale_s, aff_s):
    feat, files = unit_t.shape
    half = files // 2
    runs = half // tile
    for k, ref in enumerate((mine_ref, other_ref)):
        values = ref[:, 0:feat].astype(jnp.float32)
        unit = (
            values * lax.rsqrt(jnp.mean(values * values, axis=1, keepdims=True) + 1e-06)
        ).astype(jnp.bfloat16)
        unit_s[k * half : (k + 1) * half, :] = unit
        unit_t[:, k * half : (k + 1) * half] = unit.astype(jnp.float32).T.astype(jnp.bfloat16)
        scale_s[k * half : (k + 1) * half, :] = (
            ref[:, beta_lane : beta_lane + 1].astype(jnp.float32) / feat
        )
    per_tile = rowmask_ref.shape[1]
    run = tile // per_tile
    col_pos = lax.broadcasted_iota(jnp.int32, (tile, files), 1)
    row_pos = lax.broadcasted_iota(jnp.int32, (tile, files), 0)

    def step(t, colsum):
        p0 = pl.multiple_of(t * tile, tile)
        gram = jnp.dot(unit_s[pl.ds(p0, tile), :], unit_t[...], preferred_element_type=jnp.float32)
        scores = gram * scale_s[pl.ds(p0, tile), :]
        runs_here = rowmask_ref[t % runs]
        block_row = jnp.broadcast_to(runs_here[:, None, :], (per_tile, run, files)).reshape(tile, files)
        ok = (block_row > 0.0) & (row_pos + p0 != col_pos)
        masked = jnp.where(ok, scores, -1e30)
        top = jnp.max(masked, axis=1, keepdims=True)
        e = jnp.exp(masked - top)
        mass = jnp.sum(e, axis=1, keepdims=True)
        weights = e * (1.0 / mass)
        aff_s[pl.ds(p0, tile), :] = weights.astype(jnp.bfloat16)
        return colsum + jnp.sum(weights, axis=0, keepdims=True)

    colsum = lax.fori_loop(0, files // tile, step, jnp.zeros((1, files), jnp.float32))
    inv_root = lax.rsqrt((1.0 + colsum) * 0.5)
    n_probe = out_ref.shape[0]
    state = jnp.concatenate(
        [
            sum(
                ref[:, feat + k * n_probe : feat + (k + 1) * n_probe].astype(jnp.float32)
                for k in range(n_parts)
            ).T
            for ref in (mine_ref, other_ref)
        ],
        axis=1,
    )
    for sweep in range(n_iter):
        scaled_f = (state * inv_root).astype(jnp.bfloat16).astype(jnp.float32)
        scaled = scaled_f.astype(jnp.bfloat16)
        row_t = jnp.dot(aff_s[...], scaled_f.T.astype(jnp.bfloat16), preferred_element_type=jnp.float32)
        col_part = jnp.dot(scaled, aff_s[...], preferred_element_type=jnp.float32)
        state = (row_t.T + col_part) * (0.5 * inv_root)
    out_ref[...] = state


def dense_call(mine, other, rowmask, n_probe, feat, beta_lane):
    files = 2 * mine.shape[0]
    run = files // (2 * rowmask.shape[0])
    tile = run
    while tile * 2 <= min(512, files // 2) and (files // 2) % (tile * 2) == 0:
        tile *= 2
    rowmask = rowmask.reshape(-1, tile // run, files)
    vmem = pl.BlockSpec(memory_space=pltpu.VMEM)
    return pl.pallas_call(
        lambda *refs: dense_kernel(ITERS, tile, beta_lane, PROBE_PARTS, *refs),
        out_shape=jax.ShapeDtypeStruct((n_probe, files), jnp.float32),
        in_specs=[vmem, vmem, vmem],
        out_specs=vmem,
        scratch_shapes=[
            pltpu.VMEM((feat, files), jnp.bfloat16),
            pltpu.VMEM((files, feat), jnp.bfloat16),
            pltpu.VMEM((files, 1), jnp.float32),
            pltpu.VMEM((files, files), jnp.bfloat16),
        ],
        cost_estimate=pl.CostEstimate(
            flops=2 * files * files * feat + 4 * ITERS * files * files * n_probe,
            transcendentals=files * files,
            bytes_accessed=files * mine.shape[1] * 2 + 4 * files * n_probe,
        ),
    )(mine, other, rowmask)


def dense_path(embed, beta, block_mask, counts, probes, n_dev, n_row, me):
    shard, feat = embed.shape
    files = shard * n_dev
    half_s = shard // 2
    half_f = files // 2
    nb = block_mask.shape[1]
    blk = files // nb
    local_blocks = block_mask.shape[0]
    n_probe = probes.shape[0]
    per_row = n_dev // n_row
    mask_flat = block_mask.reshape(-1).astype(jnp.bfloat16)
    mask_cols = -(-mask_flat.shape[0] // half_s)
    mask_part = jnp.pad(mask_flat, (0, half_s * mask_cols - mask_flat.shape[0]))
    mask_part = jnp.tile(mask_part.reshape(half_s, mask_cols), (2, 1))
    used = PROBE_PARTS * n_probe + 1 + mask_cols
    lanes = -(-used // 128) * 128
    width = feat + lanes
    pieces = [
        (embed, 0),
        (split3(probes.T)[:PROBE_PARTS].transpose(1, 0, 2).reshape(shard, PROBE_PARTS * n_probe), feat),
        (beta[:, None], feat + PROBE_PARTS * n_probe),
        (mask_part, feat + PROBE_PARTS * n_probe + 1),
    ]
    payload = sum(
        jnp.pad(piece, ((0, 0), (start, width - start - piece.shape[1]))) for piece, start in pieces
    )
    width = payload.shape[1]
    halves = payload.reshape(2, half_s, width)
    wide = jnp.broadcast_to(
        halves[None, :, None], (n_row // 2, 2, per_row, half_s, width)
    ).reshape(n_dev, half_s, width)
    mine = lax.all_to_all(wide, AXES, 0, 0, tiled=True)
    other = lax.ppermute(mine, "row", [(r, r ^ 1) for r in range(n_row)])
    core = lax.axis_index("row") % 2
    pos = lax.iota(jnp.int32, files)
    run = blk // 2
    in_run = lax.iota(jnp.int32, files) % run
    run_dev = in_run // half_s
    half_of = jnp.broadcast_to((lax.iota(jnp.int32, 2) ^ core)[:, None, None], (2, nb, run))
    in_block = (run_dev % (blk // shard)) * shard + half_of.reshape(files) * half_s + in_run % half_s
    block_counts = jnp.broadcast_to(counts[None, :, None], (2, nb, run)).reshape(files)
    live = in_block < block_counts
    mine2 = mine.reshape(half_f, width)
    other2 = other.reshape(half_f, width)
    mask_got = mine[:, :, feat + PROBE_PARTS * n_probe + 1 : feat + used].reshape(n_dev, -1)
    mask_got = mask_got[:, : local_blocks * nb]
    mask_full = mask_got.reshape(n_row, per_row, local_blocks, nb)[:, 0].reshape(nb, nb)
    block_ok = jnp.broadcast_to((mask_full == 1)[:, None, :, None], (nb, 2, nb, run))
    rowmask = jnp.where(block_ok.reshape(nb, files) & live[None, :], 1.0, 0.0).astype(jnp.float32)
    state = dense_call(mine2, other2, rowmask, n_probe, feat, feat + PROBE_PARTS * n_probe)
    first = lax.dynamic_slice_in_dim(state, core * half_f + me * half_s, half_s, 1)
    second = lax.dynamic_slice_in_dim(state, (1 - core) * half_f + me * half_s, half_s, 1)
    return jnp.concatenate([first, second], axis=1)


def normalize(embed):
    values = embed.astype(jnp.float32)
    return (values * lax.rsqrt(jnp.mean(values * values, axis=1, keepdims=True) + 1e-06)).astype(
        jnp.bfloat16
    )


def split3(x):
    hi = lax.reduce_precision(x, exponent_bits=8, mantissa_bits=7)
    rest = x - hi
    mid = lax.reduce_precision(rest, exponent_bits=8, mantissa_bits=7)
    lo = rest - mid
    return jnp.stack([hi, mid, lo]).astype(jnp.bfloat16)


def join3(parts):
    parts = parts.astype(jnp.float32)
    if parts.shape[0] == 1:
        return parts[0]
    return (parts[0] + parts[1]) + parts[2]


def pack_rows(flat, width):
    rows = -(-flat.shape[0] // width)
    return jnp.pad(flat, (0, rows * width - flat.shape[0])).reshape(rows, width), rows


def body(embed, beta, block_mask, counts, probes):
    n_dev = lax.axis_size("row") * lax.axis_size("col")
    n_row = lax.axis_size("row")
    me = lax.axis_index(AXES)
    shard, feat = embed.shape
    files = shard * n_dev
    nb = block_mask.shape[1]
    blk = files // nb
    local_blocks = block_mask.shape[0]

    unit_own = normalize(embed)
    beta_rows, beta_n = pack_rows(beta, feat)
    mask_rows, mask_n = pack_rows(block_mask.reshape(-1).astype(jnp.bfloat16), feat)
    replicate = files * files <= REPLICATE_CELLS
    n_probe = probes.shape[0]
    if (
        replicate
        and n_row % 2 == 0
        and shard % 2 == 0
        and blk % shard == 0
        and (blk // 2) % 8 == 0
        and files % 128 == 0
    ):
        return dense_path(embed, beta, block_mask, counts, probes, n_dev, n_row, me)
    if replicate:
        mask_flat = block_mask.reshape(-1).astype(jnp.bfloat16)
        mask_cols = -(-mask_flat.shape[0] // shard)
        mask_part = jnp.pad(mask_flat, (0, shard * mask_cols - mask_flat.shape[0]))
        used = 3 * n_probe + 1 + mask_cols
        lanes = -(-used // 128) * 128
        extra_cols = jnp.concatenate(
            [
                jnp.moveaxis(split3(probes.T), 0, 1).reshape(shard, 3 * n_probe),
                beta[:, None],
                mask_part.reshape(shard, mask_cols),
                jnp.zeros((shard, lanes - used), jnp.bfloat16),
            ],
            axis=1,
        )
        got = gather_halves(jnp.concatenate([unit_own, extra_cols], axis=1), n_dev, n_row)
        unit_all = got[:, :, :feat].reshape(files, feat)
        tail = got[:, :, feat:].reshape(files, lanes)
        probes_t = join3(
            jnp.stack([tail[:, k * n_probe : (k + 1) * n_probe] for k in range(3)])
        )
        beta_all = tail[:, 3 * n_probe]
        mask_got = got[:, :, feat + 3 * n_probe + 1 : feat + used].reshape(n_dev, -1)
        mask_got = mask_got[:, : local_blocks * nb]
    else:
        unit_all = gather_rows(unit_own, n_dev).reshape(files, feat)
        extra = gather_rows(jnp.concatenate([beta_rows, mask_rows], axis=0), n_dev)
        beta_all = extra[:, 0, :shard].reshape(files)
        mask_got = extra[:, beta_n:, :].reshape(n_dev, -1)[:, : local_blocks * nb]
    per_row = n_dev // n_row
    mask_full = (
        mask_got.reshape(n_row, per_row, local_blocks, nb)[:, 0].reshape(nb, nb).astype(jnp.int32)
    )
    scale_all = beta_all.astype(jnp.float32) / feat

    col_ids = lax.iota(jnp.int32, files)
    col_block = col_ids // blk
    in_block = lax.iota(jnp.int32, blk)
    col_live = (in_block[None, :] < counts[:, None]).reshape(files)

    if replicate:
        gram = lax.dot_general(
            unit_all, unit_all, (((1,), (1,)), ((), ())), preferred_element_type=jnp.float32
        )
        scores = gram * scale_all[:, None]
        block_ok = jnp.broadcast_to(
            (mask_full == 1)[:, None, :, None], (nb, blk, nb, blk)
        ).reshape(files, files)
        allowed = block_ok & col_live[None, :] & (col_ids[:, None] != col_ids[None, :])
        masked = jnp.where(allowed, scores, -1e30)
        row_top = jnp.max(masked, axis=1)
        row_mass = jnp.sum(jnp.where(allowed, jnp.exp(masked - row_top[:, None]), 0.0), axis=1)
        weights = jnp.where(allowed, jnp.exp(masked - row_top[:, None]) / row_mass[:, None], 0.0)
        col_mass = jnp.sum(weights, axis=0)
        inv_root = lax.rsqrt((1.0 + col_mass) * 0.5)
        affinity = weights.astype(jnp.bfloat16)
        state = probes_t
        for sweep in range(ITERS):
            scaled = (state * inv_root[:, None]).astype(jnp.bfloat16)
            row_part = jnp.dot(affinity, scaled, preferred_element_type=jnp.float32)
            col_part = lax.dot_general(
                affinity, scaled, (((0,), (0,)), ((), ())), preferred_element_type=jnp.float32
            )
            state = (row_part + col_part) * (0.5 * inv_root)[:, None]
        return lax.dynamic_slice_in_dim(state, me * shard, shard, 0).T

    own_ids = me * shard + lax.iota(jnp.int32, shard)
    own_block = own_ids // blk
    gram = lax.dot_general(
        unit_own, unit_all, (((1,), (1,)), ((), ())), preferred_element_type=jnp.float32
    )
    own_scale = lax.dynamic_slice_in_dim(scale_all, me * shard, shard, 0)
    scores = gram * own_scale[:, None]
    row_ok = jnp.take(jnp.take(mask_full, own_block, axis=0), col_block, axis=1) == 1
    allowed = row_ok & col_live[None, :] & (own_ids[:, None] != col_ids[None, :])
    masked = jnp.where(allowed, scores, -1e30)
    row_top = jnp.max(masked, axis=1)
    row_mass = jnp.sum(jnp.where(allowed, jnp.exp(masked - row_top[:, None]), 0.0), axis=1)
    weights = jnp.where(allowed, jnp.exp(masked - row_top[:, None]) / row_mass[:, None], 0.0)
    stats = gather_rows(jnp.stack([row_top, row_mass], axis=1), n_dev).reshape(files, 2)
    top_all, mass_all = stats[:, 0], stats[:, 1]
    scores_t = gram * scale_all[None, :]
    own_live = jnp.take(col_live, own_ids, axis=0)
    col_ok = jnp.take(jnp.take(mask_full, col_block, axis=0), own_block, axis=1).T == 1
    allowed_t = col_ok & own_live[:, None] & (own_ids[:, None] != col_ids[None, :])
    masked_t = jnp.where(allowed_t, scores_t, -1e30)
    weights_t = jnp.where(
        allowed_t, jnp.exp(masked_t - top_all[None, :]) / mass_all[None, :], 0.0
    )
    col_mass = jnp.sum(weights_t, axis=1)
    inv_root = lax.rsqrt((1.0 + col_mass) * 0.5)
    aff_rows = weights.astype(jnp.bfloat16)
    aff_cols = weights_t.astype(jnp.bfloat16)
    state = probes
    for sweep in range(ITERS):
        scaled = (state * inv_root[None, :]).astype(jnp.bfloat16)
        scaled_all = gather_rows(scaled.T, n_dev).reshape(files, probes.shape[0])
        row_part = jnp.dot(aff_rows, scaled_all, preferred_element_type=jnp.float32)
        col_part = jnp.dot(aff_cols, scaled_all, preferred_element_type=jnp.float32)
        state = ((row_part + col_part) * (0.5 * inv_root)[:, None]).T
    return state


def solution(mesh):
    placed = (
        P(AXES, None),
        P(AXES),
        P("row", None),
        P(),
        P(None, AXES),
    )
    return jax.shard_map(body, mesh=mesh, in_specs=placed, out_specs=P(None, AXES), check_vma=False)
```

```python
import jax
import jax.numpy as jnp
from jax import lax
from jax.experimental import pallas as pl
from jax.experimental.pallas import tpu as pltpu
from jax.sharding import PartitionSpec as P

ITERS = 2
PROBE_PARTS = 1
AXES = ("row", "col")
A2A_BYTES = 8 << 20
REPLICATE_CELLS = 1 << 21


def gather_rows(x, n_dev):
    if n_dev * x.size * x.dtype.itemsize <= A2A_BYTES:
        wide = jnp.broadcast_to(x[None], (n_dev,) + x.shape)
        return lax.all_to_all(wide, AXES, 0, 0, tiled=True)
    return lax.all_gather(x, AXES, axis=0, tiled=False)


def gather_halves(x, n_dev, n_row):
    if n_row % 2:
        return gather_rows(x, n_dev)
    rows = x.shape[0] + x.shape[0] % 2
    halves = jnp.pad(x, ((0, rows - x.shape[0]), (0, 0))).reshape(2, rows // 2, x.shape[1])
    per_row = n_dev // n_row
    wide = jnp.broadcast_to(
        halves[None, :, None], (n_row // 2, 2, per_row, rows // 2, x.shape[1])
    ).reshape(n_dev, rows // 2, x.shape[1])
    mine = lax.all_to_all(wide, AXES, 0, 0, tiled=True)
    other = lax.ppermute(mine, "row", [(r, r ^ 1) for r in range(n_row)])
    first = lax.axis_index("row") % 2 == 0
    low = jnp.where(first, mine, other)
    high = jnp.where(first, other, mine)
    return jnp.concatenate([low, high], axis=1)[:, : x.shape[0]]


def dense_kernel(n_iter, tile, beta_lane, n_parts, mine_ref, other_ref, rowmask_ref, out_ref, unit_t, unit_s, scale_s, aff_s):
    feat, files = unit_t.shape
    half = files // 2
    runs = half // tile
    for k, ref in enumerate((mine_ref, other_ref)):
        values = ref[:, 0:feat].astype(jnp.float32)
        unit = (
            values * lax.rsqrt(jnp.mean(values * values, axis=1, keepdims=True) + 1e-06)
        ).astype(jnp.bfloat16)
        unit_s[k * half : (k + 1) * half, :] = unit
        unit_t[:, k * half : (k + 1) * half] = unit.astype(jnp.float32).T.astype(jnp.bfloat16)
        scale_s[k * half : (k + 1) * half, :] = (
            ref[:, beta_lane : beta_lane + 1].astype(jnp.float32) / feat
        )
    per_tile = rowmask_ref.shape[1]
    run = tile // per_tile
    col_pos = lax.broadcasted_iota(jnp.int32, (tile, files), 1)
    row_pos = lax.broadcasted_iota(jnp.int32, (tile, files), 0)

    def step(t, colsum):
        p0 = pl.multiple_of(t * tile, tile)
        gram = jnp.dot(unit_s[pl.ds(p0, tile), :], unit_t[...], preferred_element_type=jnp.float32)
        scores = gram * scale_s[pl.ds(p0, tile), :]
        runs_here = rowmask_ref[t % runs]
        block_row = jnp.broadcast_to(runs_here[:, None, :], (per_tile, run, files)).reshape(tile, files)
        ok = (block_row > 0.0) & (row_pos + p0 != col_pos)
        masked = jnp.where(ok, scores, -1e30)
        top = jnp.max(masked, axis=1, keepdims=True)
        e = jnp.exp(masked - top)
        mass = jnp.sum(e, axis=1, keepdims=True)
        weights = e * (1.0 / mass)
        aff_s[pl.ds(p0, tile), :] = weights.astype(jnp.bfloat16)
        return colsum + jnp.sum(weights, axis=0, keepdims=True)

    colsum = lax.fori_loop(0, files // tile, step, jnp.zeros((1, files), jnp.float32))
    inv_root = lax.rsqrt((1.0 + colsum) * 0.5)
    n_probe = out_ref.shape[1]
    state = jnp.concatenate(
        [
            sum(
                ref[:, feat + k * n_probe : feat + (k + 1) * n_probe].astype(jnp.float32)
                for k in range(n_parts)
            ).T
            for ref in (mine_ref, other_ref)
        ],
        axis=1,
    )
    for sweep in range(n_iter):
        scaled_f = (state * inv_root).astype(jnp.bfloat16).astype(jnp.float32)
        scaled = scaled_f.astype(jnp.bfloat16)
        row_t = jnp.dot(aff_s[...], scaled_f.T.astype(jnp.bfloat16), preferred_element_type=jnp.float32)
        col_part = jnp.dot(scaled, aff_s[...], preferred_element_type=jnp.float32)
        if sweep + 1 < n_iter:
            state = (row_t.T + col_part) * (0.5 * inv_root)
        else:
            out_ref[...] = (row_t + col_part.T) * (0.5 * inv_root).T


def dense_call(mine, other, rowmask, n_probe, feat, beta_lane):
    files = 2 * mine.shape[0]
    run = files // (2 * rowmask.shape[0])
    tile = run
    while tile * 2 <= min(512, files // 2) and (files // 2) % (tile * 2) == 0:
        tile *= 2
    rowmask = rowmask.reshape(-1, tile // run, files)
    vmem = pl.BlockSpec(memory_space=pltpu.VMEM)
    return pl.pallas_call(
        lambda *refs: dense_kernel(ITERS, tile, beta_lane, PROBE_PARTS, *refs),
        out_shape=jax.ShapeDtypeStruct((files, n_probe), jnp.float32),
        in_specs=[vmem, vmem, vmem],
        out_specs=vmem,
        scratch_shapes=[
            pltpu.VMEM((feat, files), jnp.bfloat16),
            pltpu.VMEM((files, feat), jnp.bfloat16),
            pltpu.VMEM((files, 1), jnp.float32),
            pltpu.VMEM((files, files), jnp.bfloat16),
        ],
        cost_estimate=pl.CostEstimate(
            flops=2 * files * files * feat + 4 * ITERS * files * files * n_probe,
            transcendentals=files * files,
            bytes_accessed=files * mine.shape[1] * 2 + 4 * files * n_probe,
        ),
    )(mine, other, rowmask)


def dense_path(embed, beta, block_mask, counts, probes, n_dev, n_row, me):
    shard, feat = embed.shape
    files = shard * n_dev
    half_s = shard // 2
    half_f = files // 2
    nb = block_mask.shape[1]
    blk = files // nb
    local_blocks = block_mask.shape[0]
    n_probe = probes.shape[0]
    per_row = n_dev // n_row
    mask_flat = block_mask.reshape(-1).astype(jnp.bfloat16)
    mask_cols = -(-mask_flat.shape[0] // half_s)
    mask_part = jnp.pad(mask_flat, (0, half_s * mask_cols - mask_flat.shape[0]))
    mask_part = jnp.tile(mask_part.reshape(half_s, mask_cols), (2, 1))
    used = PROBE_PARTS * n_probe + 1 + mask_cols
    lanes = -(-used // 128) * 128
    extras = jnp.concatenate(
        [
            split3(probes)[:PROBE_PARTS].astype(jnp.float32).reshape(PROBE_PARTS * n_probe, shard),
            beta[None, :].astype(jnp.float32),
            mask_part.T.astype(jnp.float32),
        ],
        axis=0,
    )
    payload = jnp.concatenate(
        [embed, jnp.pad(extras.T.astype(jnp.bfloat16), ((0, 0), (0, lanes - used)))], axis=1
    )
    width = payload.shape[1]
    halves = payload.reshape(2, half_s, width)
    wide = jnp.broadcast_to(
        halves[None, :, None], (n_row // 2, 2, per_row, half_s, width)
    ).reshape(n_dev, half_s, width)
    mine = lax.all_to_all(wide, AXES, 0, 0, tiled=True)
    other = lax.ppermute(mine, "row", [(r, r ^ 1) for r in range(n_row)])
    core = lax.axis_index("row") % 2
    pos = lax.iota(jnp.int32, files)
    run = blk // 2
    in_run = lax.iota(jnp.int32, files) % run
    run_dev = in_run // half_s
    half_of = jnp.broadcast_to((lax.iota(jnp.int32, 2) ^ core)[:, None, None], (2, nb, run))
    in_block = (run_dev % (blk // shard)) * shard + half_of.reshape(files) * half_s + in_run % half_s
    block_counts = jnp.broadcast_to(counts[None, :, None], (2, nb, run)).reshape(files)
    live = in_block < block_counts
    mine2 = mine.reshape(half_f, width)
    other2 = other.reshape(half_f, width)
    mask_got = mine[:, :, feat + PROBE_PARTS * n_probe + 1 : feat + used].reshape(n_dev, -1)
    mask_got = mask_got[:, : local_blocks * nb]
    mask_full = mask_got.reshape(n_row, per_row, local_blocks, nb)[:, 0].reshape(nb, nb)
    block_ok = jnp.broadcast_to((mask_full == 1)[:, None, :, None], (nb, 2, nb, run))
    rowmask = jnp.where(block_ok.reshape(nb, files) & live[None, :], 1.0, 0.0).astype(jnp.float32)
    state_t = dense_call(mine2, other2, rowmask, n_probe, feat, feat + PROBE_PARTS * n_probe)
    first = lax.dynamic_slice_in_dim(state_t, core * half_f + me * half_s, half_s, 0)
    second = lax.dynamic_slice_in_dim(state_t, (1 - core) * half_f + me * half_s, half_s, 0)
    return jnp.concatenate([first, second], axis=0).T


def normalize(embed):
    values = embed.astype(jnp.float32)
    return (values * lax.rsqrt(jnp.mean(values * values, axis=1, keepdims=True) + 1e-06)).astype(
        jnp.bfloat16
    )


def split3(x):
    hi = lax.reduce_precision(x, exponent_bits=8, mantissa_bits=7)
    rest = x - hi
    mid = lax.reduce_precision(rest, exponent_bits=8, mantissa_bits=7)
    lo = rest - mid
    return jnp.stack([hi, mid, lo]).astype(jnp.bfloat16)


def join3(parts):
    parts = parts.astype(jnp.float32)
    if parts.shape[0] == 1:
        return parts[0]
    return (parts[0] + parts[1]) + parts[2]


def pack_rows(flat, width):
    rows = -(-flat.shape[0] // width)
    return jnp.pad(flat, (0, rows * width - flat.shape[0])).reshape(rows, width), rows


def body(embed, beta, block_mask, counts, probes):
    n_dev = lax.axis_size("row") * lax.axis_size("col")
    n_row = lax.axis_size("row")
    me = lax.axis_index(AXES)
    shard, feat = embed.shape
    files = shard * n_dev
    nb = block_mask.shape[1]
    blk = files // nb
    local_blocks = block_mask.shape[0]

    unit_own = normalize(embed)
    beta_rows, beta_n = pack_rows(beta, feat)
    mask_rows, mask_n = pack_rows(block_mask.reshape(-1).astype(jnp.bfloat16), feat)
    replicate = files * files <= REPLICATE_CELLS
    n_probe = probes.shape[0]
    if (
        replicate
        and n_row % 2 == 0
        and shard % 2 == 0
        and blk % shard == 0
        and (blk // 2) % 8 == 0
        and files % 128 == 0
    ):
        return dense_path(embed, beta, block_mask, counts, probes, n_dev, n_row, me)
    if replicate:
        mask_flat = block_mask.reshape(-1).astype(jnp.bfloat16)
        mask_cols = -(-mask_flat.shape[0] // shard)
        mask_part = jnp.pad(mask_flat, (0, shard * mask_cols - mask_flat.shape[0]))
        used = 3 * n_probe + 1 + mask_cols
        lanes = -(-used // 128) * 128
        extra_cols = jnp.concatenate(
            [
                jnp.moveaxis(split3(probes.T), 0, 1).reshape(shard, 3 * n_probe),
                beta[:, None],
                mask_part.reshape(shard, mask_cols),
                jnp.zeros((shard, lanes - used), jnp.bfloat16),
            ],
            axis=1,
        )
        got = gather_halves(jnp.concatenate([unit_own, extra_cols], axis=1), n_dev, n_row)
        unit_all = got[:, :, :feat].reshape(files, feat)
        tail = got[:, :, feat:].reshape(files, lanes)
        probes_t = join3(
            jnp.stack([tail[:, k * n_probe : (k + 1) * n_probe] for k in range(3)])
        )
        beta_all = tail[:, 3 * n_probe]
        mask_got = got[:, :, feat + 3 * n_probe + 1 : feat + used].reshape(n_dev, -1)
        mask_got = mask_got[:, : local_blocks * nb]
    else:
        unit_all = gather_rows(unit_own, n_dev).reshape(files, feat)
        extra = gather_rows(jnp.concatenate([beta_rows, mask_rows], axis=0), n_dev)
        beta_all = extra[:, 0, :shard].reshape(files)
        mask_got = extra[:, beta_n:, :].reshape(n_dev, -1)[:, : local_blocks * nb]
    per_row = n_dev // n_row
    mask_full = (
        mask_got.reshape(n_row, per_row, local_blocks, nb)[:, 0].reshape(nb, nb).astype(jnp.int32)
    )
    scale_all = beta_all.astype(jnp.float32) / feat

    col_ids = lax.iota(jnp.int32, files)
    col_block = col_ids // blk
    in_block = lax.iota(jnp.int32, blk)
    col_live = (in_block[None, :] < counts[:, None]).reshape(files)

    if replicate:
        gram = lax.dot_general(
            unit_all, unit_all, (((1,), (1,)), ((), ())), preferred_element_type=jnp.float32
        )
        scores = gram * scale_all[:, None]
        block_ok = jnp.broadcast_to(
            (mask_full == 1)[:, None, :, None], (nb, blk, nb, blk)
        ).reshape(files, files)
        allowed = block_ok & col_live[None, :] & (col_ids[:, None] != col_ids[None, :])
        masked = jnp.where(allowed, scores, -1e30)
        row_top = jnp.max(masked, axis=1)
        row_mass = jnp.sum(jnp.where(allowed, jnp.exp(masked - row_top[:, None]), 0.0), axis=1)
        weights = jnp.where(allowed, jnp.exp(masked - row_top[:, None]) / row_mass[:, None], 0.0)
        col_mass = jnp.sum(weights, axis=0)
        inv_root = lax.rsqrt((1.0 + col_mass) * 0.5)
        affinity = weights.astype(jnp.bfloat16)
        state = probes_t
        for sweep in range(ITERS):
            scaled = (state * inv_root[:, None]).astype(jnp.bfloat16)
            row_part = jnp.dot(affinity, scaled, preferred_element_type=jnp.float32)
            col_part = lax.dot_general(
                affinity, scaled, (((0,), (0,)), ((), ())), preferred_element_type=jnp.float32
            )
            state = (row_part + col_part) * (0.5 * inv_root)[:, None]
        return lax.dynamic_slice_in_dim(state, me * shard, shard, 0).T

    own_ids = me * shard + lax.iota(jnp.int32, shard)
    own_block = own_ids // blk
    gram = lax.dot_general(
        unit_own, unit_all, (((1,), (1,)), ((), ())), preferred_element_type=jnp.float32
    )
    own_scale = lax.dynamic_slice_in_dim(scale_all, me * shard, shard, 0)
    scores = gram * own_scale[:, None]
    row_ok = jnp.take(jnp.take(mask_full, own_block, axis=0), col_block, axis=1) == 1
    allowed = row_ok & col_live[None, :] & (own_ids[:, None] != col_ids[None, :])
    masked = jnp.where(allowed, scores, -1e30)
    row_top = jnp.max(masked, axis=1)
    row_mass = jnp.sum(jnp.where(allowed, jnp.exp(masked - row_top[:, None]), 0.0), axis=1)
    weights = jnp.where(allowed, jnp.exp(masked - row_top[:, None]) / row_mass[:, None], 0.0)
    stats = gather_rows(jnp.stack([row_top, row_mass], axis=1), n_dev).reshape(files, 2)
    top_all, mass_all = stats[:, 0], stats[:, 1]
    scores_t = gram * scale_all[None, :]
    own_live = jnp.take(col_live, own_ids, axis=0)
    col_ok = jnp.take(jnp.take(mask_full, col_block, axis=0), own_block, axis=1).T == 1
    allowed_t = col_ok & own_live[:, None] & (own_ids[:, None] != col_ids[None, :])
    masked_t = jnp.where(allowed_t, scores_t, -1e30)
    weights_t = jnp.where(
        allowed_t, jnp.exp(masked_t - top_all[None, :]) / mass_all[None, :], 0.0
    )
    col_mass = jnp.sum(weights_t, axis=1)
    inv_root = lax.rsqrt((1.0 + col_mass) * 0.5)
    aff_rows = weights.astype(jnp.bfloat16)
    aff_cols = weights_t.astype(jnp.bfloat16)
    state = probes
    for sweep in range(ITERS):
        scaled = (state * inv_root[None, :]).astype(jnp.bfloat16)
        scaled_all = gather_rows(scaled.T, n_dev).reshape(files, probes.shape[0])
        row_part = jnp.dot(aff_rows, scaled_all, preferred_element_type=jnp.float32)
        col_part = jnp.dot(aff_cols, scaled_all, preferred_element_type=jnp.float32)
        state = ((row_part + col_part) * (0.5 * inv_root)[:, None]).T
    return state


def solution(mesh):
    placed = (
        P(AXES, None),
        P(AXES),
        P("row", None),
        P(),
        P(None, AXES),
    )
    return jax.shard_map(body, mesh=mesh, in_specs=placed, out_specs=P(None, AXES), check_vma=False)
```

```python
import jax
import jax.numpy as jnp
from jax import lax
from jax.experimental import pallas as pl
from jax.experimental.pallas import tpu as pltpu
from jax.sharding import PartitionSpec as P

ITERS = 2
PROBE_PARTS = 1
AXES = ("row", "col")
A2A_BYTES = 8 << 20
REPLICATE_CELLS = 1 << 21


def gather_rows(x, n_dev):
    if n_dev * x.size * x.dtype.itemsize <= A2A_BYTES:
        wide = jnp.broadcast_to(x[None], (n_dev,) + x.shape)
        return lax.all_to_all(wide, AXES, 0, 0, tiled=True)
    return lax.all_gather(x, AXES, axis=0, tiled=False)


def gather_halves(x, n_dev, n_row):
    if n_row % 2:
        return gather_rows(x, n_dev)
    rows = x.shape[0] + x.shape[0] % 2
    halves = jnp.pad(x, ((0, rows - x.shape[0]), (0, 0))).reshape(2, rows // 2, x.shape[1])
    per_row = n_dev // n_row
    wide = jnp.broadcast_to(
        halves[None, :, None], (n_row // 2, 2, per_row, rows // 2, x.shape[1])
    ).reshape(n_dev, rows // 2, x.shape[1])
    mine = lax.all_to_all(wide, AXES, 0, 0, tiled=True)
    other = lax.ppermute(mine, "row", [(r, r ^ 1) for r in range(n_row)])
    first = lax.axis_index("row") % 2 == 0
    low = jnp.where(first, mine, other)
    high = jnp.where(first, other, mine)
    return jnp.concatenate([low, high], axis=1)[:, : x.shape[0]]


def dense_kernel(n_iter, tile, beta_lane, n_parts, mine_ref, other_hbm, rowmask_ref, out_ref, unit_t, unit_s, scale_s, aff_s, other_ref, copy_sem):
    feat, files = unit_t.shape
    half = files // 2
    runs = half // tile
    fetch = pltpu.make_async_copy(other_hbm, other_ref, copy_sem)
    fetch.start()
    for k, ref in enumerate((mine_ref, other_ref)):
        if k == 1:
            fetch.wait()
        values = ref[:, 0:feat].astype(jnp.float32)
        unit = (
            values * lax.rsqrt(jnp.mean(values * values, axis=1, keepdims=True) + 1e-06)
        ).astype(jnp.bfloat16)
        unit_s[k * half : (k + 1) * half, :] = unit
        unit_t[:, k * half : (k + 1) * half] = unit.astype(jnp.float32).T.astype(jnp.bfloat16)
        scale_s[k * half : (k + 1) * half, :] = (
            ref[:, beta_lane : beta_lane + 1].astype(jnp.float32) / feat
        )
    per_tile = rowmask_ref.shape[1]
    run = tile // per_tile
    col_pos = lax.broadcasted_iota(jnp.int32, (tile, files), 1)
    row_pos = lax.broadcasted_iota(jnp.int32, (tile, files), 0)

    def step(t, colsum):
        p0 = pl.multiple_of(t * tile, tile)
        gram = jnp.dot(unit_s[pl.ds(p0, tile), :], unit_t[...], preferred_element_type=jnp.float32)
        scores = gram * scale_s[pl.ds(p0, tile), :]
        runs_here = rowmask_ref[t % runs]
        block_row = jnp.broadcast_to(runs_here[:, None, :], (per_tile, run, files)).reshape(tile, files)
        ok = (block_row > 0.0) & (row_pos + p0 != col_pos)
        masked = jnp.where(ok, scores, -1e30)
        top = jnp.max(masked, axis=1, keepdims=True)
        e = jnp.exp(masked - top)
        mass = jnp.sum(e, axis=1, keepdims=True)
        weights = e * (1.0 / mass)
        aff_s[pl.ds(p0, tile), :] = weights.astype(jnp.bfloat16)
        return colsum + jnp.sum(weights, axis=0, keepdims=True)

    colsum = lax.fori_loop(0, files // tile, step, jnp.zeros((1, files), jnp.float32))
    inv_root = lax.rsqrt((1.0 + colsum) * 0.5)
    n_probe = out_ref.shape[1]
    state = jnp.concatenate(
        [
            sum(
                ref[:, feat + k * n_probe : feat + (k + 1) * n_probe].astype(jnp.float32)
                for k in range(n_parts)
            ).T
            for ref in (mine_ref, other_ref)
        ],
        axis=1,
    )
    for sweep in range(n_iter):
        scaled_f = (state * inv_root).astype(jnp.bfloat16).astype(jnp.float32)
        scaled = scaled_f.astype(jnp.bfloat16)
        row_t = jnp.dot(aff_s[...], scaled_f.T.astype(jnp.bfloat16), preferred_element_type=jnp.float32)
        col_part = jnp.dot(scaled, aff_s[...], preferred_element_type=jnp.float32)
        if sweep + 1 < n_iter:
            state = (row_t.T + col_part) * (0.5 * inv_root)
        else:
            out_ref[...] = (row_t + col_part.T) * (0.5 * inv_root).T


def dense_call(mine, other, rowmask, n_probe, feat, beta_lane):
    files = 2 * mine.shape[0]
    run = files // (2 * rowmask.shape[0])
    tile = run
    while tile * 2 <= min(512, files // 2) and (files // 2) % (tile * 2) == 0:
        tile *= 2
    rowmask = rowmask.reshape(-1, tile // run, files)
    vmem = pl.BlockSpec(memory_space=pltpu.VMEM)
    return pl.pallas_call(
        lambda *refs: dense_kernel(ITERS, tile, beta_lane, PROBE_PARTS, *refs),
        out_shape=jax.ShapeDtypeStruct((files, n_probe), jnp.float32),
        in_specs=[vmem, pl.BlockSpec(memory_space=pl.ANY), vmem],
        out_specs=vmem,
        scratch_shapes=[
            pltpu.VMEM((feat, files), jnp.bfloat16),
            pltpu.VMEM((files, feat), jnp.bfloat16),
            pltpu.VMEM((files, 1), jnp.float32),
            pltpu.VMEM((files, files), jnp.bfloat16),
            pltpu.VMEM(other.shape, other.dtype),
            pltpu.SemaphoreType.DMA(()),
        ],
        cost_estimate=pl.CostEstimate(
            flops=2 * files * files * feat + 4 * ITERS * files * files * n_probe,
            transcendentals=files * files,
            bytes_accessed=files * mine.shape[1] * 2 + 4 * files * n_probe,
        ),
    )(mine, other, rowmask)


def dense_path(embed, beta, block_mask, counts, probes, n_dev, n_row, me):
    shard, feat = embed.shape
    files = shard * n_dev
    half_s = shard // 2
    half_f = files // 2
    nb = block_mask.shape[1]
    blk = files // nb
    local_blocks = block_mask.shape[0]
    n_probe = probes.shape[0]
    per_row = n_dev // n_row
    mask_flat = block_mask.reshape(-1).astype(jnp.bfloat16)
    mask_cols = -(-mask_flat.shape[0] // half_s)
    mask_part = jnp.pad(mask_flat, (0, half_s * mask_cols - mask_flat.shape[0]))
    mask_part = jnp.tile(mask_part.reshape(half_s, mask_cols), (2, 1))
    used = PROBE_PARTS * n_probe + 1 + mask_cols
    lanes = -(-used // 128) * 128
    extras = jnp.concatenate(
        [
            split3(probes)[:PROBE_PARTS].astype(jnp.float32).reshape(PROBE_PARTS * n_probe, shard),
            beta[None, :].astype(jnp.float32),
            mask_part.T.astype(jnp.float32),
        ],
        axis=0,
    )
    payload = jnp.concatenate(
        [embed, jnp.pad(extras.T.astype(jnp.bfloat16), ((0, 0), (0, lanes - used)))], axis=1
    )
    width = payload.shape[1]
    halves = payload.reshape(2, half_s, width)
    wide = jnp.broadcast_to(
        halves[None, :, None], (n_row // 2, 2, per_row, half_s, width)
    ).reshape(n_dev, half_s, width)
    mine = lax.all_to_all(wide, AXES, 0, 0, tiled=True)
    other = lax.ppermute(mine, "row", [(r, r ^ 1) for r in range(n_row)])
    core = lax.axis_index("row") % 2
    pos = lax.iota(jnp.int32, files)
    run = blk // 2
    in_run = lax.iota(jnp.int32, files) % run
    run_dev = in_run // half_s
    half_of = jnp.broadcast_to((lax.iota(jnp.int32, 2) ^ core)[:, None, None], (2, nb, run))
    in_block = (run_dev % (blk // shard)) * shard + half_of.reshape(files) * half_s + in_run % half_s
    block_counts = jnp.broadcast_to(counts[None, :, None], (2, nb, run)).reshape(files)
    live = in_block < block_counts
    mine2 = mine.reshape(half_f, width)
    other2 = other.reshape(half_f, width)
    mask_got = mine[:, :, feat + PROBE_PARTS * n_probe + 1 : feat + used].reshape(n_dev, -1)
    mask_got = mask_got[:, : local_blocks * nb]
    mask_full = mask_got.reshape(n_row, per_row, local_blocks, nb)[:, 0].reshape(nb, nb)
    block_ok = jnp.broadcast_to((mask_full == 1)[:, None, :, None], (nb, 2, nb, run))
    rowmask = jnp.where(block_ok.reshape(nb, files) & live[None, :], 1.0, 0.0).astype(jnp.float32)
    state_t = dense_call(mine2, other2, rowmask, n_probe, feat, feat + PROBE_PARTS * n_probe)
    first = lax.dynamic_slice_in_dim(state_t, core * half_f + me * half_s, half_s, 0)
    second = lax.dynamic_slice_in_dim(state_t, (1 - core) * half_f + me * half_s, half_s, 0)
    return jnp.concatenate([first, second], axis=0).T


def normalize(embed):
    values = embed.astype(jnp.float32)
    return (values * lax.rsqrt(jnp.mean(values * values, axis=1, keepdims=True) + 1e-06)).astype(
        jnp.bfloat16
    )


def split3(x):
    hi = lax.reduce_precision(x, exponent_bits=8, mantissa_bits=7)
    rest = x - hi
    mid = lax.reduce_precision(rest, exponent_bits=8, mantissa_bits=7)
    lo = rest - mid
    return jnp.stack([hi, mid, lo]).astype(jnp.bfloat16)


def join3(parts):
    parts = parts.astype(jnp.float32)
    if parts.shape[0] == 1:
        return parts[0]
    return (parts[0] + parts[1]) + parts[2]


def pack_rows(flat, width):
    rows = -(-flat.shape[0] // width)
    return jnp.pad(flat, (0, rows * width - flat.shape[0])).reshape(rows, width), rows


def body(embed, beta, block_mask, counts, probes):
    n_dev = lax.axis_size("row") * lax.axis_size("col")
    n_row = lax.axis_size("row")
    me = lax.axis_index(AXES)
    shard, feat = embed.shape
    files = shard * n_dev
    nb = block_mask.shape[1]
    blk = files // nb
    local_blocks = block_mask.shape[0]

    unit_own = normalize(embed)
    beta_rows, beta_n = pack_rows(beta, feat)
    mask_rows, mask_n = pack_rows(block_mask.reshape(-1).astype(jnp.bfloat16), feat)
    replicate = files * files <= REPLICATE_CELLS
    n_probe = probes.shape[0]
    if (
        replicate
        and n_row % 2 == 0
        and shard % 2 == 0
        and blk % shard == 0
        and (blk // 2) % 8 == 0
        and files % 128 == 0
    ):
        return dense_path(embed, beta, block_mask, counts, probes, n_dev, n_row, me)
    if replicate:
        mask_flat = block_mask.reshape(-1).astype(jnp.bfloat16)
        mask_cols = -(-mask_flat.shape[0] // shard)
        mask_part = jnp.pad(mask_flat, (0, shard * mask_cols - mask_flat.shape[0]))
        used = 3 * n_probe + 1 + mask_cols
        lanes = -(-used // 128) * 128
        extra_cols = jnp.concatenate(
            [
                jnp.moveaxis(split3(probes.T), 0, 1).reshape(shard, 3 * n_probe),
                beta[:, None],
                mask_part.reshape(shard, mask_cols),
                jnp.zeros((shard, lanes - used), jnp.bfloat16),
            ],
            axis=1,
        )
        got = gather_halves(jnp.concatenate([unit_own, extra_cols], axis=1), n_dev, n_row)
        unit_all = got[:, :, :feat].reshape(files, feat)
        tail = got[:, :, feat:].reshape(files, lanes)
        probes_t = join3(
            jnp.stack([tail[:, k * n_probe : (k + 1) * n_probe] for k in range(3)])
        )
        beta_all = tail[:, 3 * n_probe]
        mask_got = got[:, :, feat + 3 * n_probe + 1 : feat + used].reshape(n_dev, -1)
        mask_got = mask_got[:, : local_blocks * nb]
    else:
        unit_all = gather_rows(unit_own, n_dev).reshape(files, feat)
        extra = gather_rows(jnp.concatenate([beta_rows, mask_rows], axis=0), n_dev)
        beta_all = extra[:, 0, :shard].reshape(files)
        mask_got = extra[:, beta_n:, :].reshape(n_dev, -1)[:, : local_blocks * nb]
    per_row = n_dev // n_row
    mask_full = (
        mask_got.reshape(n_row, per_row, local_blocks, nb)[:, 0].reshape(nb, nb).astype(jnp.int32)
    )
    scale_all = beta_all.astype(jnp.float32) / feat

    col_ids = lax.iota(jnp.int32, files)
    col_block = col_ids // blk
    in_block = lax.iota(jnp.int32, blk)
    col_live = (in_block[None, :] < counts[:, None]).reshape(files)

    if replicate:
        gram = lax.dot_general(
            unit_all, unit_all, (((1,), (1,)), ((), ())), preferred_element_type=jnp.float32
        )
        scores = gram * scale_all[:, None]
        block_ok = jnp.broadcast_to(
            (mask_full == 1)[:, None, :, None], (nb, blk, nb, blk)
        ).reshape(files, files)
        allowed = block_ok & col_live[None, :] & (col_ids[:, None] != col_ids[None, :])
        masked = jnp.where(allowed, scores, -1e30)
        row_top = jnp.max(masked, axis=1)
        row_mass = jnp.sum(jnp.where(allowed, jnp.exp(masked - row_top[:, None]), 0.0), axis=1)
        weights = jnp.where(allowed, jnp.exp(masked - row_top[:, None]) / row_mass[:, None], 0.0)
        col_mass = jnp.sum(weights, axis=0)
        inv_root = lax.rsqrt((1.0 + col_mass) * 0.5)
        affinity = weights.astype(jnp.bfloat16)
        state = probes_t
        for sweep in range(ITERS):
            scaled = (state * inv_root[:, None]).astype(jnp.bfloat16)
            row_part = jnp.dot(affinity, scaled, preferred_element_type=jnp.float32)
            col_part = lax.dot_general(
                affinity, scaled, (((0,), (0,)), ((), ())), preferred_element_type=jnp.float32
            )
            state = (row_part + col_part) * (0.5 * inv_root)[:, None]
        return lax.dynamic_slice_in_dim(state, me * shard, shard, 0).T

    own_ids = me * shard + lax.iota(jnp.int32, shard)
    own_block = own_ids // blk
    gram = lax.dot_general(
        unit_own, unit_all, (((1,), (1,)), ((), ())), preferred_element_type=jnp.float32
    )
    own_scale = lax.dynamic_slice_in_dim(scale_all, me * shard, shard, 0)
    scores = gram * own_scale[:, None]
    row_ok = jnp.take(jnp.take(mask_full, own_block, axis=0), col_block, axis=1) == 1
    allowed = row_ok & col_live[None, :] & (own_ids[:, None] != col_ids[None, :])
    masked = jnp.where(allowed, scores, -1e30)
    row_top = jnp.max(masked, axis=1)
    row_mass = jnp.sum(jnp.where(allowed, jnp.exp(masked - row_top[:, None]), 0.0), axis=1)
    weights = jnp.where(allowed, jnp.exp(masked - row_top[:, None]) / row_mass[:, None], 0.0)
    stats = gather_rows(jnp.stack([row_top, row_mass], axis=1), n_dev).reshape(files, 2)
    top_all, mass_all = stats[:, 0], stats[:, 1]
    scores_t = gram * scale_all[None, :]
    own_live = jnp.take(col_live, own_ids, axis=0)
    col_ok = jnp.take(jnp.take(mask_full, col_block, axis=0), own_block, axis=1).T == 1
    allowed_t = col_ok & own_live[:, None] & (own_ids[:, None] != col_ids[None, :])
    masked_t = jnp.where(allowed_t, scores_t, -1e30)
    weights_t = jnp.where(
        allowed_t, jnp.exp(masked_t - top_all[None, :]) / mass_all[None, :], 0.0
    )
    col_mass = jnp.sum(weights_t, axis=1)
    inv_root = lax.rsqrt((1.0 + col_mass) * 0.5)
    aff_rows = weights.astype(jnp.bfloat16)
    aff_cols = weights_t.astype(jnp.bfloat16)
    state = probes
    for sweep in range(ITERS):
        scaled = (state * inv_root[None, :]).astype(jnp.bfloat16)
        scaled_all = gather_rows(scaled.T, n_dev).reshape(files, probes.shape[0])
        row_part = jnp.dot(aff_rows, scaled_all, preferred_element_type=jnp.float32)
        col_part = jnp.dot(aff_cols, scaled_all, preferred_element_type=jnp.float32)
        state = ((row_part + col_part) * (0.5 * inv_root)[:, None]).T
    return state


def solution(mesh):
    placed = (
        P(AXES, None),
        P(AXES),
        P("row", None),
        P(),
        P(None, AXES),
    )
    return jax.shard_map(body, mesh=mesh, in_specs=placed, out_specs=P(None, AXES), check_vma=False)
```

```python
import jax
import jax.numpy as jnp
from jax import lax
from jax.experimental import pallas as pl
from jax.experimental.pallas import tpu as pltpu
from jax.sharding import PartitionSpec as P

ITERS = 2
PROBE_PARTS = 1
AXES = ("row", "col")
A2A_BYTES = 8 << 20
REPLICATE_CELLS = 1 << 21


def gather_rows(x, n_dev):
    if n_dev * x.size * x.dtype.itemsize <= A2A_BYTES:
        wide = jnp.broadcast_to(x[None], (n_dev,) + x.shape)
        return lax.all_to_all(wide, AXES, 0, 0, tiled=True)
    return lax.all_gather(x, AXES, axis=0, tiled=False)


def gather_halves(x, n_dev, n_row):
    if n_row % 2:
        return gather_rows(x, n_dev)
    rows = x.shape[0] + x.shape[0] % 2
    halves = jnp.pad(x, ((0, rows - x.shape[0]), (0, 0))).reshape(2, rows // 2, x.shape[1])
    per_row = n_dev // n_row
    wide = jnp.broadcast_to(
        halves[None, :, None], (n_row // 2, 2, per_row, rows // 2, x.shape[1])
    ).reshape(n_dev, rows // 2, x.shape[1])
    mine = lax.all_to_all(wide, AXES, 0, 0, tiled=True)
    other = lax.ppermute(mine, "row", [(r, r ^ 1) for r in range(n_row)])
    first = lax.axis_index("row") % 2 == 0
    low = jnp.where(first, mine, other)
    high = jnp.where(first, other, mine)
    return jnp.concatenate([low, high], axis=1)[:, : x.shape[0]]


def dense_kernel(n_iter, tile, beta_lane, n_parts, mine_ref, other_ref, rowmask_ref, out_ref, unit_t, unit_s, scale_s, aff_s, state_s):
    feat, files = unit_t.shape
    half = files // 2
    runs = half // tile
    for k, ref in enumerate((mine_ref, other_ref)):
        values = ref[:, 0:feat].astype(jnp.float32)
        unit = (
            values * lax.rsqrt(jnp.mean(values * values, axis=1, keepdims=True) + 1e-06)
        ).astype(jnp.bfloat16)
        unit_s[k * half : (k + 1) * half, :] = unit
        unit_t[:, k * half : (k + 1) * half] = unit.astype(jnp.float32).T.astype(jnp.bfloat16)
        scale_s[k * half : (k + 1) * half, :] = (
            ref[:, beta_lane : beta_lane + 1].astype(jnp.float32) / feat
        )
    per_tile = rowmask_ref.shape[1]
    run = tile // per_tile
    col_pos = lax.broadcasted_iota(jnp.int32, (tile, files), 1)
    row_pos = lax.broadcasted_iota(jnp.int32, (tile, files), 0)

    def step(t, colsum):
        p0 = pl.multiple_of(t * tile, tile)
        gram = jnp.dot(unit_s[pl.ds(p0, tile), :], unit_t[...], preferred_element_type=jnp.float32)
        scores = gram * scale_s[pl.ds(p0, tile), :]
        runs_here = rowmask_ref[t % runs]
        block_row = jnp.broadcast_to(runs_here[:, None, :], (per_tile, run, files)).reshape(tile, files)
        ok = (block_row > 0.0) & (row_pos + p0 != col_pos)
        masked = jnp.where(ok, scores, -1e30)
        top = jnp.max(masked, axis=1, keepdims=True)
        e = jnp.exp(masked - top)
        mass = jnp.sum(e, axis=1, keepdims=True)
        weights = e * (1.0 / mass)
        aff_s[pl.ds(p0, tile), :] = weights.astype(jnp.bfloat16)
        return colsum + jnp.sum(weights, axis=0, keepdims=True)

    colsum = lax.fori_loop(0, files // tile, step, jnp.zeros((1, files), jnp.float32))
    inv_root = lax.rsqrt((1.0 + colsum) * 0.5)
    n_probe = out_ref.shape[1]
    state = jnp.concatenate(
        [
            sum(
                ref[:, feat + k * n_probe : feat + (k + 1) * n_probe].astype(jnp.float32)
                for k in range(n_parts)
            ).T
            for ref in (mine_ref, other_ref)
        ],
        axis=1,
    )
    for sweep in range(n_iter):
        scaled_f = (state * inv_root).astype(jnp.bfloat16).astype(jnp.float32)
        scaled = scaled_f.astype(jnp.bfloat16)
        row_t = jnp.dot(aff_s[...], scaled_f.T.astype(jnp.bfloat16), preferred_element_type=jnp.float32)
        col_part = jnp.dot(scaled, aff_s[...], preferred_element_type=jnp.float32)
        if sweep + 1 < n_iter:
            state = (row_t.T + col_part) * (0.5 * inv_root)
        else:
            state_s[...] = (row_t + col_part.T) * (0.5 * inv_root).T
    shard = out_ref.shape[0]
    half_s = shard // 2
    core = lax.axis_index("row") % 2
    me = lax.axis_index("row") * lax.axis_size("col") + lax.axis_index("col")
    for k, h in enumerate((core, 1 - core)):
        start = pl.multiple_of(h * half + me * half_s, half_s)
        out_ref[k * half_s : (k + 1) * half_s, :] = state_s[pl.ds(start, half_s), :]


def dense_call(mine, other, rowmask, n_probe, shard, feat, beta_lane):
    files = 2 * mine.shape[0]
    run = files // (2 * rowmask.shape[0])
    tile = run
    while tile * 2 <= min(512, files // 2) and (files // 2) % (tile * 2) == 0:
        tile *= 2
    rowmask = rowmask.reshape(-1, tile // run, files)
    vmem = pl.BlockSpec(memory_space=pltpu.VMEM)
    return pl.pallas_call(
        lambda *refs: dense_kernel(ITERS, tile, beta_lane, PROBE_PARTS, *refs),
        out_shape=jax.ShapeDtypeStruct((shard, n_probe), jnp.float32),
        in_specs=[vmem, vmem, vmem],
        out_specs=vmem,
        scratch_shapes=[
            pltpu.VMEM((feat, files), jnp.bfloat16),
            pltpu.VMEM((files, feat), jnp.bfloat16),
            pltpu.VMEM((files, 1), jnp.float32),
            pltpu.VMEM((files, files), jnp.bfloat16),
            pltpu.VMEM((files, n_probe), jnp.float32),
        ],
        cost_estimate=pl.CostEstimate(
            flops=2 * files * files * feat + 4 * ITERS * files * files * n_probe,
            transcendentals=files * files,
            bytes_accessed=files * mine.shape[1] * 2 + 4 * files * n_probe,
        ),
    )(mine, other, rowmask)


def dense_path(embed, beta, block_mask, counts, probes, n_dev, n_row, me):
    shard, feat = embed.shape
    files = shard * n_dev
    half_s = shard // 2
    half_f = files // 2
    nb = block_mask.shape[1]
    blk = files // nb
    local_blocks = block_mask.shape[0]
    n_probe = probes.shape[0]
    per_row = n_dev // n_row
    mask_flat = block_mask.reshape(-1).astype(jnp.bfloat16)
    mask_cols = -(-mask_flat.shape[0] // half_s)
    mask_part = jnp.pad(mask_flat, (0, half_s * mask_cols - mask_flat.shape[0]))
    mask_part = jnp.tile(mask_part.reshape(half_s, mask_cols), (2, 1))
    used = PROBE_PARTS * n_probe + 1 + mask_cols
    lanes = -(-used // 128) * 128
    extras = jnp.concatenate(
        [
            split3(probes)[:PROBE_PARTS].astype(jnp.float32).reshape(PROBE_PARTS * n_probe, shard),
            beta[None, :].astype(jnp.float32),
            mask_part.T.astype(jnp.float32),
        ],
        axis=0,
    )
    payload = jnp.concatenate(
        [embed, jnp.pad(extras.T.astype(jnp.bfloat16), ((0, 0), (0, lanes - used)))], axis=1
    )
    width = payload.shape[1]
    halves = payload.reshape(2, half_s, width)
    wide = jnp.broadcast_to(
        halves[None, :, None], (n_row // 2, 2, per_row, half_s, width)
    ).reshape(n_dev, half_s, width)
    mine = lax.all_to_all(wide, AXES, 0, 0, tiled=True)
    other = lax.ppermute(mine, "row", [(r, r ^ 1) for r in range(n_row)])
    core = lax.axis_index("row") % 2
    pos = lax.iota(jnp.int32, files)
    run = blk // 2
    in_run = lax.iota(jnp.int32, files) % run
    run_dev = in_run // half_s
    half_of = jnp.broadcast_to((lax.iota(jnp.int32, 2) ^ core)[:, None, None], (2, nb, run))
    in_block = (run_dev % (blk // shard)) * shard + half_of.reshape(files) * half_s + in_run % half_s
    block_counts = jnp.broadcast_to(counts[None, :, None], (2, nb, run)).reshape(files)
    live = in_block < block_counts
    mine2 = mine.reshape(half_f, width)
    other2 = other.reshape(half_f, width)
    mask_got = mine[:, :, feat + PROBE_PARTS * n_probe + 1 : feat + used].reshape(n_dev, -1)
    mask_got = mask_got[:, : local_blocks * nb]
    mask_full = mask_got.reshape(n_row, per_row, local_blocks, nb)[:, 0].reshape(nb, nb)
    block_ok = jnp.broadcast_to((mask_full == 1)[:, None, :, None], (nb, 2, nb, run))
    rowmask = jnp.where(block_ok.reshape(nb, files) & live[None, :], 1.0, 0.0).astype(jnp.float32)
    own_t = dense_call(mine2, other2, rowmask, n_probe, shard, feat, feat + PROBE_PARTS * n_probe)
    return own_t.T


def normalize(embed):
    values = embed.astype(jnp.float32)
    return (values * lax.rsqrt(jnp.mean(values * values, axis=1, keepdims=True) + 1e-06)).astype(
        jnp.bfloat16
    )


def split3(x):
    hi = lax.reduce_precision(x, exponent_bits=8, mantissa_bits=7)
    rest = x - hi
    mid = lax.reduce_precision(rest, exponent_bits=8, mantissa_bits=7)
    lo = rest - mid
    return jnp.stack([hi, mid, lo]).astype(jnp.bfloat16)


def join3(parts):
    parts = parts.astype(jnp.float32)
    if parts.shape[0] == 1:
        return parts[0]
    return (parts[0] + parts[1]) + parts[2]


def pack_rows(flat, width):
    rows = -(-flat.shape[0] // width)
    return jnp.pad(flat, (0, rows * width - flat.shape[0])).reshape(rows, width), rows


def body(embed, beta, block_mask, counts, probes):
    n_dev = lax.axis_size("row") * lax.axis_size("col")
    n_row = lax.axis_size("row")
    me = lax.axis_index(AXES)
    shard, feat = embed.shape
    files = shard * n_dev
    nb = block_mask.shape[1]
    blk = files // nb
    local_blocks = block_mask.shape[0]

    unit_own = normalize(embed)
    beta_rows, beta_n = pack_rows(beta, feat)
    mask_rows, mask_n = pack_rows(block_mask.reshape(-1).astype(jnp.bfloat16), feat)
    replicate = files * files <= REPLICATE_CELLS
    n_probe = probes.shape[0]
    if (
        replicate
        and n_row % 2 == 0
        and shard % 2 == 0
        and blk % shard == 0
        and (blk // 2) % 8 == 0
        and files % 128 == 0
    ):
        return dense_path(embed, beta, block_mask, counts, probes, n_dev, n_row, me)
    if replicate:
        mask_flat = block_mask.reshape(-1).astype(jnp.bfloat16)
        mask_cols = -(-mask_flat.shape[0] // shard)
        mask_part = jnp.pad(mask_flat, (0, shard * mask_cols - mask_flat.shape[0]))
        used = 3 * n_probe + 1 + mask_cols
        lanes = -(-used // 128) * 128
        extra_cols = jnp.concatenate(
            [
                jnp.moveaxis(split3(probes.T), 0, 1).reshape(shard, 3 * n_probe),
                beta[:, None],
                mask_part.reshape(shard, mask_cols),
                jnp.zeros((shard, lanes - used), jnp.bfloat16),
            ],
            axis=1,
        )
        got = gather_halves(jnp.concatenate([unit_own, extra_cols], axis=1), n_dev, n_row)
        unit_all = got[:, :, :feat].reshape(files, feat)
        tail = got[:, :, feat:].reshape(files, lanes)
        probes_t = join3(
            jnp.stack([tail[:, k * n_probe : (k + 1) * n_probe] for k in range(3)])
        )
        beta_all = tail[:, 3 * n_probe]
        mask_got = got[:, :, feat + 3 * n_probe + 1 : feat + used].reshape(n_dev, -1)
        mask_got = mask_got[:, : local_blocks * nb]
    else:
        unit_all = gather_rows(unit_own, n_dev).reshape(files, feat)
        extra = gather_rows(jnp.concatenate([beta_rows, mask_rows], axis=0), n_dev)
        beta_all = extra[:, 0, :shard].reshape(files)
        mask_got = extra[:, beta_n:, :].reshape(n_dev, -1)[:, : local_blocks * nb]
    per_row = n_dev // n_row
    mask_full = (
        mask_got.reshape(n_row, per_row, local_blocks, nb)[:, 0].reshape(nb, nb).astype(jnp.int32)
    )
    scale_all = beta_all.astype(jnp.float32) / feat

    col_ids = lax.iota(jnp.int32, files)
    col_block = col_ids // blk
    in_block = lax.iota(jnp.int32, blk)
    col_live = (in_block[None, :] < counts[:, None]).reshape(files)

    if replicate:
        gram = lax.dot_general(
            unit_all, unit_all, (((1,), (1,)), ((), ())), preferred_element_type=jnp.float32
        )
        scores = gram * scale_all[:, None]
        block_ok = jnp.broadcast_to(
            (mask_full == 1)[:, None, :, None], (nb, blk, nb, blk)
        ).reshape(files, files)
        allowed = block_ok & col_live[None, :] & (col_ids[:, None] != col_ids[None, :])
        masked = jnp.where(allowed, scores, -1e30)
        row_top = jnp.max(masked, axis=1)
        row_mass = jnp.sum(jnp.where(allowed, jnp.exp(masked - row_top[:, None]), 0.0), axis=1)
        weights = jnp.where(allowed, jnp.exp(masked - row_top[:, None]) / row_mass[:, None], 0.0)
        col_mass = jnp.sum(weights, axis=0)
        inv_root = lax.rsqrt((1.0 + col_mass) * 0.5)
        affinity = weights.astype(jnp.bfloat16)
        state = probes_t
        for sweep in range(ITERS):
            scaled = (state * inv_root[:, None]).astype(jnp.bfloat16)
            row_part = jnp.dot(affinity, scaled, preferred_element_type=jnp.float32)
            col_part = lax.dot_general(
                affinity, scaled, (((0,), (0,)), ((), ())), preferred_element_type=jnp.float32
            )
            state = (row_part + col_part) * (0.5 * inv_root)[:, None]
        return lax.dynamic_slice_in_dim(state, me * shard, shard, 0).T

    own_ids = me * shard + lax.iota(jnp.int32, shard)
    own_block = own_ids // blk
    gram = lax.dot_general(
        unit_own, unit_all, (((1,), (1,)), ((), ())), preferred_element_type=jnp.float32
    )
    own_scale = lax.dynamic_slice_in_dim(scale_all, me * shard, shard, 0)
    scores = gram * own_scale[:, None]
    row_ok = jnp.take(jnp.take(mask_full, own_block, axis=0), col_block, axis=1) == 1
    allowed = row_ok & col_live[None, :] & (own_ids[:, None] != col_ids[None, :])
    masked = jnp.where(allowed, scores, -1e30)
    row_top = jnp.max(masked, axis=1)
    row_mass = jnp.sum(jnp.where(allowed, jnp.exp(masked - row_top[:, None]), 0.0), axis=1)
    weights = jnp.where(allowed, jnp.exp(masked - row_top[:, None]) / row_mass[:, None], 0.0)
    stats = gather_rows(jnp.stack([row_top, row_mass], axis=1), n_dev).reshape(files, 2)
    top_all, mass_all = stats[:, 0], stats[:, 1]
    scores_t = gram * scale_all[None, :]
    own_live = jnp.take(col_live, own_ids, axis=0)
    col_ok = jnp.take(jnp.take(mask_full, col_block, axis=0), own_block, axis=1).T == 1
    allowed_t = col_ok & own_live[:, None] & (own_ids[:, None] != col_ids[None, :])
    masked_t = jnp.where(allowed_t, scores_t, -1e30)
    weights_t = jnp.where(
        allowed_t, jnp.exp(masked_t - top_all[None, :]) / mass_all[None, :], 0.0
    )
    col_mass = jnp.sum(weights_t, axis=1)
    inv_root = lax.rsqrt((1.0 + col_mass) * 0.5)
    aff_rows = weights.astype(jnp.bfloat16)
    aff_cols = weights_t.astype(jnp.bfloat16)
    state = probes
    for sweep in range(ITERS):
        scaled = (state * inv_root[None, :]).astype(jnp.bfloat16)
        scaled_all = gather_rows(scaled.T, n_dev).reshape(files, probes.shape[0])
        row_part = jnp.dot(aff_rows, scaled_all, preferred_element_type=jnp.float32)
        col_part = jnp.dot(aff_cols, scaled_all, preferred_element_type=jnp.float32)
        state = ((row_part + col_part) * (0.5 * inv_root)[:, None]).T
    return state


def solution(mesh):
    placed = (
        P(AXES, None),
        P(AXES),
        P("row", None),
        P(),
        P(None, AXES),
    )
    return jax.shard_map(body, mesh=mesh, in_specs=placed, out_specs=P(None, AXES), check_vma=False)
```

```python
import jax
import jax.numpy as jnp
from jax import lax
from jax.experimental import pallas as pl
from jax.experimental.pallas import tpu as pltpu
from jax.sharding import PartitionSpec as P

ITERS = 2
PROBE_PARTS = 1
AXES = ("row", "col")
A2A_BYTES = 8 << 20
REPLICATE_CELLS = 1 << 21


def gather_rows(x, n_dev):
    if n_dev * x.size * x.dtype.itemsize <= A2A_BYTES:
        wide = jnp.broadcast_to(x[None], (n_dev,) + x.shape)
        return lax.all_to_all(wide, AXES, 0, 0, tiled=True)
    return lax.all_gather(x, AXES, axis=0, tiled=False)


def gather_halves(x, n_dev, n_row):
    if n_row % 2:
        return gather_rows(x, n_dev)
    rows = x.shape[0] + x.shape[0] % 2
    halves = jnp.pad(x, ((0, rows - x.shape[0]), (0, 0))).reshape(2, rows // 2, x.shape[1])
    per_row = n_dev // n_row
    wide = jnp.broadcast_to(
        halves[None, :, None], (n_row // 2, 2, per_row, rows // 2, x.shape[1])
    ).reshape(n_dev, rows // 2, x.shape[1])
    mine = lax.all_to_all(wide, AXES, 0, 0, tiled=True)
    other = lax.ppermute(mine, "row", [(r, r ^ 1) for r in range(n_row)])
    first = lax.axis_index("row") % 2 == 0
    low = jnp.where(first, mine, other)
    high = jnp.where(first, other, mine)
    return jnp.concatenate([low, high], axis=1)[:, : x.shape[0]]


def dense_kernel(n_iter, tile, beta_lane, n_parts, mine_ref, other_ref, rowmask_ref, out_ref, unit_t, unit_s, scale_s, aff_s, state_s):
    feat, files = unit_t.shape
    half = files // 2
    runs = half // tile
    for k, ref in enumerate((mine_ref, other_ref)):
        values = ref[:, 0:feat].astype(jnp.float32)
        unit = (
            values * lax.rsqrt(jnp.mean(values * values, axis=1, keepdims=True) + 1e-06)
        ).astype(jnp.bfloat16)
        unit_s[k * half : (k + 1) * half, :] = unit
        unit_t[:, k * half : (k + 1) * half] = unit.astype(jnp.float32).T.astype(jnp.bfloat16)
        scale_s[k * half : (k + 1) * half, :] = (
            ref[:, beta_lane : beta_lane + 1].astype(jnp.float32) / feat
        )
    per_tile = rowmask_ref.shape[1]
    run = tile // per_tile
    col_pos = lax.broadcasted_iota(jnp.int32, (tile, files), 1)
    row_pos = lax.broadcasted_iota(jnp.int32, (tile, files), 0)

    def step(t, colsum):
        p0 = pl.multiple_of(t * tile, tile)
        gram = jnp.dot(unit_s[pl.ds(p0, tile), :], unit_t[...], preferred_element_type=jnp.float32)
        scores = gram * scale_s[pl.ds(p0, tile), :]
        runs_here = rowmask_ref[t % runs]
        block_row = jnp.broadcast_to(runs_here[:, None, :], (per_tile, run, files)).reshape(tile, files)
        ok = (block_row > 0.0) & (row_pos + p0 != col_pos)
        masked = jnp.where(ok, scores, -1e30)
        top = jnp.max(masked, axis=1, keepdims=True)
        e = jnp.exp(masked - top)
        mass = jnp.sum(e, axis=1, keepdims=True)
        weights = e * (1.0 / mass)
        aff_s[pl.ds(p0, tile), :] = weights.astype(jnp.bfloat16)
        return colsum + jnp.sum(weights, axis=0, keepdims=True)

    colsum = lax.fori_loop(0, files // tile, step, jnp.zeros((1, files), jnp.float32))
    inv_root = lax.rsqrt((1.0 + colsum) * 0.5)
    n_probe = out_ref.shape[1]
    state = jnp.concatenate(
        [
            sum(
                ref[:, feat + k * n_probe : feat + (k + 1) * n_probe].astype(jnp.float32)
                for k in range(n_parts)
            ).T
            for ref in (mine_ref, other_ref)
        ],
        axis=1,
    )
    for sweep in range(n_iter):
        scaled_f = (state * inv_root).astype(jnp.bfloat16).astype(jnp.float32)
        scaled = scaled_f.astype(jnp.bfloat16)
        row_t = jnp.dot(aff_s[...], scaled_f.T.astype(jnp.bfloat16), preferred_element_type=jnp.float32)
        col_part = jnp.dot(scaled, aff_s[...], preferred_element_type=jnp.float32)
        if sweep + 1 < n_iter:
            state = (row_t.T + col_part) * (0.5 * inv_root)
        else:
            state_s[...] = (row_t + col_part.T) * (0.5 * inv_root).T
    shard = out_ref.shape[0]
    half_s = shard // 2
    core = lax.axis_index("row") % 2
    me = lax.axis_index("row") * lax.axis_size("col") + lax.axis_index("col")
    for k, h in enumerate((core, 1 - core)):
        start = pl.multiple_of(h * half + me * half_s, half_s)
        out_ref[k * half_s : (k + 1) * half_s, :] = state_s[pl.ds(start, half_s), :]


def dense_call(mine, other, rowmask, n_probe, shard, feat, beta_lane):
    files = 2 * mine.shape[0]
    run = files // (2 * rowmask.shape[0])
    tile = run
    while tile * 2 <= min(512, files // 2) and (files // 2) % (tile * 2) == 0:
        tile *= 2
    rowmask = rowmask.reshape(-1, tile // run, files)
    vmem = pl.BlockSpec(memory_space=pltpu.VMEM)
    return pl.pallas_call(
        lambda *refs: dense_kernel(ITERS, tile, beta_lane, PROBE_PARTS, *refs),
        out_shape=jax.ShapeDtypeStruct((shard, n_probe), jnp.float32),
        in_specs=[vmem, vmem, vmem],
        out_specs=vmem,
        scratch_shapes=[
            pltpu.VMEM((feat, files), jnp.bfloat16),
            pltpu.VMEM((files, feat), jnp.bfloat16),
            pltpu.VMEM((files, 1), jnp.float32),
            pltpu.VMEM((files, files), jnp.bfloat16),
            pltpu.VMEM((files, n_probe), jnp.float32),
        ],
        cost_estimate=pl.CostEstimate(
            flops=2 * files * files * feat + 4 * ITERS * files * files * n_probe,
            transcendentals=files * files,
            bytes_accessed=files * mine.shape[1] * 2 + 4 * files * n_probe,
        ),
    )(mine, other, rowmask)


def dense_path(embed, beta, block_mask, counts, probes, n_dev, n_row, me):
    shard, feat = embed.shape
    files = shard * n_dev
    half_s = shard // 2
    half_f = files // 2
    nb = block_mask.shape[1]
    blk = files // nb
    local_blocks = block_mask.shape[0]
    n_probe = probes.shape[0]
    per_row = n_dev // n_row
    mask_flat = block_mask.reshape(-1).astype(jnp.float32)
    mask_cols = -(-mask_flat.shape[0] // half_s)
    mask_part = jnp.pad(mask_flat, (0, half_s * mask_cols - mask_flat.shape[0]))
    mask_part = jnp.tile(mask_part.reshape(half_s, mask_cols), (2, 1))
    used = PROBE_PARTS * n_probe + 1 + mask_cols
    lanes = -(-used // 128) * 128
    extras = jnp.concatenate(
        [
            split3(probes)[:PROBE_PARTS].astype(jnp.float32).reshape(PROBE_PARTS * n_probe, shard),
            beta[None, :].astype(jnp.float32),
            mask_part.T,
        ],
        axis=0,
    )
    payload = jnp.concatenate(
        [embed, jnp.pad(extras.T.astype(jnp.bfloat16), ((0, 0), (0, lanes - used)))], axis=1
    )
    width = payload.shape[1]
    halves = payload.reshape(2, half_s, width)
    wide = jnp.broadcast_to(
        halves[None, :, None], (n_row // 2, 2, per_row, half_s, width)
    ).reshape(n_dev, half_s, width)
    mine = lax.all_to_all(wide, AXES, 0, 0, tiled=True)
    other = lax.ppermute(mine, "row", [(r, r ^ 1) for r in range(n_row)])
    core = lax.axis_index("row") % 2
    pos = lax.iota(jnp.int32, files)
    run = blk // 2
    in_run = lax.iota(jnp.int32, files) % run
    run_dev = in_run // half_s
    half_of = jnp.broadcast_to((lax.iota(jnp.int32, 2) ^ core)[:, None, None], (2, nb, run))
    in_block = (run_dev % (blk // shard)) * shard + half_of.reshape(files) * half_s + in_run % half_s
    block_counts = jnp.broadcast_to(counts[None, :, None], (2, nb, run)).reshape(files)
    live = in_block < block_counts
    mine2 = mine.reshape(half_f, width)
    other2 = other.reshape(half_f, width)
    mask_got = mine[:, :, feat + PROBE_PARTS * n_probe + 1 : feat + used].reshape(n_dev, -1)
    mask_got = mask_got[:, : local_blocks * nb]
    mask_full = mask_got.reshape(n_row, per_row, local_blocks, nb)[:, 0].reshape(nb, nb)
    block_ok = jnp.broadcast_to((mask_full == 1)[:, None, :, None], (nb, 2, nb, run))
    rowmask = jnp.where(block_ok.reshape(nb, files) & live[None, :], 1.0, 0.0).astype(jnp.float32)
    own_t = dense_call(mine2, other2, rowmask, n_probe, shard, feat, feat + PROBE_PARTS * n_probe)
    return own_t.T


def normalize(embed):
    values = embed.astype(jnp.float32)
    return (values * lax.rsqrt(jnp.mean(values * values, axis=1, keepdims=True) + 1e-06)).astype(
        jnp.bfloat16
    )


def split3(x):
    hi = lax.reduce_precision(x, exponent_bits=8, mantissa_bits=7)
    rest = x - hi
    mid = lax.reduce_precision(rest, exponent_bits=8, mantissa_bits=7)
    lo = rest - mid
    return jnp.stack([hi, mid, lo]).astype(jnp.bfloat16)


def join3(parts):
    parts = parts.astype(jnp.float32)
    if parts.shape[0] == 1:
        return parts[0]
    return (parts[0] + parts[1]) + parts[2]


def pack_rows(flat, width):
    rows = -(-flat.shape[0] // width)
    return jnp.pad(flat, (0, rows * width - flat.shape[0])).reshape(rows, width), rows


def body(embed, beta, block_mask, counts, probes):
    n_dev = lax.axis_size("row") * lax.axis_size("col")
    n_row = lax.axis_size("row")
    me = lax.axis_index(AXES)
    shard, feat = embed.shape
    files = shard * n_dev
    nb = block_mask.shape[1]
    blk = files // nb
    local_blocks = block_mask.shape[0]

    unit_own = normalize(embed)
    beta_rows, beta_n = pack_rows(beta, feat)
    mask_rows, mask_n = pack_rows(block_mask.reshape(-1).astype(jnp.bfloat16), feat)
    replicate = files * files <= REPLICATE_CELLS
    n_probe = probes.shape[0]
    if (
        replicate
        and n_row % 2 == 0
        and shard % 2 == 0
        and blk % shard == 0
        and (blk // 2) % 8 == 0
        and files % 128 == 0
    ):
        return dense_path(embed, beta, block_mask, counts, probes, n_dev, n_row, me)
    if replicate:
        mask_flat = block_mask.reshape(-1).astype(jnp.bfloat16)
        mask_cols = -(-mask_flat.shape[0] // shard)
        mask_part = jnp.pad(mask_flat, (0, shard * mask_cols - mask_flat.shape[0]))
        used = 3 * n_probe + 1 + mask_cols
        lanes = -(-used // 128) * 128
        extra_cols = jnp.concatenate(
            [
                jnp.moveaxis(split3(probes.T), 0, 1).reshape(shard, 3 * n_probe),
                beta[:, None],
                mask_part.reshape(shard, mask_cols),
                jnp.zeros((shard, lanes - used), jnp.bfloat16),
            ],
            axis=1,
        )
        got = gather_halves(jnp.concatenate([unit_own, extra_cols], axis=1), n_dev, n_row)
        unit_all = got[:, :, :feat].reshape(files, feat)
        tail = got[:, :, feat:].reshape(files, lanes)
        probes_t = join3(
            jnp.stack([tail[:, k * n_probe : (k + 1) * n_probe] for k in range(3)])
        )
        beta_all = tail[:, 3 * n_probe]
        mask_got = got[:, :, feat + 3 * n_probe + 1 : feat + used].reshape(n_dev, -1)
        mask_got = mask_got[:, : local_blocks * nb]
    else:
        unit_all = gather_rows(unit_own, n_dev).reshape(files, feat)
        extra = gather_rows(jnp.concatenate([beta_rows, mask_rows], axis=0), n_dev)
        beta_all = extra[:, 0, :shard].reshape(files)
        mask_got = extra[:, beta_n:, :].reshape(n_dev, -1)[:, : local_blocks * nb]
    per_row = n_dev // n_row
    mask_full = (
        mask_got.reshape(n_row, per_row, local_blocks, nb)[:, 0].reshape(nb, nb).astype(jnp.int32)
    )
    scale_all = beta_all.astype(jnp.float32) / feat

    col_ids = lax.iota(jnp.int32, files)
    col_block = col_ids // blk
    in_block = lax.iota(jnp.int32, blk)
    col_live = (in_block[None, :] < counts[:, None]).reshape(files)

    if replicate:
        gram = lax.dot_general(
            unit_all, unit_all, (((1,), (1,)), ((), ())), preferred_element_type=jnp.float32
        )
        scores = gram * scale_all[:, None]
        block_ok = jnp.broadcast_to(
            (mask_full == 1)[:, None, :, None], (nb, blk, nb, blk)
        ).reshape(files, files)
        allowed = block_ok & col_live[None, :] & (col_ids[:, None] != col_ids[None, :])
        masked = jnp.where(allowed, scores, -1e30)
        row_top = jnp.max(masked, axis=1)
        row_mass = jnp.sum(jnp.where(allowed, jnp.exp(masked - row_top[:, None]), 0.0), axis=1)
        weights = jnp.where(allowed, jnp.exp(masked - row_top[:, None]) / row_mass[:, None], 0.0)
        col_mass = jnp.sum(weights, axis=0)
        inv_root = lax.rsqrt((1.0 + col_mass) * 0.5)
        affinity = weights.astype(jnp.bfloat16)
        state = probes_t
        for sweep in range(ITERS):
            scaled = (state * inv_root[:, None]).astype(jnp.bfloat16)
            row_part = jnp.dot(affinity, scaled, preferred_element_type=jnp.float32)
            col_part = lax.dot_general(
                affinity, scaled, (((0,), (0,)), ((), ())), preferred_element_type=jnp.float32
            )
            state = (row_part + col_part) * (0.5 * inv_root)[:, None]
        return lax.dynamic_slice_in_dim(state, me * shard, shard, 0).T

    own_ids = me * shard + lax.iota(jnp.int32, shard)
    own_block = own_ids // blk
    gram = lax.dot_general(
        unit_own, unit_all, (((1,), (1,)), ((), ())), preferred_element_type=jnp.float32
    )
    own_scale = lax.dynamic_slice_in_dim(scale_all, me * shard, shard, 0)
    scores = gram * own_scale[:, None]
    row_ok = jnp.take(jnp.take(mask_full, own_block, axis=0), col_block, axis=1) == 1
    allowed = row_ok & col_live[None, :] & (own_ids[:, None] != col_ids[None, :])
    masked = jnp.where(allowed, scores, -1e30)
    row_top = jnp.max(masked, axis=1)
    row_mass = jnp.sum(jnp.where(allowed, jnp.exp(masked - row_top[:, None]), 0.0), axis=1)
    weights = jnp.where(allowed, jnp.exp(masked - row_top[:, None]) / row_mass[:, None], 0.0)
    stats = gather_rows(jnp.stack([row_top, row_mass], axis=1), n_dev).reshape(files, 2)
    top_all, mass_all = stats[:, 0], stats[:, 1]
    scores_t = gram * scale_all[None, :]
    own_live = jnp.take(col_live, own_ids, axis=0)
    col_ok = jnp.take(jnp.take(mask_full, col_block, axis=0), own_block, axis=1).T == 1
    allowed_t = col_ok & own_live[:, None] & (own_ids[:, None] != col_ids[None, :])
    masked_t = jnp.where(allowed_t, scores_t, -1e30)
    weights_t = jnp.where(
        allowed_t, jnp.exp(masked_t - top_all[None, :]) / mass_all[None, :], 0.0
    )
    col_mass = jnp.sum(weights_t, axis=1)
    inv_root = lax.rsqrt((1.0 + col_mass) * 0.5)
    aff_rows = weights.astype(jnp.bfloat16)
    aff_cols = weights_t.astype(jnp.bfloat16)
    state = probes
    for sweep in range(ITERS):
        scaled = (state * inv_root[None, :]).astype(jnp.bfloat16)
        scaled_all = gather_rows(scaled.T, n_dev).reshape(files, probes.shape[0])
        row_part = jnp.dot(aff_rows, scaled_all, preferred_element_type=jnp.float32)
        col_part = jnp.dot(aff_cols, scaled_all, preferred_element_type=jnp.float32)
        state = ((row_part + col_part) * (0.5 * inv_root)[:, None]).T
    return state


def solution(mesh):
    placed = (
        P(AXES, None),
        P(AXES),
        P("row", None),
        P(),
        P(None, AXES),
    )
    return jax.shard_map(body, mesh=mesh, in_specs=placed, out_specs=P(None, AXES), check_vma=False)
```

```python
import jax
import jax.numpy as jnp
from jax import lax
from jax.experimental import pallas as pl
from jax.experimental.pallas import tpu as pltpu
from jax.sharding import PartitionSpec as P

ITERS = 2
PROBE_PARTS = 1
AXES = ("row", "col")
A2A_BYTES = 8 << 20
REPLICATE_CELLS = 1 << 21


def gather_rows(x, n_dev):
    if n_dev * x.size * x.dtype.itemsize <= A2A_BYTES:
        wide = jnp.broadcast_to(x[None], (n_dev,) + x.shape)
        return lax.all_to_all(wide, AXES, 0, 0, tiled=True)
    return lax.all_gather(x, AXES, axis=0, tiled=False)


def gather_halves(x, n_dev, n_row):
    if n_row % 2:
        return gather_rows(x, n_dev)
    rows = x.shape[0] + x.shape[0] % 2
    halves = jnp.pad(x, ((0, rows - x.shape[0]), (0, 0))).reshape(2, rows // 2, x.shape[1])
    per_row = n_dev // n_row
    wide = jnp.broadcast_to(
        halves[None, :, None], (n_row // 2, 2, per_row, rows // 2, x.shape[1])
    ).reshape(n_dev, rows // 2, x.shape[1])
    mine = lax.all_to_all(wide, AXES, 0, 0, tiled=True)
    other = lax.ppermute(mine, "row", [(r, r ^ 1) for r in range(n_row)])
    first = lax.axis_index("row") % 2 == 0
    low = jnp.where(first, mine, other)
    high = jnp.where(first, other, mine)
    return jnp.concatenate([low, high], axis=1)[:, : x.shape[0]]


def dense_kernel(n_iter, tile, beta_lane, n_parts, mine_ref, other_ref, rowmask_ref, out_ref, unit_t, unit_s, scale_s, aff_s, state_s, aff_t):
    feat, files = unit_t.shape
    half = files // 2
    runs = half // tile
    for k, ref in enumerate((mine_ref, other_ref)):
        values = ref[:, 0:feat].astype(jnp.float32)
        unit = (
            values * lax.rsqrt(jnp.mean(values * values, axis=1, keepdims=True) + 1e-06)
        ).astype(jnp.bfloat16)
        unit_s[k * half : (k + 1) * half, :] = unit
        unit_t[:, k * half : (k + 1) * half] = unit.astype(jnp.float32).T.astype(jnp.bfloat16)
        scale_s[k * half : (k + 1) * half, :] = (
            ref[:, beta_lane : beta_lane + 1].astype(jnp.float32) / feat
        )
    per_tile = rowmask_ref.shape[1]
    run = tile // per_tile
    col_pos = lax.broadcasted_iota(jnp.int32, (tile, files), 1)
    row_pos = lax.broadcasted_iota(jnp.int32, (tile, files), 0)

    def step(t, colsum):
        p0 = pl.multiple_of(t * tile, tile)
        gram = jnp.dot(unit_s[pl.ds(p0, tile), :], unit_t[...], preferred_element_type=jnp.float32)
        scores = gram * scale_s[pl.ds(p0, tile), :]
        runs_here = rowmask_ref[t % runs]
        block_row = jnp.broadcast_to(runs_here[:, None, :], (per_tile, run, files)).reshape(tile, files)
        ok = (block_row > 0.0) & (row_pos + p0 != col_pos)
        masked = jnp.where(ok, scores, -1e30)
        top = jnp.max(masked, axis=1, keepdims=True)
        e = jnp.exp(masked - top)
        mass = jnp.sum(e, axis=1, keepdims=True)
        weights = e * (1.0 / mass)
        aff_s[pl.ds(p0, tile), :] = weights.astype(jnp.bfloat16)
        weights_t = weights.T
        aff_t[:, pl.ds(p0, tile)] = weights_t.astype(jnp.bfloat16)
        return colsum + jnp.sum(weights_t, axis=1, keepdims=True)

    colsum = lax.fori_loop(0, files // tile, step, jnp.zeros((files, 1), jnp.float32))
    inv_root = lax.rsqrt((1.0 + colsum) * 0.5)
    n_probe = out_ref.shape[1]
    state = jnp.concatenate(
        [
            sum(
                ref[:, feat + k * n_probe : feat + (k + 1) * n_probe].astype(jnp.float32)
                for k in range(n_parts)
            )
            for ref in (mine_ref, other_ref)
        ],
        axis=0,
    )
    for sweep in range(n_iter):
        scaled = (state * inv_root).astype(jnp.bfloat16)
        row_part = jnp.dot(aff_s[...], scaled, preferred_element_type=jnp.float32)
        col_part = jnp.dot(aff_t[...], scaled, preferred_element_type=jnp.float32)
        state = (row_part + col_part) * (0.5 * inv_root)
    state_s[...] = state
    shard = out_ref.shape[0]
    half_s = shard // 2
    core = lax.axis_index("row") % 2
    me = lax.axis_index("row") * lax.axis_size("col") + lax.axis_index("col")
    for k, h in enumerate((core, 1 - core)):
        start = pl.multiple_of(h * half + me * half_s, half_s)
        out_ref[k * half_s : (k + 1) * half_s, :] = state_s[pl.ds(start, half_s), :]


def dense_call(mine, other, rowmask, n_probe, shard, feat, beta_lane):
    files = 2 * mine.shape[0]
    run = files // (2 * rowmask.shape[0])
    tile = run
    while tile * 2 <= min(512, files // 2) and (files // 2) % (tile * 2) == 0:
        tile *= 2
    rowmask = rowmask.reshape(-1, tile // run, files)
    vmem = pl.BlockSpec(memory_space=pltpu.VMEM)
    return pl.pallas_call(
        lambda *refs: dense_kernel(ITERS, tile, beta_lane, PROBE_PARTS, *refs),
        out_shape=jax.ShapeDtypeStruct((shard, n_probe), jnp.float32),
        in_specs=[vmem, vmem, vmem],
        out_specs=vmem,
        scratch_shapes=[
            pltpu.VMEM((feat, files), jnp.bfloat16),
            pltpu.VMEM((files, feat), jnp.bfloat16),
            pltpu.VMEM((files, 1), jnp.float32),
            pltpu.VMEM((files, files), jnp.bfloat16),
            pltpu.VMEM((files, n_probe), jnp.float32),
            pltpu.VMEM((files, files), jnp.bfloat16),
        ],
        cost_estimate=pl.CostEstimate(
            flops=2 * files * files * feat + 4 * ITERS * files * files * n_probe,
            transcendentals=files * files,
            bytes_accessed=files * mine.shape[1] * 2 + 4 * files * n_probe,
        ),
    )(mine, other, rowmask)


def dense_path(embed, beta, block_mask, counts, probes, n_dev, n_row, me):
    shard, feat = embed.shape
    files = shard * n_dev
    half_s = shard // 2
    half_f = files // 2
    nb = block_mask.shape[1]
    blk = files // nb
    local_blocks = block_mask.shape[0]
    n_probe = probes.shape[0]
    per_row = n_dev // n_row
    mask_flat = block_mask.reshape(-1).astype(jnp.float32)
    mask_cols = -(-mask_flat.shape[0] // half_s)
    mask_part = jnp.pad(mask_flat, (0, half_s * mask_cols - mask_flat.shape[0]))
    mask_part = jnp.tile(mask_part.reshape(half_s, mask_cols), (2, 1))
    used = PROBE_PARTS * n_probe + 1 + mask_cols
    lanes = -(-used // 128) * 128
    extras = jnp.concatenate(
        [
            split3(probes)[:PROBE_PARTS].astype(jnp.float32).reshape(PROBE_PARTS * n_probe, shard),
            beta[None, :].astype(jnp.float32),
            mask_part.T,
        ],
        axis=0,
    )
    payload = jnp.concatenate(
        [embed, jnp.pad(extras.T.astype(jnp.bfloat16), ((0, 0), (0, lanes - used)))], axis=1
    )
    width = payload.shape[1]
    halves = payload.reshape(2, half_s, width)
    wide = jnp.broadcast_to(
        halves[None, :, None], (n_row // 2, 2, per_row, half_s, width)
    ).reshape(n_dev, half_s, width)
    mine = lax.all_to_all(wide, AXES, 0, 0, tiled=True)
    other = lax.ppermute(mine, "row", [(r, r ^ 1) for r in range(n_row)])
    core = lax.axis_index("row") % 2
    pos = lax.iota(jnp.int32, files)
    run = blk // 2
    in_run = lax.iota(jnp.int32, files) % run
    run_dev = in_run // half_s
    half_of = jnp.broadcast_to((lax.iota(jnp.int32, 2) ^ core)[:, None, None], (2, nb, run))
    in_block = (run_dev % (blk // shard)) * shard + half_of.reshape(files) * half_s + in_run % half_s
    block_counts = jnp.broadcast_to(counts[None, :, None], (2, nb, run)).reshape(files)
    live = in_block < block_counts
    mine2 = mine.reshape(half_f, width)
    other2 = other.reshape(half_f, width)
    mask_got = mine[:, :, feat + PROBE_PARTS * n_probe + 1 : feat + used].reshape(n_dev, -1)
    mask_got = mask_got[:, : local_blocks * nb]
    mask_full = mask_got.reshape(n_row, per_row, local_blocks, nb)[:, 0].reshape(nb, nb)
    block_ok = jnp.broadcast_to((mask_full == 1)[:, None, :, None], (nb, 2, nb, run))
    rowmask = jnp.where(block_ok.reshape(nb, files) & live[None, :], 1.0, 0.0).astype(jnp.float32)
    own_t = dense_call(mine2, other2, rowmask, n_probe, shard, feat, feat + PROBE_PARTS * n_probe)
    return own_t.T


def normalize(embed):
    values = embed.astype(jnp.float32)
    return (values * lax.rsqrt(jnp.mean(values * values, axis=1, keepdims=True) + 1e-06)).astype(
        jnp.bfloat16
    )


def split3(x):
    hi = lax.reduce_precision(x, exponent_bits=8, mantissa_bits=7)
    rest = x - hi
    mid = lax.reduce_precision(rest, exponent_bits=8, mantissa_bits=7)
    lo = rest - mid
    return jnp.stack([hi, mid, lo]).astype(jnp.bfloat16)


def join3(parts):
    parts = parts.astype(jnp.float32)
    if parts.shape[0] == 1:
        return parts[0]
    return (parts[0] + parts[1]) + parts[2]


def pack_rows(flat, width):
    rows = -(-flat.shape[0] // width)
    return jnp.pad(flat, (0, rows * width - flat.shape[0])).reshape(rows, width), rows


def body(embed, beta, block_mask, counts, probes):
    n_dev = lax.axis_size("row") * lax.axis_size("col")
    n_row = lax.axis_size("row")
    me = lax.axis_index(AXES)
    shard, feat = embed.shape
    files = shard * n_dev
    nb = block_mask.shape[1]
    blk = files // nb
    local_blocks = block_mask.shape[0]

    unit_own = normalize(embed)
    beta_rows, beta_n = pack_rows(beta, feat)
    mask_rows, mask_n = pack_rows(block_mask.reshape(-1).astype(jnp.bfloat16), feat)
    replicate = files * files <= REPLICATE_CELLS
    n_probe = probes.shape[0]
    if (
        replicate
        and n_row % 2 == 0
        and shard % 2 == 0
        and blk % shard == 0
        and (blk // 2) % 8 == 0
        and files % 128 == 0
    ):
        return dense_path(embed, beta, block_mask, counts, probes, n_dev, n_row, me)
    if replicate:
        mask_flat = block_mask.reshape(-1).astype(jnp.bfloat16)
        mask_cols = -(-mask_flat.shape[0] // shard)
        mask_part = jnp.pad(mask_flat, (0, shard * mask_cols - mask_flat.shape[0]))
        used = 3 * n_probe + 1 + mask_cols
        lanes = -(-used // 128) * 128
        extra_cols = jnp.concatenate(
            [
                jnp.moveaxis(split3(probes.T), 0, 1).reshape(shard, 3 * n_probe),
                beta[:, None],
                mask_part.reshape(shard, mask_cols),
                jnp.zeros((shard, lanes - used), jnp.bfloat16),
            ],
            axis=1,
        )
        got = gather_halves(jnp.concatenate([unit_own, extra_cols], axis=1), n_dev, n_row)
        unit_all = got[:, :, :feat].reshape(files, feat)
        tail = got[:, :, feat:].reshape(files, lanes)
        probes_t = join3(
            jnp.stack([tail[:, k * n_probe : (k + 1) * n_probe] for k in range(3)])
        )
        beta_all = tail[:, 3 * n_probe]
        mask_got = got[:, :, feat + 3 * n_probe + 1 : feat + used].reshape(n_dev, -1)
        mask_got = mask_got[:, : local_blocks * nb]
    else:
        unit_all = gather_rows(unit_own, n_dev).reshape(files, feat)
        extra = gather_rows(jnp.concatenate([beta_rows, mask_rows], axis=0), n_dev)
        beta_all = extra[:, 0, :shard].reshape(files)
        mask_got = extra[:, beta_n:, :].reshape(n_dev, -1)[:, : local_blocks * nb]
    per_row = n_dev // n_row
    mask_full = (
        mask_got.reshape(n_row, per_row, local_blocks, nb)[:, 0].reshape(nb, nb).astype(jnp.int32)
    )
    scale_all = beta_all.astype(jnp.float32) / feat

    col_ids = lax.iota(jnp.int32, files)
    col_block = col_ids // blk
    in_block = lax.iota(jnp.int32, blk)
    col_live = (in_block[None, :] < counts[:, None]).reshape(files)

    if replicate:
        gram = lax.dot_general(
            unit_all, unit_all, (((1,), (1,)), ((), ())), preferred_element_type=jnp.float32
        )
        scores = gram * scale_all[:, None]
        block_ok = jnp.broadcast_to(
            (mask_full == 1)[:, None, :, None], (nb, blk, nb, blk)
        ).reshape(files, files)
        allowed = block_ok & col_live[None, :] & (col_ids[:, None] != col_ids[None, :])
        masked = jnp.where(allowed, scores, -1e30)
        row_top = jnp.max(masked, axis=1)
        row_mass = jnp.sum(jnp.where(allowed, jnp.exp(masked - row_top[:, None]), 0.0), axis=1)
        weights = jnp.where(allowed, jnp.exp(masked - row_top[:, None]) / row_mass[:, None], 0.0)
        col_mass = jnp.sum(weights, axis=0)
        inv_root = lax.rsqrt((1.0 + col_mass) * 0.5)
        affinity = weights.astype(jnp.bfloat16)
        state = probes_t
        for sweep in range(ITERS):
            scaled = (state * inv_root[:, None]).astype(jnp.bfloat16)
            row_part = jnp.dot(affinity, scaled, preferred_element_type=jnp.float32)
            col_part = lax.dot_general(
                affinity, scaled, (((0,), (0,)), ((), ())), preferred_element_type=jnp.float32
            )
            state = (row_part + col_part) * (0.5 * inv_root)[:, None]
        return lax.dynamic_slice_in_dim(state, me * shard, shard, 0).T

    own_ids = me * shard + lax.iota(jnp.int32, shard)
    own_block = own_ids // blk
    gram = lax.dot_general(
        unit_own, unit_all, (((1,), (1,)), ((), ())), preferred_element_type=jnp.float32
    )
    own_scale = lax.dynamic_slice_in_dim(scale_all, me * shard, shard, 0)
    scores = gram * own_scale[:, None]
    row_ok = jnp.take(jnp.take(mask_full, own_block, axis=0), col_block, axis=1) == 1
    allowed = row_ok & col_live[None, :] & (own_ids[:, None] != col_ids[None, :])
    masked = jnp.where(allowed, scores, -1e30)
    row_top = jnp.max(masked, axis=1)
    row_mass = jnp.sum(jnp.where(allowed, jnp.exp(masked - row_top[:, None]), 0.0), axis=1)
    weights = jnp.where(allowed, jnp.exp(masked - row_top[:, None]) / row_mass[:, None], 0.0)
    stats = gather_rows(jnp.stack([row_top, row_mass], axis=1), n_dev).reshape(files, 2)
    top_all, mass_all = stats[:, 0], stats[:, 1]
    scores_t = gram * scale_all[None, :]
    own_live = jnp.take(col_live, own_ids, axis=0)
    col_ok = jnp.take(jnp.take(mask_full, col_block, axis=0), own_block, axis=1).T == 1
    allowed_t = col_ok & own_live[:, None] & (own_ids[:, None] != col_ids[None, :])
    masked_t = jnp.where(allowed_t, scores_t, -1e30)
    weights_t = jnp.where(
        allowed_t, jnp.exp(masked_t - top_all[None, :]) / mass_all[None, :], 0.0
    )
    col_mass = jnp.sum(weights_t, axis=1)
    inv_root = lax.rsqrt((1.0 + col_mass) * 0.5)
    aff_rows = weights.astype(jnp.bfloat16)
    aff_cols = weights_t.astype(jnp.bfloat16)
    state = probes
    for sweep in range(ITERS):
        scaled = (state * inv_root[None, :]).astype(jnp.bfloat16)
        scaled_all = gather_rows(scaled.T, n_dev).reshape(files, probes.shape[0])
        row_part = jnp.dot(aff_rows, scaled_all, preferred_element_type=jnp.float32)
        col_part = jnp.dot(aff_cols, scaled_all, preferred_element_type=jnp.float32)
        state = ((row_part + col_part) * (0.5 * inv_root)[:, None]).T
    return state


def solution(mesh):
    placed = (
        P(AXES, None),
        P(AXES),
        P("row", None),
        P(),
        P(None, AXES),
    )
    return jax.shard_map(body, mesh=mesh, in_specs=placed, out_specs=P(None, AXES), check_vma=False)
```

```python
import jax
import jax.numpy as jnp
from jax import lax
from jax.experimental import pallas as pl
from jax.experimental.pallas import tpu as pltpu
from jax.sharding import PartitionSpec as P

ITERS = 2
PROBE_PARTS = 1
AXES = ("row", "col")
A2A_BYTES = 8 << 20
REPLICATE_CELLS = 1 << 21


def gather_rows(x, n_dev):
    if n_dev * x.size * x.dtype.itemsize <= A2A_BYTES:
        wide = jnp.broadcast_to(x[None], (n_dev,) + x.shape)
        return lax.all_to_all(wide, AXES, 0, 0, tiled=True)
    return lax.all_gather(x, AXES, axis=0, tiled=False)


def gather_halves(x, n_dev, n_row):
    if n_row % 2:
        return gather_rows(x, n_dev)
    rows = x.shape[0] + x.shape[0] % 2
    halves = jnp.pad(x, ((0, rows - x.shape[0]), (0, 0))).reshape(2, rows // 2, x.shape[1])
    per_row = n_dev // n_row
    wide = jnp.broadcast_to(
        halves[None, :, None], (n_row // 2, 2, per_row, rows // 2, x.shape[1])
    ).reshape(n_dev, rows // 2, x.shape[1])
    mine = lax.all_to_all(wide, AXES, 0, 0, tiled=True)
    other = lax.ppermute(mine, "row", [(r, r ^ 1) for r in range(n_row)])
    first = lax.axis_index("row") % 2 == 0
    low = jnp.where(first, mine, other)
    high = jnp.where(first, other, mine)
    return jnp.concatenate([low, high], axis=1)[:, : x.shape[0]]


def dense_kernel(n_iter, tile, beta_lane, n_parts, mine_ref, other_ref, rowmask_ref, out_ref, unit_t, unit_s, scale_s, aff_s, state_s):
    feat, files = unit_t.shape
    half = files // 2
    runs = half // tile
    for k, ref in enumerate((mine_ref, other_ref)):
        values = ref[:, 0:feat].astype(jnp.float32)
        unit = (
            values * lax.rsqrt(jnp.mean(values * values, axis=1, keepdims=True) + 1e-06)
        ).astype(jnp.bfloat16)
        unit_s[k * half : (k + 1) * half, :] = unit
        unit_t[:, k * half : (k + 1) * half] = unit.T
        scale_s[k * half : (k + 1) * half, :] = (
            ref[:, beta_lane : beta_lane + 1].astype(jnp.float32) / feat
        )
    per_tile = rowmask_ref.shape[1]
    run = tile // per_tile
    col_pos = lax.broadcasted_iota(jnp.int32, (tile, files), 1)
    row_pos = lax.broadcasted_iota(jnp.int32, (tile, files), 0)

    def step(t, colsum):
        p0 = pl.multiple_of(t * tile, tile)
        gram = jnp.dot(unit_s[pl.ds(p0, tile), :], unit_t[...], preferred_element_type=jnp.float32)
        scores = gram * scale_s[pl.ds(p0, tile), :]
        runs_here = rowmask_ref[t % runs]
        block_row = jnp.broadcast_to(runs_here[:, None, :], (per_tile, run, files)).reshape(tile, files)
        ok = (block_row > 0.0) & (row_pos + p0 != col_pos)
        masked = jnp.where(ok, scores, -1e30)
        top = jnp.max(masked, axis=1, keepdims=True)
        e = jnp.exp(masked - top)
        mass = jnp.sum(e, axis=1, keepdims=True)
        weights = e * (1.0 / mass)
        aff_s[pl.ds(p0, tile), :] = weights.astype(jnp.bfloat16)
        return colsum + jnp.sum(weights, axis=0, keepdims=True)

    colsum = lax.fori_loop(0, files // tile, step, jnp.zeros((1, files), jnp.float32))
    inv_root = lax.rsqrt((1.0 + colsum) * 0.5)
    n_probe = out_ref.shape[1]
    state = jnp.concatenate(
        [
            sum(
                ref[:, feat + k * n_probe : feat + (k + 1) * n_probe].astype(jnp.float32)
                for k in range(n_parts)
            ).T
            for ref in (mine_ref, other_ref)
        ],
        axis=1,
    )
    for sweep in range(n_iter):
        scaled_f = (state * inv_root).astype(jnp.bfloat16).astype(jnp.float32)
        scaled = scaled_f.astype(jnp.bfloat16)
        row_t = jnp.dot(aff_s[...], scaled_f.T.astype(jnp.bfloat16), preferred_element_type=jnp.float32)
        col_part = jnp.dot(scaled, aff_s[...], preferred_element_type=jnp.float32)
        if sweep + 1 < n_iter:
            state = (row_t.T + col_part) * (0.5 * inv_root)
        else:
            state_s[...] = (row_t + col_part.T) * (0.5 * inv_root).T
    shard = out_ref.shape[0]
    half_s = shard // 2
    core = lax.axis_index("row") % 2
    me = lax.axis_index("row") * lax.axis_size("col") + lax.axis_index("col")
    for k, h in enumerate((core, 1 - core)):
        start = pl.multiple_of(h * half + me * half_s, half_s)
        out_ref[k * half_s : (k + 1) * half_s, :] = state_s[pl.ds(start, half_s), :]


def dense_call(mine, other, rowmask, n_probe, shard, feat, beta_lane):
    files = 2 * mine.shape[0]
    run = files // (2 * rowmask.shape[0])
    tile = run
    while tile * 2 <= min(512, files // 2) and (files // 2) % (tile * 2) == 0:
        tile *= 2
    rowmask = rowmask.reshape(-1, tile // run, files)
    vmem = pl.BlockSpec(memory_space=pltpu.VMEM)
    return pl.pallas_call(
        lambda *refs: dense_kernel(ITERS, tile, beta_lane, PROBE_PARTS, *refs),
        out_shape=jax.ShapeDtypeStruct((shard, n_probe), jnp.float32),
        in_specs=[vmem, vmem, vmem],
        out_specs=vmem,
        scratch_shapes=[
            pltpu.VMEM((feat, files), jnp.bfloat16),
            pltpu.VMEM((files, feat), jnp.bfloat16),
            pltpu.VMEM((files, 1), jnp.float32),
            pltpu.VMEM((files, files), jnp.bfloat16),
            pltpu.VMEM((files, n_probe), jnp.float32),
        ],
        cost_estimate=pl.CostEstimate(
            flops=2 * files * files * feat + 4 * ITERS * files * files * n_probe,
            transcendentals=files * files,
            bytes_accessed=files * mine.shape[1] * 2 + 4 * files * n_probe,
        ),
    )(mine, other, rowmask)


def dense_path(embed, beta, block_mask, counts, probes, n_dev, n_row, me):
    shard, feat = embed.shape
    files = shard * n_dev
    half_s = shard // 2
    half_f = files // 2
    nb = block_mask.shape[1]
    blk = files // nb
    local_blocks = block_mask.shape[0]
    n_probe = probes.shape[0]
    per_row = n_dev // n_row
    mask_flat = block_mask.reshape(-1).astype(jnp.float32)
    mask_cols = -(-mask_flat.shape[0] // half_s)
    mask_part = jnp.pad(mask_flat, (0, half_s * mask_cols - mask_flat.shape[0]))
    mask_part = jnp.tile(mask_part.reshape(half_s, mask_cols), (2, 1))
    used = PROBE_PARTS * n_probe + 1 + mask_cols
    lanes = -(-used // 128) * 128
    extras = jnp.concatenate(
        [
            split3(probes)[:PROBE_PARTS].astype(jnp.float32).reshape(PROBE_PARTS * n_probe, shard),
            beta[None, :].astype(jnp.float32),
            mask_part.T,
        ],
        axis=0,
    )
    payload = jnp.concatenate(
        [embed, jnp.pad(extras.T.astype(jnp.bfloat16), ((0, 0), (0, lanes - used)))], axis=1
    )
    width = payload.shape[1]
    halves = payload.reshape(2, half_s, width)
    wide = jnp.broadcast_to(
        halves[None, :, None], (n_row // 2, 2, per_row, half_s, width)
    ).reshape(n_dev, half_s, width)
    mine = lax.all_to_all(wide, AXES, 0, 0, tiled=True)
    other = lax.ppermute(mine, "row", [(r, r ^ 1) for r in range(n_row)])
    core = lax.axis_index("row") % 2
    pos = lax.iota(jnp.int32, files)
    run = blk // 2
    in_run = lax.iota(jnp.int32, files) % run
    run_dev = in_run // half_s
    half_of = jnp.broadcast_to((lax.iota(jnp.int32, 2) ^ core)[:, None, None], (2, nb, run))
    in_block = (run_dev % (blk // shard)) * shard + half_of.reshape(files) * half_s + in_run % half_s
    block_counts = jnp.broadcast_to(counts[None, :, None], (2, nb, run)).reshape(files)
    live = in_block < block_counts
    mine2 = mine.reshape(half_f, width)
    other2 = other.reshape(half_f, width)
    mask_got = mine[:, :, feat + PROBE_PARTS * n_probe + 1 : feat + used].reshape(n_dev, -1)
    mask_got = mask_got[:, : local_blocks * nb]
    mask_full = mask_got.reshape(n_row, per_row, local_blocks, nb)[:, 0].reshape(nb, nb)
    block_ok = jnp.broadcast_to((mask_full == 1)[:, None, :, None], (nb, 2, nb, run))
    rowmask = jnp.where(block_ok.reshape(nb, files) & live[None, :], 1.0, 0.0).astype(jnp.float32)
    own_t = dense_call(mine2, other2, rowmask, n_probe, shard, feat, feat + PROBE_PARTS * n_probe)
    return own_t.T


def normalize(embed):
    values = embed.astype(jnp.float32)
    return (values * lax.rsqrt(jnp.mean(values * values, axis=1, keepdims=True) + 1e-06)).astype(
        jnp.bfloat16
    )


def split3(x):
    hi = lax.reduce_precision(x, exponent_bits=8, mantissa_bits=7)
    rest = x - hi
    mid = lax.reduce_precision(rest, exponent_bits=8, mantissa_bits=7)
    lo = rest - mid
    return jnp.stack([hi, mid, lo]).astype(jnp.bfloat16)


def join3(parts):
    parts = parts.astype(jnp.float32)
    if parts.shape[0] == 1:
        return parts[0]
    return (parts[0] + parts[1]) + parts[2]


def pack_rows(flat, width):
    rows = -(-flat.shape[0] // width)
    return jnp.pad(flat, (0, rows * width - flat.shape[0])).reshape(rows, width), rows


def body(embed, beta, block_mask, counts, probes):
    n_dev = lax.axis_size("row") * lax.axis_size("col")
    n_row = lax.axis_size("row")
    me = lax.axis_index(AXES)
    shard, feat = embed.shape
    files = shard * n_dev
    nb = block_mask.shape[1]
    blk = files // nb
    local_blocks = block_mask.shape[0]

    unit_own = normalize(embed)
    beta_rows, beta_n = pack_rows(beta, feat)
    mask_rows, mask_n = pack_rows(block_mask.reshape(-1).astype(jnp.bfloat16), feat)
    replicate = files * files <= REPLICATE_CELLS
    n_probe = probes.shape[0]
    if (
        replicate
        and n_row % 2 == 0
        and shard % 2 == 0
        and blk % shard == 0
        and (blk // 2) % 8 == 0
        and files % 128 == 0
    ):
        return dense_path(embed, beta, block_mask, counts, probes, n_dev, n_row, me)
    if replicate:
        mask_flat = block_mask.reshape(-1).astype(jnp.bfloat16)
        mask_cols = -(-mask_flat.shape[0] // shard)
        mask_part = jnp.pad(mask_flat, (0, shard * mask_cols - mask_flat.shape[0]))
        used = 3 * n_probe + 1 + mask_cols
        lanes = -(-used // 128) * 128
        extra_cols = jnp.concatenate(
            [
                jnp.moveaxis(split3(probes.T), 0, 1).reshape(shard, 3 * n_probe),
                beta[:, None],
                mask_part.reshape(shard, mask_cols),
                jnp.zeros((shard, lanes - used), jnp.bfloat16),
            ],
            axis=1,
        )
        got = gather_halves(jnp.concatenate([unit_own, extra_cols], axis=1), n_dev, n_row)
        unit_all = got[:, :, :feat].reshape(files, feat)
        tail = got[:, :, feat:].reshape(files, lanes)
        probes_t = join3(
            jnp.stack([tail[:, k * n_probe : (k + 1) * n_probe] for k in range(3)])
        )
        beta_all = tail[:, 3 * n_probe]
        mask_got = got[:, :, feat + 3 * n_probe + 1 : feat + used].reshape(n_dev, -1)
        mask_got = mask_got[:, : local_blocks * nb]
    else:
        unit_all = gather_rows(unit_own, n_dev).reshape(files, feat)
        extra = gather_rows(jnp.concatenate([beta_rows, mask_rows], axis=0), n_dev)
        beta_all = extra[:, 0, :shard].reshape(files)
        mask_got = extra[:, beta_n:, :].reshape(n_dev, -1)[:, : local_blocks * nb]
    per_row = n_dev // n_row
    mask_full = (
        mask_got.reshape(n_row, per_row, local_blocks, nb)[:, 0].reshape(nb, nb).astype(jnp.int32)
    )
    scale_all = beta_all.astype(jnp.float32) / feat

    col_ids = lax.iota(jnp.int32, files)
    col_block = col_ids // blk
    in_block = lax.iota(jnp.int32, blk)
    col_live = (in_block[None, :] < counts[:, None]).reshape(files)

    if replicate:
        gram = lax.dot_general(
            unit_all, unit_all, (((1,), (1,)), ((), ())), preferred_element_type=jnp.float32
        )
        scores = gram * scale_all[:, None]
        block_ok = jnp.broadcast_to(
            (mask_full == 1)[:, None, :, None], (nb, blk, nb, blk)
        ).reshape(files, files)
        allowed = block_ok & col_live[None, :] & (col_ids[:, None] != col_ids[None, :])
        masked = jnp.where(allowed, scores, -1e30)
        row_top = jnp.max(masked, axis=1)
        row_mass = jnp.sum(jnp.where(allowed, jnp.exp(masked - row_top[:, None]), 0.0), axis=1)
        weights = jnp.where(allowed, jnp.exp(masked - row_top[:, None]) / row_mass[:, None], 0.0)
        col_mass = jnp.sum(weights, axis=0)
        inv_root = lax.rsqrt((1.0 + col_mass) * 0.5)
        affinity = weights.astype(jnp.bfloat16)
        state = probes_t
        for sweep in range(ITERS):
            scaled = (state * inv_root[:, None]).astype(jnp.bfloat16)
            row_part = jnp.dot(affinity, scaled, preferred_element_type=jnp.float32)
            col_part = lax.dot_general(
                affinity, scaled, (((0,), (0,)), ((), ())), preferred_element_type=jnp.float32
            )
            state = (row_part + col_part) * (0.5 * inv_root)[:, None]
        return lax.dynamic_slice_in_dim(state, me * shard, shard, 0).T

    own_ids = me * shard + lax.iota(jnp.int32, shard)
    own_block = own_ids // blk
    gram = lax.dot_general(
        unit_own, unit_all, (((1,), (1,)), ((), ())), preferred_element_type=jnp.float32
    )
    own_scale = lax.dynamic_slice_in_dim(scale_all, me * shard, shard, 0)
    scores = gram * own_scale[:, None]
    row_ok = jnp.take(jnp.take(mask_full, own_block, axis=0), col_block, axis=1) == 1
    allowed = row_ok & col_live[None, :] & (own_ids[:, None] != col_ids[None, :])
    masked = jnp.where(allowed, scores, -1e30)
    row_top = jnp.max(masked, axis=1)
    row_mass = jnp.sum(jnp.where(allowed, jnp.exp(masked - row_top[:, None]), 0.0), axis=1)
    weights = jnp.where(allowed, jnp.exp(masked - row_top[:, None]) / row_mass[:, None], 0.0)
    stats = gather_rows(jnp.stack([row_top, row_mass], axis=1), n_dev).reshape(files, 2)
    top_all, mass_all = stats[:, 0], stats[:, 1]
    scores_t = gram * scale_all[None, :]
    own_live = jnp.take(col_live, own_ids, axis=0)
    col_ok = jnp.take(jnp.take(mask_full, col_block, axis=0), own_block, axis=1).T == 1
    allowed_t = col_ok & own_live[:, None] & (own_ids[:, None] != col_ids[None, :])
    masked_t = jnp.where(allowed_t, scores_t, -1e30)
    weights_t = jnp.where(
        allowed_t, jnp.exp(masked_t - top_all[None, :]) / mass_all[None, :], 0.0
    )
    col_mass = jnp.sum(weights_t, axis=1)
    inv_root = lax.rsqrt((1.0 + col_mass) * 0.5)
    aff_rows = weights.astype(jnp.bfloat16)
    aff_cols = weights_t.astype(jnp.bfloat16)
    state = probes
    for sweep in range(ITERS):
        scaled = (state * inv_root[None, :]).astype(jnp.bfloat16)
        scaled_all = gather_rows(scaled.T, n_dev).reshape(files, probes.shape[0])
        row_part = jnp.dot(aff_rows, scaled_all, preferred_element_type=jnp.float32)
        col_part = jnp.dot(aff_cols, scaled_all, preferred_element_type=jnp.float32)
        state = ((row_part + col_part) * (0.5 * inv_root)[:, None]).T
    return state


def solution(mesh):
    placed = (
        P(AXES, None),
        P(AXES),
        P("row", None),
        P(),
        P(None, AXES),
    )
    return jax.shard_map(body, mesh=mesh, in_specs=placed, out_specs=P(None, AXES), check_vma=False)
```

```python
import jax
import jax.numpy as jnp
from jax import lax
from jax.experimental import pallas as pl
from jax.experimental.pallas import tpu as pltpu
from jax.sharding import PartitionSpec as P

ITERS = 2
PROBE_PARTS = 1
AXES = ("row", "col")
A2A_BYTES = 8 << 20
REPLICATE_CELLS = 1 << 21


def gather_rows(x, n_dev):
    if n_dev * x.size * x.dtype.itemsize <= A2A_BYTES:
        wide = jnp.broadcast_to(x[None], (n_dev,) + x.shape)
        return lax.all_to_all(wide, AXES, 0, 0, tiled=True)
    return lax.all_gather(x, AXES, axis=0, tiled=False)


def gather_halves(x, n_dev, n_row):
    if n_row % 2:
        return gather_rows(x, n_dev)
    rows = x.shape[0] + x.shape[0] % 2
    halves = jnp.pad(x, ((0, rows - x.shape[0]), (0, 0))).reshape(2, rows // 2, x.shape[1])
    per_row = n_dev // n_row
    wide = jnp.broadcast_to(
        halves[None, :, None], (n_row // 2, 2, per_row, rows // 2, x.shape[1])
    ).reshape(n_dev, rows // 2, x.shape[1])
    mine = lax.all_to_all(wide, AXES, 0, 0, tiled=True)
    other = lax.ppermute(mine, "row", [(r, r ^ 1) for r in range(n_row)])
    first = lax.axis_index("row") % 2 == 0
    low = jnp.where(first, mine, other)
    high = jnp.where(first, other, mine)
    return jnp.concatenate([low, high], axis=1)[:, : x.shape[0]]


def dense_kernel(n_iter, tile, beta_lane, n_parts, mine_ref, other_ref, rowmask_ref, out_ref, unit_t, unit_s, scale_s, aff_s, state_s):
    feat, files = unit_t.shape
    half = files // 2
    runs = max(half // tile, 1)
    for k, ref in enumerate((mine_ref, other_ref)):
        values = ref[:, 0:feat].astype(jnp.float32)
        unit = (
            values * lax.rsqrt(jnp.mean(values * values, axis=1, keepdims=True) + 1e-06)
        ).astype(jnp.bfloat16)
        unit_s[k * half : (k + 1) * half, :] = unit
        unit_t[:, k * half : (k + 1) * half] = unit.astype(jnp.float32).T.astype(jnp.bfloat16)
        scale_s[k * half : (k + 1) * half, :] = (
            ref[:, beta_lane : beta_lane + 1].astype(jnp.float32) / feat
        )
    per_tile = rowmask_ref.shape[1]
    run = tile // per_tile
    col_pos = lax.broadcasted_iota(jnp.int32, (tile, files), 1)
    row_pos = lax.broadcasted_iota(jnp.int32, (tile, files), 0)

    def step(t, colsum):
        p0 = pl.multiple_of(t * tile, tile)
        gram = jnp.dot(unit_s[pl.ds(p0, tile), :], unit_t[...], preferred_element_type=jnp.float32)
        scores = gram * scale_s[pl.ds(p0, tile), :]
        runs_here = rowmask_ref[t % runs]
        block_row = jnp.broadcast_to(runs_here[:, None, :], (per_tile, run, files)).reshape(tile, files)
        ok = (block_row > 0.0) & (row_pos + p0 != col_pos)
        masked = jnp.where(ok, scores, -1e30)
        top = jnp.max(masked, axis=1, keepdims=True)
        e = jnp.exp(masked - top)
        mass = jnp.sum(e, axis=1, keepdims=True)
        weights = e * (1.0 / mass)
        aff_s[pl.ds(p0, tile), :] = weights.astype(jnp.bfloat16)
        return colsum + jnp.sum(weights, axis=0, keepdims=True)

    colsum = lax.fori_loop(0, files // tile, step, jnp.zeros((1, files), jnp.float32))
    inv_root = lax.rsqrt((1.0 + colsum) * 0.5)
    n_probe = out_ref.shape[1]
    state = jnp.concatenate(
        [
            sum(
                ref[:, feat + k * n_probe : feat + (k + 1) * n_probe].astype(jnp.float32)
                for k in range(n_parts)
            ).T
            for ref in (mine_ref, other_ref)
        ],
        axis=1,
    )
    for sweep in range(n_iter):
        scaled_f = (state * inv_root).astype(jnp.bfloat16).astype(jnp.float32)
        scaled = scaled_f.astype(jnp.bfloat16)
        row_t = jnp.dot(aff_s[...], scaled_f.T.astype(jnp.bfloat16), preferred_element_type=jnp.float32)
        col_part = jnp.dot(scaled, aff_s[...], preferred_element_type=jnp.float32)
        if sweep + 1 < n_iter:
            state = (row_t.T + col_part) * (0.5 * inv_root)
        else:
            state_s[...] = (row_t + col_part.T) * (0.5 * inv_root).T
    shard = out_ref.shape[0]
    half_s = shard // 2
    core = lax.axis_index("row") % 2
    me = lax.axis_index("row") * lax.axis_size("col") + lax.axis_index("col")
    for k, h in enumerate((core, 1 - core)):
        start = pl.multiple_of(h * half + me * half_s, half_s)
        out_ref[k * half_s : (k + 1) * half_s, :] = state_s[pl.ds(start, half_s), :]


def dense_call(mine, other, rowmask, n_probe, shard, feat, beta_lane):
    files = 2 * mine.shape[0]
    run = files // (2 * rowmask.shape[0])
    tile = run
    while tile * 2 <= min(1024, files) and files % (tile * 2) == 0:
        tile *= 2
    if tile > files // 2:
        rowmask = jnp.tile(rowmask, (tile // (files // 2), 1))
    rowmask = rowmask.reshape(-1, tile // run, files)
    vmem = pl.BlockSpec(memory_space=pltpu.VMEM)
    return pl.pallas_call(
        lambda *refs: dense_kernel(ITERS, tile, beta_lane, PROBE_PARTS, *refs),
        out_shape=jax.ShapeDtypeStruct((shard, n_probe), jnp.float32),
        in_specs=[vmem, vmem, vmem],
        out_specs=vmem,
        scratch_shapes=[
            pltpu.VMEM((feat, files), jnp.bfloat16),
            pltpu.VMEM((files, feat), jnp.bfloat16),
            pltpu.VMEM((files, 1), jnp.float32),
            pltpu.VMEM((files, files), jnp.bfloat16),
            pltpu.VMEM((files, n_probe), jnp.float32),
        ],
        cost_estimate=pl.CostEstimate(
            flops=2 * files * files * feat + 4 * ITERS * files * files * n_probe,
            transcendentals=files * files,
            bytes_accessed=files * mine.shape[1] * 2 + 4 * files * n_probe,
        ),
    )(mine, other, rowmask)


def dense_path(embed, beta, block_mask, counts, probes, n_dev, n_row, me):
    shard, feat = embed.shape
    files = shard * n_dev
    half_s = shard // 2
    half_f = files // 2
    nb = block_mask.shape[1]
    blk = files // nb
    local_blocks = block_mask.shape[0]
    n_probe = probes.shape[0]
    per_row = n_dev // n_row
    mask_flat = block_mask.reshape(-1).astype(jnp.float32)
    mask_cols = -(-mask_flat.shape[0] // half_s)
    mask_part = jnp.pad(mask_flat, (0, half_s * mask_cols - mask_flat.shape[0]))
    mask_part = jnp.tile(mask_part.reshape(half_s, mask_cols), (2, 1))
    used = PROBE_PARTS * n_probe + 1 + mask_cols
    lanes = -(-used // 128) * 128
    extras = jnp.concatenate(
        [
            split3(probes)[:PROBE_PARTS].astype(jnp.float32).reshape(PROBE_PARTS * n_probe, shard),
            beta[None, :].astype(jnp.float32),
            mask_part.T,
        ],
        axis=0,
    )
    payload = jnp.concatenate(
        [embed, jnp.pad(extras.T.astype(jnp.bfloat16), ((0, 0), (0, lanes - used)))], axis=1
    )
    width = payload.shape[1]
    halves = payload.reshape(2, half_s, width)
    wide = jnp.broadcast_to(
        halves[None, :, None], (n_row // 2, 2, per_row, half_s, width)
    ).reshape(n_dev, half_s, width)
    mine = lax.all_to_all(wide, AXES, 0, 0, tiled=True)
    other = lax.ppermute(mine, "row", [(r, r ^ 1) for r in range(n_row)])
    core = lax.axis_index("row") % 2
    pos = lax.iota(jnp.int32, files)
    run = blk // 2
    in_run = lax.iota(jnp.int32, files) % run
    run_dev = in_run // half_s
    half_of = jnp.broadcast_to((lax.iota(jnp.int32, 2) ^ core)[:, None, None], (2, nb, run))
    in_block = (run_dev % (blk // shard)) * shard + half_of.reshape(files) * half_s + in_run % half_s
    block_counts = jnp.broadcast_to(counts[None, :, None], (2, nb, run)).reshape(files)
    live = in_block < block_counts
    mine2 = mine.reshape(half_f, width)
    other2 = other.reshape(half_f, width)
    mask_got = mine[:, :, feat + PROBE_PARTS * n_probe + 1 : feat + used].reshape(n_dev, -1)
    mask_got = mask_got[:, : local_blocks * nb]
    mask_full = mask_got.reshape(n_row, per_row, local_blocks, nb)[:, 0].reshape(nb, nb)
    block_ok = jnp.broadcast_to((mask_full == 1)[:, None, :, None], (nb, 2, nb, run))
    rowmask = jnp.where(block_ok.reshape(nb, files) & live[None, :], 1.0, 0.0).astype(jnp.float32)
    own_t = dense_call(mine2, other2, rowmask, n_probe, shard, feat, feat + PROBE_PARTS * n_probe)
    return own_t.T


def normalize(embed):
    values = embed.astype(jnp.float32)
    return (values * lax.rsqrt(jnp.mean(values * values, axis=1, keepdims=True) + 1e-06)).astype(
        jnp.bfloat16
    )


def split3(x):
    hi = lax.reduce_precision(x, exponent_bits=8, mantissa_bits=7)
    rest = x - hi
    mid = lax.reduce_precision(rest, exponent_bits=8, mantissa_bits=7)
    lo = rest - mid
    return jnp.stack([hi, mid, lo]).astype(jnp.bfloat16)


def join3(parts):
    parts = parts.astype(jnp.float32)
    if parts.shape[0] == 1:
        return parts[0]
    return (parts[0] + parts[1]) + parts[2]


def pack_rows(flat, width):
    rows = -(-flat.shape[0] // width)
    return jnp.pad(flat, (0, rows * width - flat.shape[0])).reshape(rows, width), rows


def body(embed, beta, block_mask, counts, probes):
    n_dev = lax.axis_size("row") * lax.axis_size("col")
    n_row = lax.axis_size("row")
    me = lax.axis_index(AXES)
    shard, feat = embed.shape
    files = shard * n_dev
    nb = block_mask.shape[1]
    blk = files // nb
    local_blocks = block_mask.shape[0]

    unit_own = normalize(embed)
    beta_rows, beta_n = pack_rows(beta, feat)
    mask_rows, mask_n = pack_rows(block_mask.reshape(-1).astype(jnp.bfloat16), feat)
    replicate = files * files <= REPLICATE_CELLS
    n_probe = probes.shape[0]
    if (
        replicate
        and n_row % 2 == 0
        and shard % 2 == 0
        and blk % shard == 0
        and (blk // 2) % 8 == 0
        and files % 128 == 0
    ):
        return dense_path(embed, beta, block_mask, counts, probes, n_dev, n_row, me)
    if replicate:
        mask_flat = block_mask.reshape(-1).astype(jnp.bfloat16)
        mask_cols = -(-mask_flat.shape[0] // shard)
        mask_part = jnp.pad(mask_flat, (0, shard * mask_cols - mask_flat.shape[0]))
        used = 3 * n_probe + 1 + mask_cols
        lanes = -(-used // 128) * 128
        extra_cols = jnp.concatenate(
            [
                jnp.moveaxis(split3(probes.T), 0, 1).reshape(shard, 3 * n_probe),
                beta[:, None],
                mask_part.reshape(shard, mask_cols),
                jnp.zeros((shard, lanes - used), jnp.bfloat16),
            ],
            axis=1,
        )
        got = gather_halves(jnp.concatenate([unit_own, extra_cols], axis=1), n_dev, n_row)
        unit_all = got[:, :, :feat].reshape(files, feat)
        tail = got[:, :, feat:].reshape(files, lanes)
        probes_t = join3(
            jnp.stack([tail[:, k * n_probe : (k + 1) * n_probe] for k in range(3)])
        )
        beta_all = tail[:, 3 * n_probe]
        mask_got = got[:, :, feat + 3 * n_probe + 1 : feat + used].reshape(n_dev, -1)
        mask_got = mask_got[:, : local_blocks * nb]
    else:
        unit_all = gather_rows(unit_own, n_dev).reshape(files, feat)
        extra = gather_rows(jnp.concatenate([beta_rows, mask_rows], axis=0), n_dev)
        beta_all = extra[:, 0, :shard].reshape(files)
        mask_got = extra[:, beta_n:, :].reshape(n_dev, -1)[:, : local_blocks * nb]
    per_row = n_dev // n_row
    mask_full = (
        mask_got.reshape(n_row, per_row, local_blocks, nb)[:, 0].reshape(nb, nb).astype(jnp.int32)
    )
    scale_all = beta_all.astype(jnp.float32) / feat

    col_ids = lax.iota(jnp.int32, files)
    col_block = col_ids // blk
    in_block = lax.iota(jnp.int32, blk)
    col_live = (in_block[None, :] < counts[:, None]).reshape(files)

    if replicate:
        gram = lax.dot_general(
            unit_all, unit_all, (((1,), (1,)), ((), ())), preferred_element_type=jnp.float32
        )
        scores = gram * scale_all[:, None]
        block_ok = jnp.broadcast_to(
            (mask_full == 1)[:, None, :, None], (nb, blk, nb, blk)
        ).reshape(files, files)
        allowed = block_ok & col_live[None, :] & (col_ids[:, None] != col_ids[None, :])
        masked = jnp.where(allowed, scores, -1e30)
        row_top = jnp.max(masked, axis=1)
        row_mass = jnp.sum(jnp.where(allowed, jnp.exp(masked - row_top[:, None]), 0.0), axis=1)
        weights = jnp.where(allowed, jnp.exp(masked - row_top[:, None]) / row_mass[:, None], 0.0)
        col_mass = jnp.sum(weights, axis=0)
        inv_root = lax.rsqrt((1.0 + col_mass) * 0.5)
        affinity = weights.astype(jnp.bfloat16)
        state = probes_t
        for sweep in range(ITERS):
            scaled = (state * inv_root[:, None]).astype(jnp.bfloat16)
            row_part = jnp.dot(affinity, scaled, preferred_element_type=jnp.float32)
            col_part = lax.dot_general(
                affinity, scaled, (((0,), (0,)), ((), ())), preferred_element_type=jnp.float32
            )
            state = (row_part + col_part) * (0.5 * inv_root)[:, None]
        return lax.dynamic_slice_in_dim(state, me * shard, shard, 0).T

    own_ids = me * shard + lax.iota(jnp.int32, shard)
    own_block = own_ids // blk
    gram = lax.dot_general(
        unit_own, unit_all, (((1,), (1,)), ((), ())), preferred_element_type=jnp.float32
    )
    own_scale = lax.dynamic_slice_in_dim(scale_all, me * shard, shard, 0)
    scores = gram * own_scale[:, None]
    row_ok = jnp.take(jnp.take(mask_full, own_block, axis=0), col_block, axis=1) == 1
    allowed = row_ok & col_live[None, :] & (own_ids[:, None] != col_ids[None, :])
    masked = jnp.where(allowed, scores, -1e30)
    row_top = jnp.max(masked, axis=1)
    row_mass = jnp.sum(jnp.where(allowed, jnp.exp(masked - row_top[:, None]), 0.0), axis=1)
    weights = jnp.where(allowed, jnp.exp(masked - row_top[:, None]) / row_mass[:, None], 0.0)
    stats = gather_rows(jnp.stack([row_top, row_mass], axis=1), n_dev).reshape(files, 2)
    top_all, mass_all = stats[:, 0], stats[:, 1]
    scores_t = gram * scale_all[None, :]
    own_live = jnp.take(col_live, own_ids, axis=0)
    col_ok = jnp.take(jnp.take(mask_full, col_block, axis=0), own_block, axis=1).T == 1
    allowed_t = col_ok & own_live[:, None] & (own_ids[:, None] != col_ids[None, :])
    masked_t = jnp.where(allowed_t, scores_t, -1e30)
    weights_t = jnp.where(
        allowed_t, jnp.exp(masked_t - top_all[None, :]) / mass_all[None, :], 0.0
    )
    col_mass = jnp.sum(weights_t, axis=1)
    inv_root = lax.rsqrt((1.0 + col_mass) * 0.5)
    aff_rows = weights.astype(jnp.bfloat16)
    aff_cols = weights_t.astype(jnp.bfloat16)
    state = probes
    for sweep in range(ITERS):
        scaled = (state * inv_root[None, :]).astype(jnp.bfloat16)
        scaled_all = gather_rows(scaled.T, n_dev).reshape(files, probes.shape[0])
        row_part = jnp.dot(aff_rows, scaled_all, preferred_element_type=jnp.float32)
        col_part = jnp.dot(aff_cols, scaled_all, preferred_element_type=jnp.float32)
        state = ((row_part + col_part) * (0.5 * inv_root)[:, None]).T
    return state


def solution(mesh):
    placed = (
        P(AXES, None),
        P(AXES),
        P("row", None),
        P(),
        P(None, AXES),
    )
    return jax.shard_map(body, mesh=mesh, in_specs=placed, out_specs=P(None, AXES), check_vma=False)
```

```python
import jax
import jax.numpy as jnp
from jax import lax
from jax.experimental import pallas as pl
from jax.experimental.pallas import tpu as pltpu
from jax.sharding import PartitionSpec as P

ITERS = 2
PROBE_PARTS = 1
AXES = ("row", "col")
A2A_BYTES = 8 << 20
REPLICATE_CELLS = 1 << 21


def gather_rows(x, n_dev):
    if n_dev * x.size * x.dtype.itemsize <= A2A_BYTES:
        wide = jnp.broadcast_to(x[None], (n_dev,) + x.shape)
        return lax.all_to_all(wide, AXES, 0, 0, tiled=True)
    return lax.all_gather(x, AXES, axis=0, tiled=False)


def gather_halves(x, n_dev, n_row):
    if n_row % 2:
        return gather_rows(x, n_dev)
    rows = x.shape[0] + x.shape[0] % 2
    halves = jnp.pad(x, ((0, rows - x.shape[0]), (0, 0))).reshape(2, rows // 2, x.shape[1])
    per_row = n_dev // n_row
    wide = jnp.broadcast_to(
        halves[None, :, None], (n_row // 2, 2, per_row, rows // 2, x.shape[1])
    ).reshape(n_dev, rows // 2, x.shape[1])
    mine = lax.all_to_all(wide, AXES, 0, 0, tiled=True)
    other = lax.ppermute(mine, "row", [(r, r ^ 1) for r in range(n_row)])
    first = lax.axis_index("row") % 2 == 0
    low = jnp.where(first, mine, other)
    high = jnp.where(first, other, mine)
    return jnp.concatenate([low, high], axis=1)[:, : x.shape[0]]


def dense_kernel(n_iter, tile, beta_lane, n_parts, mine_ref, other_ref, rowmask_ref, out_ref, unit_t, unit_s, scale_s, aff_s, state_s, gram_s):
    feat, files = unit_t.shape
    half = files // 2
    runs = half // tile
    for k, ref in enumerate((mine_ref, other_ref)):
        values = ref[:, 0:feat].astype(jnp.float32)
        unit = (
            values * lax.rsqrt(jnp.mean(values * values, axis=1, keepdims=True) + 1e-06)
        ).astype(jnp.bfloat16)
        unit_s[k * half : (k + 1) * half, :] = unit
        unit_t[:, k * half : (k + 1) * half] = unit.astype(jnp.float32).T.astype(jnp.bfloat16)
        scale_s[k * half : (k + 1) * half, :] = (
            ref[:, beta_lane : beta_lane + 1].astype(jnp.float32) / feat
        )
    gram_s[...] = jnp.dot(unit_s[...], unit_t[...], preferred_element_type=jnp.float32)
    per_tile = rowmask_ref.shape[1]
    run = tile // per_tile
    col_pos = lax.broadcasted_iota(jnp.int32, (tile, files), 1)
    row_pos = lax.broadcasted_iota(jnp.int32, (tile, files), 0)

    def step(t, colsum):
        p0 = pl.multiple_of(t * tile, tile)
        scores = gram_s[pl.ds(p0, tile), :] * scale_s[pl.ds(p0, tile), :]
        runs_here = rowmask_ref[t % runs]
        block_row = jnp.broadcast_to(runs_here[:, None, :], (per_tile, run, files)).reshape(tile, files)
        ok = (block_row > 0.0) & (row_pos + p0 != col_pos)
        masked = jnp.where(ok, scores, -1e30)
        top = jnp.max(masked, axis=1, keepdims=True)
        e = jnp.exp(masked - top)
        mass = jnp.sum(e, axis=1, keepdims=True)
        weights = e * (1.0 / mass)
        aff_s[pl.ds(p0, tile), :] = weights.astype(jnp.bfloat16)
        return colsum + jnp.sum(weights, axis=0, keepdims=True)

    colsum = lax.fori_loop(0, files // tile, step, jnp.zeros((1, files), jnp.float32))
    inv_root = lax.rsqrt((1.0 + colsum) * 0.5)
    n_probe = out_ref.shape[1]
    state = jnp.concatenate(
        [
            sum(
                ref[:, feat + k * n_probe : feat + (k + 1) * n_probe].astype(jnp.float32)
                for k in range(n_parts)
            ).T
            for ref in (mine_ref, other_ref)
        ],
        axis=1,
    )
    for sweep in range(n_iter):
        scaled_f = (state * inv_root).astype(jnp.bfloat16).astype(jnp.float32)
        scaled = scaled_f.astype(jnp.bfloat16)
        row_t = jnp.dot(aff_s[...], scaled_f.T.astype(jnp.bfloat16), preferred_element_type=jnp.float32)
        col_part = jnp.dot(scaled, aff_s[...], preferred_element_type=jnp.float32)
        if sweep + 1 < n_iter:
            state = (row_t.T + col_part) * (0.5 * inv_root)
        else:
            state_s[...] = (row_t + col_part.T) * (0.5 * inv_root).T
    shard = out_ref.shape[0]
    half_s = shard // 2
    core = lax.axis_index("row") % 2
    me = lax.axis_index("row") * lax.axis_size("col") + lax.axis_index("col")
    for k, h in enumerate((core, 1 - core)):
        start = pl.multiple_of(h * half + me * half_s, half_s)
        out_ref[k * half_s : (k + 1) * half_s, :] = state_s[pl.ds(start, half_s), :]


def dense_call(mine, other, rowmask, n_probe, shard, feat, beta_lane):
    files = 2 * mine.shape[0]
    run = files // (2 * rowmask.shape[0])
    tile = run
    while tile * 2 <= min(512, files // 2) and (files // 2) % (tile * 2) == 0:
        tile *= 2
    rowmask = rowmask.reshape(-1, tile // run, files)
    vmem = pl.BlockSpec(memory_space=pltpu.VMEM)
    return pl.pallas_call(
        lambda *refs: dense_kernel(ITERS, tile, beta_lane, PROBE_PARTS, *refs),
        out_shape=jax.ShapeDtypeStruct((shard, n_probe), jnp.float32),
        in_specs=[vmem, vmem, vmem],
        out_specs=vmem,
        scratch_shapes=[
            pltpu.VMEM((feat, files), jnp.bfloat16),
            pltpu.VMEM((files, feat), jnp.bfloat16),
            pltpu.VMEM((files, 1), jnp.float32),
            pltpu.VMEM((files, files), jnp.bfloat16),
            pltpu.VMEM((files, n_probe), jnp.float32),
            pltpu.VMEM((files, files), jnp.float32),
        ],
        cost_estimate=pl.CostEstimate(
            flops=2 * files * files * feat + 4 * ITERS * files * files * n_probe,
            transcendentals=files * files,
            bytes_accessed=files * mine.shape[1] * 2 + 4 * files * n_probe,
        ),
    )(mine, other, rowmask)


def dense_path(embed, beta, block_mask, counts, probes, n_dev, n_row, me):
    shard, feat = embed.shape
    files = shard * n_dev
    half_s = shard // 2
    half_f = files // 2
    nb = block_mask.shape[1]
    blk = files // nb
    local_blocks = block_mask.shape[0]
    n_probe = probes.shape[0]
    per_row = n_dev // n_row
    mask_flat = block_mask.reshape(-1).astype(jnp.float32)
    mask_cols = -(-mask_flat.shape[0] // half_s)
    mask_part = jnp.pad(mask_flat, (0, half_s * mask_cols - mask_flat.shape[0]))
    mask_part = jnp.tile(mask_part.reshape(half_s, mask_cols), (2, 1))
    used = PROBE_PARTS * n_probe + 1 + mask_cols
    lanes = -(-used // 128) * 128
    extras = jnp.concatenate(
        [
            split3(probes)[:PROBE_PARTS].astype(jnp.float32).reshape(PROBE_PARTS * n_probe, shard),
            beta[None, :].astype(jnp.float32),
            mask_part.T,
        ],
        axis=0,
    )
    payload = jnp.concatenate(
        [embed, jnp.pad(extras.T.astype(jnp.bfloat16), ((0, 0), (0, lanes - used)))], axis=1
    )
    width = payload.shape[1]
    halves = payload.reshape(2, half_s, width)
    wide = jnp.broadcast_to(
        halves[None, :, None], (n_row // 2, 2, per_row, half_s, width)
    ).reshape(n_dev, half_s, width)
    mine = lax.all_to_all(wide, AXES, 0, 0, tiled=True)
    other = lax.ppermute(mine, "row", [(r, r ^ 1) for r in range(n_row)])
    core = lax.axis_index("row") % 2
    pos = lax.iota(jnp.int32, files)
    run = blk // 2
    in_run = lax.iota(jnp.int32, files) % run
    run_dev = in_run // half_s
    half_of = jnp.broadcast_to((lax.iota(jnp.int32, 2) ^ core)[:, None, None], (2, nb, run))
    in_block = (run_dev % (blk // shard)) * shard + half_of.reshape(files) * half_s + in_run % half_s
    block_counts = jnp.broadcast_to(counts[None, :, None], (2, nb, run)).reshape(files)
    live = in_block < block_counts
    mine2 = mine.reshape(half_f, width)
    other2 = other.reshape(half_f, width)
    mask_got = mine[:, :, feat + PROBE_PARTS * n_probe + 1 : feat + used].reshape(n_dev, -1)
    mask_got = mask_got[:, : local_blocks * nb]
    mask_full = mask_got.reshape(n_row, per_row, local_blocks, nb)[:, 0].reshape(nb, nb)
    block_ok = jnp.broadcast_to((mask_full == 1)[:, None, :, None], (nb, 2, nb, run))
    rowmask = jnp.where(block_ok.reshape(nb, files) & live[None, :], 1.0, 0.0).astype(jnp.float32)
    own_t = dense_call(mine2, other2, rowmask, n_probe, shard, feat, feat + PROBE_PARTS * n_probe)
    return own_t.T


def normalize(embed):
    values = embed.astype(jnp.float32)
    return (values * lax.rsqrt(jnp.mean(values * values, axis=1, keepdims=True) + 1e-06)).astype(
        jnp.bfloat16
    )


def split3(x):
    hi = lax.reduce_precision(x, exponent_bits=8, mantissa_bits=7)
    rest = x - hi
    mid = lax.reduce_precision(rest, exponent_bits=8, mantissa_bits=7)
    lo = rest - mid
    return jnp.stack([hi, mid, lo]).astype(jnp.bfloat16)


def join3(parts):
    parts = parts.astype(jnp.float32)
    if parts.shape[0] == 1:
        return parts[0]
    return (parts[0] + parts[1]) + parts[2]


def pack_rows(flat, width):
    rows = -(-flat.shape[0] // width)
    return jnp.pad(flat, (0, rows * width - flat.shape[0])).reshape(rows, width), rows


def body(embed, beta, block_mask, counts, probes):
    n_dev = lax.axis_size("row") * lax.axis_size("col")
    n_row = lax.axis_size("row")
    me = lax.axis_index(AXES)
    shard, feat = embed.shape
    files = shard * n_dev
    nb = block_mask.shape[1]
    blk = files // nb
    local_blocks = block_mask.shape[0]

    unit_own = normalize(embed)
    beta_rows, beta_n = pack_rows(beta, feat)
    mask_rows, mask_n = pack_rows(block_mask.reshape(-1).astype(jnp.bfloat16), feat)
    replicate = files * files <= REPLICATE_CELLS
    n_probe = probes.shape[0]
    if (
        replicate
        and n_row % 2 == 0
        and shard % 2 == 0
        and blk % shard == 0
        and (blk // 2) % 8 == 0
        and files % 128 == 0
    ):
        return dense_path(embed, beta, block_mask, counts, probes, n_dev, n_row, me)
    if replicate:
        mask_flat = block_mask.reshape(-1).astype(jnp.bfloat16)
        mask_cols = -(-mask_flat.shape[0] // shard)
        mask_part = jnp.pad(mask_flat, (0, shard * mask_cols - mask_flat.shape[0]))
        used = 3 * n_probe + 1 + mask_cols
        lanes = -(-used // 128) * 128
        extra_cols = jnp.concatenate(
            [
                jnp.moveaxis(split3(probes.T), 0, 1).reshape(shard, 3 * n_probe),
                beta[:, None],
                mask_part.reshape(shard, mask_cols),
                jnp.zeros((shard, lanes - used), jnp.bfloat16),
            ],
            axis=1,
        )
        got = gather_halves(jnp.concatenate([unit_own, extra_cols], axis=1), n_dev, n_row)
        unit_all = got[:, :, :feat].reshape(files, feat)
        tail = got[:, :, feat:].reshape(files, lanes)
        probes_t = join3(
            jnp.stack([tail[:, k * n_probe : (k + 1) * n_probe] for k in range(3)])
        )
        beta_all = tail[:, 3 * n_probe]
        mask_got = got[:, :, feat + 3 * n_probe + 1 : feat + used].reshape(n_dev, -1)
        mask_got = mask_got[:, : local_blocks * nb]
    else:
        unit_all = gather_rows(unit_own, n_dev).reshape(files, feat)
        extra = gather_rows(jnp.concatenate([beta_rows, mask_rows], axis=0), n_dev)
        beta_all = extra[:, 0, :shard].reshape(files)
        mask_got = extra[:, beta_n:, :].reshape(n_dev, -1)[:, : local_blocks * nb]
    per_row = n_dev // n_row
    mask_full = (
        mask_got.reshape(n_row, per_row, local_blocks, nb)[:, 0].reshape(nb, nb).astype(jnp.int32)
    )
    scale_all = beta_all.astype(jnp.float32) / feat

    col_ids = lax.iota(jnp.int32, files)
    col_block = col_ids // blk
    in_block = lax.iota(jnp.int32, blk)
    col_live = (in_block[None, :] < counts[:, None]).reshape(files)

    if replicate:
        gram = lax.dot_general(
            unit_all, unit_all, (((1,), (1,)), ((), ())), preferred_element_type=jnp.float32
        )
        scores = gram * scale_all[:, None]
        block_ok = jnp.broadcast_to(
            (mask_full == 1)[:, None, :, None], (nb, blk, nb, blk)
        ).reshape(files, files)
        allowed = block_ok & col_live[None, :] & (col_ids[:, None] != col_ids[None, :])
        masked = jnp.where(allowed, scores, -1e30)
        row_top = jnp.max(masked, axis=1)
        row_mass = jnp.sum(jnp.where(allowed, jnp.exp(masked - row_top[:, None]), 0.0), axis=1)
        weights = jnp.where(allowed, jnp.exp(masked - row_top[:, None]) / row_mass[:, None], 0.0)
        col_mass = jnp.sum(weights, axis=0)
        inv_root = lax.rsqrt((1.0 + col_mass) * 0.5)
        affinity = weights.astype(jnp.bfloat16)
        state = probes_t
        for sweep in range(ITERS):
            scaled = (state * inv_root[:, None]).astype(jnp.bfloat16)
            row_part = jnp.dot(affinity, scaled, preferred_element_type=jnp.float32)
            col_part = lax.dot_general(
                affinity, scaled, (((0,), (0,)), ((), ())), preferred_element_type=jnp.float32
            )
            state = (row_part + col_part) * (0.5 * inv_root)[:, None]
        return lax.dynamic_slice_in_dim(state, me * shard, shard, 0).T

    own_ids = me * shard + lax.iota(jnp.int32, shard)
    own_block = own_ids // blk
    gram = lax.dot_general(
        unit_own, unit_all, (((1,), (1,)), ((), ())), preferred_element_type=jnp.float32
    )
    own_scale = lax.dynamic_slice_in_dim(scale_all, me * shard, shard, 0)
    scores = gram * own_scale[:, None]
    row_ok = jnp.take(jnp.take(mask_full, own_block, axis=0), col_block, axis=1) == 1
    allowed = row_ok & col_live[None, :] & (own_ids[:, None] != col_ids[None, :])
    masked = jnp.where(allowed, scores, -1e30)
    row_top = jnp.max(masked, axis=1)
    row_mass = jnp.sum(jnp.where(allowed, jnp.exp(masked - row_top[:, None]), 0.0), axis=1)
    weights = jnp.where(allowed, jnp.exp(masked - row_top[:, None]) / row_mass[:, None], 0.0)
    stats = gather_rows(jnp.stack([row_top, row_mass], axis=1), n_dev).reshape(files, 2)
    top_all, mass_all = stats[:, 0], stats[:, 1]
    scores_t = gram * scale_all[None, :]
    own_live = jnp.take(col_live, own_ids, axis=0)
    col_ok = jnp.take(jnp.take(mask_full, col_block, axis=0), own_block, axis=1).T == 1
    allowed_t = col_ok & own_live[:, None] & (own_ids[:, None] != col_ids[None, :])
    masked_t = jnp.where(allowed_t, scores_t, -1e30)
    weights_t = jnp.where(
        allowed_t, jnp.exp(masked_t - top_all[None, :]) / mass_all[None, :], 0.0
    )
    col_mass = jnp.sum(weights_t, axis=1)
    inv_root = lax.rsqrt((1.0 + col_mass) * 0.5)
    aff_rows = weights.astype(jnp.bfloat16)
    aff_cols = weights_t.astype(jnp.bfloat16)
    state = probes
    for sweep in range(ITERS):
        scaled = (state * inv_root[None, :]).astype(jnp.bfloat16)
        scaled_all = gather_rows(scaled.T, n_dev).reshape(files, probes.shape[0])
        row_part = jnp.dot(aff_rows, scaled_all, preferred_element_type=jnp.float32)
        col_part = jnp.dot(aff_cols, scaled_all, preferred_element_type=jnp.float32)
        state = ((row_part + col_part) * (0.5 * inv_root)[:, None]).T
    return state


def solution(mesh):
    placed = (
        P(AXES, None),
        P(AXES),
        P("row", None),
        P(),
        P(None, AXES),
    )
    return jax.shard_map(body, mesh=mesh, in_specs=placed, out_specs=P(None, AXES), check_vma=False)
```
